128 devices in a mesh: tm: 8 (over z_lo, y), space: 16 (over z_hi, x, core).
Axes of the slice: x: 4, y: 4, z: 4 (z_hi: 2, z_lo: 2; z = z_hi * 2 + z_lo), core: 2. Of those that a mesh axis runs over, the one named last changes fastest.
Arguments:
- spectrum: float32 [2, 512, 128, 1024], P(None, 'tm', 'space'), may hold values from -6 to 6
- diffusivity: float32 [128, 1024], P('space'), may hold values from 0.5 to 2
Outputs:
- solution: float32 [2, 512, 128, 1024], P(None, 'tm', 'space')
The draws below stay inside these ranges and needn't reach their ends.
All inputs are finite; a program needn't handle non-finite values.
Results may differ from the reference program's by a relative error of at most 0.00016.
Values sent between devices are 32-bit elements; how exact they have to be, the bound alone decides.
No kernel may reach another device: no remote copies, remote signals or barrier semaphores. Data moves between devices by JAX's collectives and lax.ppermute only.
A program may use at most 128 MiB of HBM per device.

```python
import math
import jax
import jax.numpy as jnp
import numpy as np
from jax import lax

STEPS = 512
COLS = 1024
ROWS = 128
N_TM = 8


def levels(stream_key, shape, cuts, low, top_value):
    def one(position, shards_of):
        draws = jax.random.uniform(jax.random.fold_in(jax.random.fold_in(stream_key, 6), position), (shards_of,), jnp.float32, low / len(cuts), top_value / len(cuts))
        return jnp.repeat(jnp.exp(draws), shape[position] // shards_of).reshape((-1,) + (1,) * (len(shape) - position - 1))

    gain = one(*cuts[0])
    for cut in cuts[1:]:
        gain = gain * one(*cut)
    return gain


def normal_values(own_key, extent, width, most, split=(), kind=jnp.bfloat16):
    gain = levels(own_key, extent, split, -0.22, 0.18) if split else 1.0
    drawn = jax.random.normal(own_key, extent, jnp.float32) * width * gain
    return jnp.minimum(jnp.maximum(drawn, -most), most).astype(kind)


def setup_inputs(seed: int = 0) -> dict:
    arg_keys = jax.random.split(jax.random.key(seed), 3)
    spectrum = normal_values(arg_keys[0], (2, STEPS, ROWS, COLS), 1.0, 6.0, ((1, 8), (2, 16)), jnp.float32)
    diffusivity = jnp.clip(jnp.exp(math.log(2.0) - 1.3862944 * jax.random.uniform(arg_keys[1], (ROWS, COLS), jnp.float32) ** levels(arg_keys[1], (ROWS, COLS), ((0, 16),), -0.2, 0.2)), 0.5, 2.0)
    return {"spectrum": spectrum, "diffusivity": diffusivity}


alpha_wrap = 0.25
step_rate = 0.5
flow_speed = 2.0
sweep_weights = [1.0 / (1.0 + 0.7 * math.cos(math.pi * (2 * order + 1) / 6.0)) for order in range(3)]

def reverse_bits(number, bit_count):
    result = number * 0
    for bit_place in range(bit_count):
        result = result + (number >> bit_place & 1) * (1 << bit_count - 1 - bit_place)
    return result

def shift_parts(freq_ids, total_steps):
    phase_angle = freq_ids.astype(jnp.float32) * (2.0 * math.pi / total_steps)
    root_scale = alpha_wrap ** (1.0 / total_steps)
    return (step_rate * (1.0 - root_scale * jnp.cos(phase_angle)), step_rate * root_scale * jnp.sin(phase_angle))

def divide_diag(residual, diag_real, diag_imag, magnitude):
    real_part = (residual[0] * diag_real + residual[1] * diag_imag) / magnitude
    imag_part = (residual[1] * diag_real - residual[0] * diag_imag) / magnitude
    return jnp.stack([real_part, imag_part])

def apply_operator(current, diffusion, diag_real, diag_imag):
    padded = jnp.pad(current, ((0, 0), (0, 0), (0, 0), (1, 1)))
    center = padded[:, :, 1:-1, 1:-1]
    from_north = padded[:, :, :-2, 1:-1]
    from_south = padded[:, :, 2:, 1:-1]
    from_west = padded[:, :, 1:-1, :-2]
    from_east = padded[:, :, 1:-1, 2:]
    beside_all = from_north + from_south + from_west + from_east
    real_part = diag_real * center[0] - diag_imag * center[1] - diffusion * beside_all[0] - flow_speed * from_north[0]
    imag_part = diag_real * center[1] + diag_imag * center[0] - diffusion * beside_all[1] - flow_speed * from_north[1]
    return jnp.stack([real_part, imag_part])

def sweeps(right_side, diffusion, lam_real, lam_imag, extend):
    diag_real = lam_real[:, None, None] + 4.0 * diffusion + flow_speed
    diag_imag = lam_imag[:, None, None] + jnp.zeros_like(diag_real)
    magnitude = diag_real * diag_real + diag_imag * diag_imag
    current = sweep_weights[0] * divide_diag(right_side, diag_real, diag_imag, magnitude)
    for order in (1, 2):
        applied = apply_operator(extend(current), diffusion, diag_real, diag_imag)
        current = current + sweep_weights[order] * divide_diag(right_side - applied, diag_real, diag_imag, magnitude)
    return current

def pad_rows(current):
    return jnp.pad(current, ((0, 0), (0, 0), (1, 1), (0, 0)))

def reference(spectrum, diffusivity):
    local_count = STEPS // N_TM
    bit_count = N_TM.bit_length() - 1
    freq_of_pos = np.array([pos % local_count * N_TM + reverse_bits(pos // local_count, bit_count) for pos in range(STEPS)])
    inverse = np.argsort(freq_of_pos)
    natural = spectrum[:, inverse]
    block_size = 16
    blocks = natural.reshape(2, STEPS // block_size, block_size, ROWS, COLS).transpose(1, 0, 2, 3, 4)
    freq_ids = jnp.arange(STEPS, dtype=jnp.int32).reshape(STEPS // block_size, block_size)

    def solve_block(pieces):
        right_side, block_ids = pieces
        lam_real, lam_imag = shift_parts(block_ids, STEPS)
        return sweeps(right_side, diffusivity, lam_real, lam_imag, pad_rows)
    solved = lax.map(solve_block, (blocks, freq_ids))
    solved = solved.transpose(1, 0, 2, 3, 4).reshape(2, STEPS, ROWS, COLS)
    temporal = jnp.fft.ifft(lax.complex(solved[0], solved[1]), axis=0) * math.sqrt(STEPS)
    step_ids = jnp.arange(STEPS, dtype=jnp.int32).astype(jnp.float32)
    factor = jnp.exp(step_ids * (-math.log(alpha_wrap) / STEPS))[:, None, None]
    return jnp.stack([jnp.real(temporal) * factor, jnp.imag(temporal) * factor]).astype(jnp.float32)
```

```python
import math

import jax
import jax.numpy as jnp
import numpy as np
from jax import lax
from jax.sharding import PartitionSpec as P

alpha_wrap = 0.25
step_rate = 0.5
flow_speed = 2.0
sweep_weights = [
    1.0 / (1.0 + 0.7 * math.cos(math.pi * (2 * order + 1) / 6.0)) for order in range(3)
]
Q_CHUNKS = 4
HALO = 2


def reverse_bits(number, bit_count):
    result = number * 0
    for bit_place in range(bit_count):
        result = result + (number >> bit_place & 1) * (1 << bit_count - 1 - bit_place)
    return result


def shift_parts(freq_ids, total_steps):
    phase_angle = freq_ids.astype(jnp.float32) * (2.0 * math.pi / total_steps)
    root_scale = alpha_wrap ** (1.0 / total_steps)
    return (
        step_rate * (1.0 - root_scale * jnp.cos(phase_angle)),
        step_rate * root_scale * jnp.sin(phase_angle),
    )


def halo_rows(block, axis, dim, width):
    count = lax.axis_size(axis)
    forward = [(i, i + 1) for i in range(count - 1)]
    backward = [(i + 1, i) for i in range(count - 1)]
    size = block.shape[dim]
    top = lax.ppermute(lax.slice_in_dim(block, size - width, size, axis=dim), axis, forward)
    bottom = lax.ppermute(lax.slice_in_dim(block, 0, width, axis=dim), axis, backward)
    return jnp.concatenate([top, block, bottom], axis=dim)


def divide_diag(re, im, diag_real, diag_imag, inv_mag):
    return (re * diag_real + im * diag_imag) * inv_mag, (im * diag_real - re * diag_imag) * inv_mag


def shift_cols(v, direction):
    zeros = jnp.zeros_like(v[..., :1])
    if direction > 0:
        return jnp.concatenate([zeros, v[..., :-1]], axis=-1)
    return jnp.concatenate([v[..., 1:], zeros], axis=-1)


def apply_operator(v_re, v_im, lo, hi, diffusion, diag_real, diag_imag):
    def parts(v):
        center = v[:, 1:-1]
        north = v[:, :-2]
        south = v[:, 2:]
        beside = north + south + shift_cols(center, 1) + shift_cols(center, -1)
        return center, north, beside

    c_re, n_re, b_re = parts(v_re)
    c_im, n_im, b_im = parts(v_im)
    d = diffusion[lo:hi]
    real_part = diag_real * c_re - diag_imag * c_im - d * b_re - flow_speed * n_re
    imag_part = diag_real * c_im + diag_imag * c_re - d * b_im - flow_speed * n_im
    return real_part, imag_part


def on_device(spectrum, diffusivity):
    local_count = spectrum.shape[1]
    row_count = spectrum.shape[2]
    col_count = spectrum.shape[3]
    tm_count = lax.axis_size("tm")
    space_count = lax.axis_size("space")
    bit_count = tm_count.bit_length() - 1
    total_steps = local_count * tm_count
    tm_place = lax.axis_index("tm")
    space_place = lax.axis_index("space")
    residue = reverse_bits(tm_place, bit_count)
    index_f = jnp.arange(local_count, dtype=jnp.int32)
    freq_ids = index_f * tm_count + residue
    lam_real, lam_imag = shift_parts(freq_ids, total_steps)

    rhs = halo_rows(spectrum, "space", 2, HALO)
    diff = halo_rows(diffusivity, "space", 0, HALO)
    ext_rows = row_count + 2 * HALO
    global_row = space_place * row_count - HALO + jnp.arange(ext_rows, dtype=jnp.int32)
    inside = ((global_row >= 0) & (global_row < space_count * row_count))[None, :, None]

    diag_real = lam_real[:, None, None] + 4.0 * diff + flow_speed
    diag_imag = jnp.broadcast_to(lam_imag[:, None, None], diag_real.shape)
    inv_mag = 1.0 / (diag_real * diag_real + diag_imag * diag_imag)

    r_re, r_im = rhs[0], rhs[1]
    c_re, c_im = divide_diag(r_re, r_im, diag_real, diag_imag, inv_mag)
    c_re = sweep_weights[0] * c_re
    c_im = sweep_weights[0] * c_im
    lo, hi = 0, ext_rows
    for order in (1, 2):
        lo, hi = lo + 1, hi - 1
        a_re, a_im = apply_operator(c_re, c_im, lo, hi, diff, diag_real[:, lo:hi], diag_imag[:, lo:hi])
        u_re, u_im = divide_diag(
            r_re[:, lo:hi] - a_re, r_im[:, lo:hi] - a_im,
            diag_real[:, lo:hi], diag_imag[:, lo:hi], inv_mag[:, lo:hi],
        )
        c_re = c_re[:, 1:-1] + sweep_weights[order] * u_re
        c_im = c_im[:, 1:-1] + sweep_weights[order] * u_im
        if order == 1:
            keep = inside[:, lo:hi]
            c_re = jnp.where(keep, c_re, 0.0)
            c_im = jnp.where(keep, c_im, 0.0)
    flat_field = jnp.concatenate([c_re, c_im], 0).reshape(2 * local_count, row_count * col_count)

    grid_angle = (index_f[:, None] * index_f[None, :] % local_count).astype(jnp.float32) * (
        2.0 * math.pi / local_count
    )
    cosine = jnp.cos(grid_angle)
    sine = jnp.sin(grid_angle)
    twist_angle = (residue * index_f % total_steps).astype(jnp.float32) * (
        2.0 * math.pi / total_steps
    )
    twist_cos = jnp.cos(twist_angle)
    twist_sin = jnp.sin(twist_angle)

    source_residue = np.array([reverse_bits(source, bit_count) for source in range(tm_count)])
    class_index = np.arange(tm_count)[:, None] * source_residue[None, :] % tm_count
    class_angle = class_index.astype(np.float64) * (2.0 * math.pi / tm_count)
    class_cos = jnp.asarray(np.cos(class_angle), jnp.float32)
    class_sin = jnp.asarray(np.sin(class_angle), jnp.float32)
    high = lax.Precision.HIGHEST
    step_rate_log = -math.log(alpha_wrap) / total_steps
    col_block = col_count // tm_count

    chunk = local_count // Q_CHUNKS
    pieces = []
    for c in range(Q_CHUNKS):
        qs = slice(c * chunk, (c + 1) * chunk)
        table = jnp.concatenate(
            [jnp.concatenate([cosine[qs], -sine[qs]], 1), jnp.concatenate([sine[qs], cosine[qs]], 1)], 0
        )
        spectral = jnp.dot(table, flat_field, precision=high).reshape(2, chunk, row_count, col_count)
        tc = twist_cos[qs][:, None, None]
        ts = twist_sin[qs][:, None, None]
        tw_re = tc * spectral[0] - ts * spectral[1]
        tw_im = ts * spectral[0] + tc * spectral[1]
        outgoing = jnp.stack([tw_re, tw_im]).reshape(2, chunk, row_count, tm_count, col_block)
        outgoing = jnp.moveaxis(outgoing, 3, 0)
        arrived = lax.all_to_all(outgoing, "tm", 0, 0, tiled=True)
        a_re = arrived[:, 0].reshape(tm_count, -1)
        a_im = arrived[:, 1].reshape(tm_count, -1)
        comb_re = jnp.dot(class_cos, a_re, precision=high) - jnp.dot(class_sin, a_im, precision=high)
        comb_im = jnp.dot(class_sin, a_re, precision=high) + jnp.dot(class_cos, a_im, precision=high)
        step_ids = (
            jnp.arange(tm_count, dtype=jnp.int32)[:, None] * local_count + c * chunk
            + jnp.arange(chunk, dtype=jnp.int32)[None, :]
        ).astype(jnp.float32)
        factor = (jnp.exp(step_ids * step_rate_log) / math.sqrt(total_steps))[:, :, None, None]
        comb_re = comb_re.reshape(tm_count, chunk, row_count, col_block) * factor
        comb_im = comb_im.reshape(tm_count, chunk, row_count, col_block) * factor
        combined = jnp.stack([comb_re, comb_im], 1)
        returned = lax.all_to_all(combined, "tm", 0, 0, tiled=True)
        pieces.append(jnp.moveaxis(returned, 0, 3).reshape(2, chunk, row_count, col_count))
    return jnp.concatenate(pieces, axis=1)


def solution(mesh):
    in_specs = (P(None, "tm", "space", None), P("space", None))
    out_specs = P(None, "tm", "space", None)
    return jax.shard_map(
        on_device, mesh=mesh, in_specs=in_specs, out_specs=out_specs, check_vma=False
    )
```

```python
import math

import jax
import jax.numpy as jnp
import numpy as np
from jax import lax
from jax.experimental import pallas as pl
from jax.experimental.pallas import tpu as pltpu
from jax.sharding import PartitionSpec as P

alpha_wrap = 0.25
step_rate = 0.5
flow_speed = 2.0
sweep_weights = [
    1.0 / (1.0 + 0.7 * math.cos(math.pi * (2 * order + 1) / 6.0)) for order in range(3)
]
Q_CHUNKS = 1
F_BLOCK = 4
HALO = 2


def reverse_bits(number, bit_count):
    result = number * 0
    for bit_place in range(bit_count):
        result = result + (number >> bit_place & 1) * (1 << bit_count - 1 - bit_place)
    return result


def shift_parts(freq_ids, total_steps):
    phase_angle = freq_ids.astype(jnp.float32) * (2.0 * math.pi / total_steps)
    root_scale = alpha_wrap ** (1.0 / total_steps)
    return (
        step_rate * (1.0 - root_scale * jnp.cos(phase_angle)),
        step_rate * root_scale * jnp.sin(phase_angle),
    )


def halo_pair(block, axis, dim, width):
    count = lax.axis_size(axis)
    forward = [(i, i + 1) for i in range(count - 1)]
    backward = [(i + 1, i) for i in range(count - 1)]
    size = block.shape[dim]
    top = lax.ppermute(lax.slice_in_dim(block, size - width, size, axis=dim), axis, forward)
    bottom = lax.ppermute(lax.slice_in_dim(block, 0, width, axis=dim), axis, backward)
    return top, bottom


def sweep_kernel(lam_ref, rhs_ref, top_ref, bot_ref, diff_ref, mask_ref, o_ref):
    block = rhs_ref.shape[1]
    cols = rhs_ref.shape[3]
    base = pl.program_id(0) * block
    diff = diff_ref[...]
    diag_base = 4.0 * diff + flow_speed
    keep = mask_ref[...]
    row8 = lax.broadcasted_iota(jnp.int32, (8, cols), 0)
    col = lax.broadcasted_iota(jnp.int32, (16, cols), 1)

    def frame(x, f):
        local = rhs_ref[x, f]
        bv = bot_ref[x, f]
        tv = top_ref[x, f]
        hi = jnp.where(row8 == 0, jnp.broadcast_to(bv[0:1], (8, cols)), 0.0)
        hi = jnp.where(row8 == 1, jnp.broadcast_to(bv[1:2], (8, cols)), hi)
        hi = jnp.where(row8 == 6, jnp.broadcast_to(tv[0:1], (8, cols)), hi)
        hi = jnp.where(row8 == 7, jnp.broadcast_to(tv[1:2], (8, cols)), hi)
        return jnp.concatenate([local, hi], axis=0)

    def around(v):
        north = pltpu.roll(v, 1, 0)
        south = pltpu.roll(v, 15, 0)
        west = jnp.where(col == 0, 0.0, pltpu.roll(v, 1, 1))
        east = jnp.where(col == cols - 1, 0.0, pltpu.roll(v, cols - 1, 1))
        return north, north + south + west + east

    def body(f, carry):
        lam_r = lam_ref[0, base + f]
        lam_i = lam_ref[1, base + f]
        dr = diag_base + lam_r
        inv_mag = 1.0 / (dr * dr + lam_i * lam_i)
        r_re = frame(0, f)
        r_im = frame(1, f)
        c_re = sweep_weights[0] * ((r_re * dr + r_im * lam_i) * inv_mag)
        c_im = sweep_weights[0] * ((r_im * dr - r_re * lam_i) * inv_mag)
        for order in (1, 2):
            n_re, b_re = around(c_re)
            n_im, b_im = around(c_im)
            a_re = dr * c_re - lam_i * c_im - diff * b_re - flow_speed * n_re
            a_im = dr * c_im + lam_i * c_re - diff * b_im - flow_speed * n_im
            s_re = r_re - a_re
            s_im = r_im - a_im
            c_re = c_re + sweep_weights[order] * ((s_re * dr + s_im * lam_i) * inv_mag)
            c_im = c_im + sweep_weights[order] * ((s_im * dr - s_re * lam_i) * inv_mag)
            if order == 1:
                c_re = c_re * keep
                c_im = c_im * keep
        o_ref[0, f] = c_re[0:8]
        o_ref[1, f] = c_im[0:8]
        return carry

    lax.fori_loop(0, block, body, 0)


def sweep_call(lam, spectrum, top, bottom, diff_frame, mask_frame):
    _, count, rows, cols = spectrum.shape
    block = F_BLOCK
    big = pl.BlockSpec((2, block, rows, cols), lambda g: (0, g, 0, 0))
    edge = pl.BlockSpec((2, block, HALO, cols), lambda g: (0, g, 0, 0))
    whole = pl.BlockSpec((16, cols), lambda g: (0, 0))
    return pl.pallas_call(
        sweep_kernel,
        out_shape=jax.ShapeDtypeStruct(spectrum.shape, jnp.float32),
        grid=(count // block,),
        in_specs=[pl.BlockSpec(memory_space=pltpu.SMEM), big, edge, edge, whole, whole],
        out_specs=big,
        compiler_params=pltpu.CompilerParams(dimension_semantics=("arbitrary",)),
        cost_estimate=pl.CostEstimate(
            flops=200 * spectrum.size, transcendentals=0, bytes_accessed=8 * spectrum.size
        ),
    )(lam, spectrum, top, bottom, diff_frame, mask_frame)


def frames(diffusivity, space_place, space_count):
    rows, cols = diffusivity.shape
    d_top, d_bot = halo_pair(diffusivity, "space", 0, HALO)
    gap = jnp.zeros((16 - rows - 2 * HALO, cols), jnp.float32)
    diff_frame = jnp.concatenate([diffusivity, d_bot, gap, d_top], axis=0)
    row = jnp.arange(16, dtype=jnp.int32)
    keep = (row < rows) | ((row == rows) & (space_place < space_count - 1)) | (
        (row == 15) & (space_place > 0)
    )
    mask_frame = jnp.broadcast_to(keep.astype(jnp.float32)[:, None], (16, cols))
    return diff_frame, mask_frame


def on_device(spectrum, diffusivity):
    local_count = spectrum.shape[1]
    row_count = spectrum.shape[2]
    col_count = spectrum.shape[3]
    tm_count = lax.axis_size("tm")
    space_count = lax.axis_size("space")
    bit_count = tm_count.bit_length() - 1
    total_steps = local_count * tm_count
    tm_place = lax.axis_index("tm")
    space_place = lax.axis_index("space")
    residue = reverse_bits(tm_place, bit_count)
    index_f = jnp.arange(local_count, dtype=jnp.int32)
    freq_ids = index_f * tm_count + residue
    lam = jnp.stack(shift_parts(freq_ids, total_steps))

    top, bottom = halo_pair(spectrum, "space", 2, HALO)
    diff_frame, mask_frame = frames(diffusivity, space_place, space_count)
    current = sweep_call(lam, spectrum, top, bottom, diff_frame, mask_frame)
    flat_field = current.reshape(2 * local_count, row_count * col_count)

    grid_angle = (index_f[:, None] * freq_ids[None, :] % total_steps).astype(jnp.float32) * (
        2.0 * math.pi / total_steps
    )
    cosine = jnp.cos(grid_angle)
    sine = jnp.sin(grid_angle)

    source_residue = np.array([reverse_bits(source, bit_count) for source in range(tm_count)])
    class_index = np.arange(tm_count)[:, None] * source_residue[None, :] % tm_count
    class_angle = class_index.astype(np.float64) * (2.0 * math.pi / tm_count)
    class_cos = jnp.asarray(np.cos(class_angle), jnp.float32)
    class_sin = jnp.asarray(np.sin(class_angle), jnp.float32)
    high = lax.Precision.HIGHEST
    step_rate_log = -math.log(alpha_wrap) / total_steps
    col_block = col_count // tm_count

    chunk = local_count // Q_CHUNKS
    pieces = []
    for c in range(Q_CHUNKS):
        qs = slice(c * chunk, (c + 1) * chunk)
        table = jnp.concatenate(
            [jnp.concatenate([cosine[qs], -sine[qs]], 1), jnp.concatenate([sine[qs], cosine[qs]], 1)], 0
        )
        spectral = jnp.dot(table, flat_field, precision=high)
        outgoing = spectral.reshape(2, chunk, row_count, tm_count, col_block)
        outgoing = jnp.moveaxis(outgoing, 3, 0)
        arrived = lax.all_to_all(outgoing, "tm", 0, 0, tiled=True)
        a_re = arrived[:, 0].reshape(tm_count, -1)
        a_im = arrived[:, 1].reshape(tm_count, -1)
        comb_re = jnp.dot(class_cos, a_re, precision=high) - jnp.dot(class_sin, a_im, precision=high)
        comb_im = jnp.dot(class_sin, a_re, precision=high) + jnp.dot(class_cos, a_im, precision=high)
        step_ids = (
            jnp.arange(tm_count, dtype=jnp.int32)[:, None] * local_count + c * chunk
            + jnp.arange(chunk, dtype=jnp.int32)[None, :]
        ).astype(jnp.float32)
        factor = (jnp.exp(step_ids * step_rate_log) / math.sqrt(total_steps))[:, :, None, None]
        comb_re = comb_re.reshape(tm_count, chunk, row_count, col_block) * factor
        comb_im = comb_im.reshape(tm_count, chunk, row_count, col_block) * factor
        combined = jnp.stack([comb_re, comb_im], 1)
        returned = lax.all_to_all(combined, "tm", 0, 0, tiled=True)
        pieces.append(jnp.moveaxis(returned, 0, 3).reshape(2, chunk, row_count, col_count))
    return jnp.concatenate(pieces, axis=1) if len(pieces) > 1 else pieces[0]


def solution(mesh):
    in_specs = (P(None, "tm", "space", None), P("space", None))
    out_specs = P(None, "tm", "space", None)
    return jax.shard_map(
        on_device, mesh=mesh, in_specs=in_specs, out_specs=out_specs, check_vma=False
    )
```

```python
import functools
import math

import jax
import jax.numpy as jnp
import numpy as np
from jax import lax
from jax.experimental import pallas as pl
from jax.experimental.pallas import tpu as pltpu
from jax.sharding import PartitionSpec as P

alpha_wrap = 0.25
step_rate = 0.5
flow_speed = 2.0
sweep_weights = [
    1.0 / (1.0 + 0.7 * math.cos(math.pi * (2 * order + 1) / 6.0)) for order in range(3)
]
Q_BLOCK = 16
F_BLOCK = 4
HALO = 2


def reverse_bits(number, bit_count):
    result = number * 0
    for bit_place in range(bit_count):
        result = result + (number >> bit_place & 1) * (1 << bit_count - 1 - bit_place)
    return result


def shift_parts(freq_ids, total_steps):
    phase_angle = freq_ids.astype(jnp.float32) * (2.0 * math.pi / total_steps)
    root_scale = alpha_wrap ** (1.0 / total_steps)
    return (
        step_rate * (1.0 - root_scale * jnp.cos(phase_angle)),
        step_rate * root_scale * jnp.sin(phase_angle),
    )


def halo_pair(block, axis, dim, width):
    count = lax.axis_size(axis)
    forward = [(i, i + 1) for i in range(count - 1)]
    backward = [(i + 1, i) for i in range(count - 1)]
    size = block.shape[dim]
    top = lax.ppermute(lax.slice_in_dim(block, size - width, size, axis=dim), axis, forward)
    bottom = lax.ppermute(lax.slice_in_dim(block, 0, width, axis=dim), axis, backward)
    return top, bottom


def sweep_kernel(lam_ref, rhs_ref, top_ref, bot_ref, diff_ref, mask_ref, table_ref, o_ref, field):
    block = rhs_ref.shape[1]
    count = lam_ref.shape[1]
    cols = rhs_ref.shape[3]
    base = pl.program_id(0) * block
    diff = diff_ref[...]
    diag_base = 4.0 * diff + flow_speed
    keep = mask_ref[...]
    row8 = lax.broadcasted_iota(jnp.int32, (8, cols), 0)
    col = lax.broadcasted_iota(jnp.int32, (16, cols), 1)

    def frame(x, f):
        local = rhs_ref[x, f]
        bv = bot_ref[x, f]
        tv = top_ref[x, f]
        hi = jnp.where(row8 == 0, jnp.broadcast_to(bv[0:1], (8, cols)), 0.0)
        hi = jnp.where(row8 == 1, jnp.broadcast_to(bv[1:2], (8, cols)), hi)
        hi = jnp.where(row8 == 6, jnp.broadcast_to(tv[0:1], (8, cols)), hi)
        hi = jnp.where(row8 == 7, jnp.broadcast_to(tv[1:2], (8, cols)), hi)
        return jnp.concatenate([local, hi], axis=0)

    def around(v):
        north = pltpu.roll(v, 1, 0)
        south = pltpu.roll(v, 15, 0)
        west = jnp.where(col == 0, 0.0, pltpu.roll(v, 1, 1))
        east = jnp.where(col == cols - 1, 0.0, pltpu.roll(v, cols - 1, 1))
        return north, north + south + west + east

    def body(f, carry):
        lam_r = lam_ref[0, base + f]
        lam_i = lam_ref[1, base + f]
        dr = diag_base + lam_r
        inv_mag = 1.0 / (dr * dr + lam_i * lam_i)
        r_re = frame(0, f)
        r_im = frame(1, f)
        c_re = sweep_weights[0] * ((r_re * dr + r_im * lam_i) * inv_mag)
        c_im = sweep_weights[0] * ((r_im * dr - r_re * lam_i) * inv_mag)
        for order in (1, 2):
            n_re, b_re = around(c_re)
            n_im, b_im = around(c_im)
            a_re = dr * c_re - lam_i * c_im - diff * b_re - flow_speed * n_re
            a_im = dr * c_im + lam_i * c_re - diff * b_im - flow_speed * n_im
            s_re = r_re - a_re
            s_im = r_im - a_im
            c_re = c_re + sweep_weights[order] * ((s_re * dr + s_im * lam_i) * inv_mag)
            c_im = c_im + sweep_weights[order] * ((s_im * dr - s_re * lam_i) * inv_mag)
            if order == 1:
                c_re = c_re * keep
                c_im = c_im * keep
        width = field.shape[2]
        for blk in range(field.shape[0]):
            lanes = slice(blk * width, (blk + 1) * width)
            field[blk, pl.ds(pl.multiple_of((base + f) * 8, 8), 8), :] = c_re[0:8, lanes]
            field[blk, pl.ds(pl.multiple_of((count + base + f) * 8, 8), 8), :] = c_im[0:8, lanes]
        return carry

    lax.fori_loop(0, block, body, 0)

    @pl.when(pl.program_id(0) == pl.num_programs(0) - 1)
    def _():
        table = table_ref[...]
        for blk in range(o_ref.shape[0]):
            for r in range(8):
                plane = field[blk, pl.ds(r, 2 * count, stride=8), :]
                o_ref[blk, pl.ds(r, 2 * count, stride=8), :] = jnp.dot(
                    table, plane, precision=lax.Precision.HIGHEST, preferred_element_type=jnp.float32
                )


def sweep_call(lam, spectrum, top, bottom, diff_frame, mask_frame, table, blocks):
    _, count, rows, cols = spectrum.shape
    block = F_BLOCK
    width = cols // blocks
    big = pl.BlockSpec((2, block, rows, cols), lambda g: (0, g, 0, 0))
    edge = pl.BlockSpec((2, block, HALO, cols), lambda g: (0, g, 0, 0))
    whole = pl.BlockSpec((16, cols), lambda g: (0, 0))
    square = pl.BlockSpec((2 * count, 2 * count), lambda g: (0, 0))
    out_rows = 2 * count * rows
    return pl.pallas_call(
        sweep_kernel,
        out_shape=jax.ShapeDtypeStruct((blocks, out_rows, width), jnp.float32),
        grid=(count // block,),
        in_specs=[pl.BlockSpec(memory_space=pltpu.SMEM), big, edge, edge, whole, whole, square],
        out_specs=pl.BlockSpec((blocks, out_rows, width), lambda g: (0, 0, 0)),
        scratch_shapes=[pltpu.VMEM((blocks, out_rows, width), jnp.float32)],
        compiler_params=pltpu.CompilerParams(dimension_semantics=("arbitrary",)),
        cost_estimate=pl.CostEstimate(
            flops=200 * spectrum.size, transcendentals=0, bytes_accessed=8 * spectrum.size
        ),
    )(lam, spectrum, top, bottom, diff_frame, mask_frame, table)


def combine_kernel(weights, fac_ref, a_ref, o_ref):
    block = a_ref.shape[2] // 8
    base = pl.program_id(0) * block

    def body(qi, carry):
        rows = pl.ds(pl.multiple_of(qi * 8, 8), 8)
        parts = [(a_ref[s, 0, rows, :], a_ref[s, 1, rows, :]) for s in range(a_ref.shape[0])]
        for m, row in enumerate(weights):
            acc_re = []
            acc_im = []
            for (c, s), (x_re, x_im) in zip(row, parts):
                for coef, val, acc in ((c, x_re, acc_re), (-s, x_im, acc_re), (s, x_re, acc_im), (c, x_im, acc_im)):
                    if coef == 1.0:
                        acc.append(val)
                    elif coef == -1.0:
                        acc.append(-val)
                    elif coef != 0.0:
                        acc.append(coef * val)
            scale = fac_ref[m, base + qi]
            o_ref[m, 0, rows, :] = sum(acc_re[1:], acc_re[0]) * scale
            o_ref[m, 1, rows, :] = sum(acc_im[1:], acc_im[0]) * scale
        return carry

    lax.fori_loop(0, block, body, 0)


def combine_call(weights, factor, arrived, q_block):
    blocks, _, rows, width = arrived.shape
    spec = pl.BlockSpec((blocks, 2, q_block * 8, width), lambda g: (0, 0, g, 0))
    return pl.pallas_call(
        functools.partial(combine_kernel, weights),
        out_shape=jax.ShapeDtypeStruct(arrived.shape, jnp.float32),
        grid=(rows // (q_block * 8),),
        in_specs=[pl.BlockSpec(memory_space=pltpu.SMEM), spec],
        out_specs=spec,
        compiler_params=pltpu.CompilerParams(dimension_semantics=("arbitrary",)),
        cost_estimate=pl.CostEstimate(
            flops=40 * arrived.size, transcendentals=0, bytes_accessed=8 * arrived.size
        ),
    )(factor, arrived)


def class_weights(tm_count, bit_count):
    rows = []
    for m in range(tm_count):
        row = []
        for source in range(tm_count):
            angle = 2.0 * math.pi * ((m * reverse_bits(source, bit_count)) % tm_count) / tm_count
            c, s = math.cos(angle), math.sin(angle)
            c = float(np.float32(0.0 if abs(c) < 1e-9 else c))
            s = float(np.float32(0.0 if abs(s) < 1e-9 else s))
            row.append((c, s))
        rows.append(tuple(row))
    return tuple(rows)


def frames(diffusivity, space_place, space_count):
    rows, cols = diffusivity.shape
    d_top, d_bot = halo_pair(diffusivity, "space", 0, HALO)
    gap = jnp.zeros((16 - rows - 2 * HALO, cols), jnp.float32)
    diff_frame = jnp.concatenate([diffusivity, d_bot, gap, d_top], axis=0)
    row = jnp.arange(16, dtype=jnp.int32)
    keep = (row < rows) | ((row == rows) & (space_place < space_count - 1)) | (
        (row == 15) & (space_place > 0)
    )
    mask_frame = jnp.broadcast_to(keep.astype(jnp.float32)[:, None], (16, cols))
    return diff_frame, mask_frame


def on_device(spectrum, diffusivity):
    local_count = spectrum.shape[1]
    row_count = spectrum.shape[2]
    col_count = spectrum.shape[3]
    tm_count = lax.axis_size("tm")
    space_count = lax.axis_size("space")
    bit_count = tm_count.bit_length() - 1
    total_steps = local_count * tm_count
    tm_place = lax.axis_index("tm")
    space_place = lax.axis_index("space")
    residue = reverse_bits(tm_place, bit_count)
    index_f = jnp.arange(local_count, dtype=jnp.int32)
    freq_ids = index_f * tm_count + residue
    lam = jnp.stack(shift_parts(freq_ids, total_steps))

    top, bottom = halo_pair(spectrum, "space", 2, HALO)
    diff_frame, mask_frame = frames(diffusivity, space_place, space_count)
    grid_angle = (index_f[:, None] * freq_ids[None, :] % total_steps).astype(jnp.float32) * (
        2.0 * math.pi / total_steps
    )
    cosine = jnp.cos(grid_angle)
    sine = jnp.sin(grid_angle)
    table = jnp.concatenate(
        [jnp.concatenate([cosine, -sine], 1), jnp.concatenate([sine, cosine], 1)], 0
    )
    outgoing = sweep_call(lam, spectrum, top, bottom, diff_frame, mask_frame, table, tm_count)
    col_block = col_count // tm_count
    outgoing = outgoing.reshape(tm_count, 2, local_count * row_count, col_block)
    arrived = lax.all_to_all(outgoing, "tm", 0, 0, tiled=True)

    step_ids = (
        jnp.arange(tm_count, dtype=jnp.int32)[:, None] * local_count
        + jnp.arange(local_count, dtype=jnp.int32)[None, :]
    ).astype(jnp.float32)
    factor = jnp.exp(step_ids * (-math.log(alpha_wrap) / total_steps)) / math.sqrt(total_steps)
    combined = combine_call(class_weights(tm_count, bit_count), factor, arrived, Q_BLOCK)
    returned = lax.all_to_all(combined, "tm", 0, 0, tiled=True)
    returned = returned.reshape(tm_count, 2, local_count, row_count, col_block)
    return jnp.moveaxis(returned, 0, 3).reshape(2, local_count, row_count, col_count)


def solution(mesh):
    in_specs = (P(None, "tm", "space", None), P("space", None))
    out_specs = P(None, "tm", "space", None)
    return jax.shard_map(
        on_device, mesh=mesh, in_specs=in_specs, out_specs=out_specs, check_vma=False
    )
```

```python
import functools
import math

import jax
import jax.numpy as jnp
import numpy as np
from jax import lax
from jax.experimental import pallas as pl
from jax.experimental.pallas import tpu as pltpu
from jax.sharding import PartitionSpec as P

alpha_wrap = 0.25
step_rate = 0.5
flow_speed = 2.0
sweep_weights = [
    1.0 / (1.0 + 0.7 * math.cos(math.pi * (2 * order + 1) / 6.0)) for order in range(3)
]
Q_BLOCK = 16
F_BLOCK = 4
HALO = 2


def reverse_bits(number, bit_count):
    result = number * 0
    for bit_place in range(bit_count):
        result = result + (number >> bit_place & 1) * (1 << bit_count - 1 - bit_place)
    return result


def shift_parts(freq_ids, total_steps):
    phase_angle = freq_ids.astype(jnp.float32) * (2.0 * math.pi / total_steps)
    root_scale = alpha_wrap ** (1.0 / total_steps)
    return (
        step_rate * (1.0 - root_scale * jnp.cos(phase_angle)),
        step_rate * root_scale * jnp.sin(phase_angle),
    )


def halo_pair(block, axis, dim, width):
    count = lax.axis_size(axis)
    forward = [(i, i + 1) for i in range(count - 1)]
    backward = [(i + 1, i) for i in range(count - 1)]
    size = block.shape[dim]
    top = lax.ppermute(lax.slice_in_dim(block, size - width, size, axis=dim), axis, forward)
    bottom = lax.ppermute(lax.slice_in_dim(block, 0, width, axis=dim), axis, backward)
    return top, bottom


def sweep_kernel(dev_ref, lam_ref, rhs_ref, top_ref, bot_ref, diff_ref, mask_ref, table_ref, *rest):
    out_refs, field = rest[:-1], rest[-1]
    block = rhs_ref.shape[1]
    count = lam_ref.shape[1]
    cols = rhs_ref.shape[3]
    base = pl.program_id(0) * block
    diff = diff_ref[...]
    diag_base = 4.0 * diff + flow_speed
    keep = mask_ref[...]
    row8 = lax.broadcasted_iota(jnp.int32, (8, cols), 0)
    col = lax.broadcasted_iota(jnp.int32, (16, cols), 1)

    def frame(x, f):
        local = rhs_ref[x, f]
        bv = bot_ref[x, f]
        tv = top_ref[x, f]
        hi = jnp.where(row8 == 0, jnp.broadcast_to(bv[0:1], (8, cols)), 0.0)
        hi = jnp.where(row8 == 1, jnp.broadcast_to(bv[1:2], (8, cols)), hi)
        hi = jnp.where(row8 == 6, jnp.broadcast_to(tv[0:1], (8, cols)), hi)
        hi = jnp.where(row8 == 7, jnp.broadcast_to(tv[1:2], (8, cols)), hi)
        return jnp.concatenate([local, hi], axis=0)

    def around(v):
        north = pltpu.roll(v, 1, 0)
        south = pltpu.roll(v, 15, 0)
        west = jnp.where(col == 0, 0.0, pltpu.roll(v, 1, 1))
        east = jnp.where(col == cols - 1, 0.0, pltpu.roll(v, cols - 1, 1))
        return north, north + south + west + east

    def body(f, carry):
        lam_r = lam_ref[0, base + f]
        lam_i = lam_ref[1, base + f]
        dr = diag_base + lam_r
        inv_mag = 1.0 / (dr * dr + lam_i * lam_i)
        r_re = frame(0, f)
        r_im = frame(1, f)
        c_re = sweep_weights[0] * ((r_re * dr + r_im * lam_i) * inv_mag)
        c_im = sweep_weights[0] * ((r_im * dr - r_re * lam_i) * inv_mag)
        for order in (1, 2):
            n_re, b_re = around(c_re)
            n_im, b_im = around(c_im)
            a_re = dr * c_re - lam_i * c_im - diff * b_re - flow_speed * n_re
            a_im = dr * c_im + lam_i * c_re - diff * b_im - flow_speed * n_im
            s_re = r_re - a_re
            s_im = r_im - a_im
            c_re = c_re + sweep_weights[order] * ((s_re * dr + s_im * lam_i) * inv_mag)
            c_im = c_im + sweep_weights[order] * ((s_im * dr - s_re * lam_i) * inv_mag)
            if order == 1:
                c_re = c_re * keep
                c_im = c_im * keep
        width = field.shape[2]
        for blk in range(field.shape[0]):
            lanes = slice(blk * width, (blk + 1) * width)
            field[blk, pl.ds(pl.multiple_of((base + f) * 8, 8), 8), :] = c_re[0:8, lanes]
            field[blk, pl.ds(pl.multiple_of((count + base + f) * 8, 8), 8), :] = c_im[0:8, lanes]
        return carry

    lax.fori_loop(0, block, body, 0)

    @pl.when(pl.program_id(0) == pl.num_programs(0) - 1)
    def _():
        table = table_ref[...]
        device = dev_ref[0]
        for slot, o_ref in enumerate(out_refs):
            source = field.at[device ^ slot]
            for r in range(8):
                plane = source[pl.ds(r, 2 * count, stride=8), :]
                o_ref[pl.ds(r, 2 * count, stride=8), :] = jnp.dot(
                    table, plane, precision=lax.Precision.HIGHEST, preferred_element_type=jnp.float32
                )


def sweep_call(device, lam, spectrum, top, bottom, diff_frame, mask_frame, table, blocks):
    _, count, rows, cols = spectrum.shape
    block = F_BLOCK
    width = cols // blocks
    big = pl.BlockSpec((2, block, rows, cols), lambda g: (0, g, 0, 0))
    edge = pl.BlockSpec((2, block, HALO, cols), lambda g: (0, g, 0, 0))
    whole = pl.BlockSpec((16, cols), lambda g: (0, 0))
    square = pl.BlockSpec((2 * count, 2 * count), lambda g: (0, 0))
    out_rows = 2 * count * rows
    return pl.pallas_call(
        sweep_kernel,
        out_shape=[jax.ShapeDtypeStruct((out_rows, width), jnp.float32)] * blocks,
        grid=(count // block,),
        in_specs=[pl.BlockSpec(memory_space=pltpu.SMEM)] * 2 + [big, edge, edge, whole, whole, square],
        out_specs=[pl.BlockSpec((out_rows, width), lambda g: (0, 0))] * blocks,
        scratch_shapes=[pltpu.VMEM((blocks, out_rows, width), jnp.float32)],
        compiler_params=pltpu.CompilerParams(dimension_semantics=("arbitrary",)),
        cost_estimate=pl.CostEstimate(
            flops=200 * spectrum.size, transcendentals=0, bytes_accessed=8 * spectrum.size
        ),
    )(device, lam, spectrum, top, bottom, diff_frame, mask_frame, table)


def combine_kernel(w_ref, fac_ref, *refs):
    count = len(refs) // 2
    in_refs, out_refs = refs[:count], refs[count:]
    block = in_refs[0].shape[1] // 8
    base = pl.program_id(0) * block

    def body(qi, carry):
        rows = pl.ds(pl.multiple_of(qi * 8, 8), 8)
        parts = [(ref[0, rows, :], ref[1, rows, :]) for ref in in_refs]
        for so, o_ref in enumerate(out_refs):
            acc_re = None
            acc_im = None
            for si, (x_re, x_im) in enumerate(parts):
                c = w_ref[0, so, si]
                s = w_ref[1, so, si]
                t_re = c * x_re - s * x_im
                t_im = s * x_re + c * x_im
                acc_re = t_re if acc_re is None else acc_re + t_re
                acc_im = t_im if acc_im is None else acc_im + t_im
            scale = fac_ref[so, base + qi]
            o_ref[0, rows, :] = acc_re * scale
            o_ref[1, rows, :] = acc_im * scale
        return carry

    lax.fori_loop(0, block, body, 0)


def combine_call(weights, factor, slots, q_block):
    _, rows, width = slots[0].shape
    spec = pl.BlockSpec((2, q_block * 8, width), lambda g: (0, g, 0))
    count = len(slots)
    return pl.pallas_call(
        combine_kernel,
        out_shape=[jax.ShapeDtypeStruct(slots[0].shape, jnp.float32)] * count,
        grid=(rows // (q_block * 8),),
        in_specs=[pl.BlockSpec(memory_space=pltpu.SMEM)] * 2 + [spec] * count,
        out_specs=[spec] * count,
        compiler_params=pltpu.CompilerParams(dimension_semantics=("arbitrary",)),
        cost_estimate=pl.CostEstimate(
            flops=64 * count * slots[0].size, transcendentals=0, bytes_accessed=8 * count * slots[0].size
        ),
    )(weights, factor, *slots)


def place_kernel(dev_ref, *refs):
    count = len(refs) - 1
    in_refs, o_ref = refs[:count], refs[count]
    width = in_refs[0].shape[2]
    device = dev_ref[0]
    for slot, ref in enumerate(in_refs):
        start = pl.multiple_of((device ^ slot) * width, width)
        o_ref[:, :, pl.ds(start, width)] = ref[...]


def place_call(device, slots, q_block):
    _, rows, width = slots[0].shape
    count = len(slots)
    spec = pl.BlockSpec((2, q_block * 8, width), lambda g: (0, g, 0))
    return pl.pallas_call(
        place_kernel,
        out_shape=jax.ShapeDtypeStruct((2, rows, width * count), jnp.float32),
        grid=(rows // (q_block * 8),),
        in_specs=[pl.BlockSpec(memory_space=pltpu.SMEM)] + [spec] * count,
        out_specs=pl.BlockSpec((2, q_block * 8, width * count), lambda g: (0, g, 0)),
        compiler_params=pltpu.CompilerParams(dimension_semantics=("arbitrary",)),
    )(device, *slots)


def xor_exchange(slots, axis):
    received = [slots[0]]
    for slot in range(1, len(slots)):
        pairs = [(i, i ^ slot) for i in range(len(slots))]
        received.append(lax.ppermute(slots[slot], axis, pairs))
    return received


def frames(diffusivity, space_place, space_count):
    rows, cols = diffusivity.shape
    d_top, d_bot = halo_pair(diffusivity, "space", 0, HALO)
    gap = jnp.zeros((16 - rows - 2 * HALO, cols), jnp.float32)
    diff_frame = jnp.concatenate([diffusivity, d_bot, gap, d_top], axis=0)
    row = jnp.arange(16, dtype=jnp.int32)
    keep = (row < rows) | ((row == rows) & (space_place < space_count - 1)) | (
        (row == 15) & (space_place > 0)
    )
    mask_frame = jnp.broadcast_to(keep.astype(jnp.float32)[:, None], (16, cols))
    return diff_frame, mask_frame


def on_device(spectrum, diffusivity):
    local_count = spectrum.shape[1]
    row_count = spectrum.shape[2]
    col_count = spectrum.shape[3]
    tm_count = lax.axis_size("tm")
    space_count = lax.axis_size("space")
    bit_count = tm_count.bit_length() - 1
    total_steps = local_count * tm_count
    tm_place = lax.axis_index("tm")
    space_place = lax.axis_index("space")
    residue = reverse_bits(tm_place, bit_count)
    index_f = jnp.arange(local_count, dtype=jnp.int32)
    freq_ids = index_f * tm_count + residue
    lam = jnp.stack(shift_parts(freq_ids, total_steps))

    top, bottom = halo_pair(spectrum, "space", 2, HALO)
    diff_frame, mask_frame = frames(diffusivity, space_place, space_count)
    grid_angle = (index_f[:, None] * freq_ids[None, :] % total_steps).astype(jnp.float32) * (
        2.0 * math.pi / total_steps
    )
    cosine = jnp.cos(grid_angle)
    sine = jnp.sin(grid_angle)
    table = jnp.concatenate(
        [jnp.concatenate([cosine, -sine], 1), jnp.concatenate([sine, cosine], 1)], 0
    )
    device = jnp.reshape(tm_place, (1,)).astype(jnp.int32)
    outgoing = sweep_call(device, lam, spectrum, top, bottom, diff_frame, mask_frame, table, tm_count)
    col_block = col_count // tm_count
    outgoing = [piece.reshape(2, local_count * row_count, col_block) for piece in outgoing]
    arrived = xor_exchange(outgoing, "tm")

    slot = jnp.arange(tm_count, dtype=jnp.int32)
    target = tm_place ^ slot
    source_residue = reverse_bits(target, bit_count)
    class_angle = (target[:, None] * source_residue[None, :] % tm_count).astype(jnp.float32) * (
        2.0 * math.pi / tm_count
    )
    weights = jnp.stack([jnp.cos(class_angle), jnp.sin(class_angle)])
    step_ids = (target[:, None] * local_count + index_f[None, :]).astype(jnp.float32)
    factor = jnp.exp(step_ids * (-math.log(alpha_wrap) / total_steps)) / math.sqrt(total_steps)
    combined = combine_call(weights, factor, arrived, Q_BLOCK)
    returned = xor_exchange(combined, "tm")
    placed = place_call(device, returned, Q_BLOCK)
    return placed.reshape(2, local_count, row_count, col_count)


def solution(mesh):
    in_specs = (P(None, "tm", "space", None), P("space", None))
    out_specs = P(None, "tm", "space", None)
    return jax.shard_map(
        on_device, mesh=mesh, in_specs=in_specs, out_specs=out_specs, check_vma=False
    )
```

```python
import functools
import math

import jax
import jax.numpy as jnp
import numpy as np
from jax import lax
from jax.experimental import pallas as pl
from jax.experimental.pallas import tpu as pltpu
from jax.sharding import PartitionSpec as P

alpha_wrap = 0.25
step_rate = 0.5
flow_speed = 2.0
sweep_weights = [
    1.0 / (1.0 + 0.7 * math.cos(math.pi * (2 * order + 1) / 6.0)) for order in range(3)
]
Q_BLOCK = 16
XOR_ORDER = (6, 2, 5, 7, 3, 1, 4)
F_BLOCK = 4
HALO = 2


def reverse_bits(number, bit_count):
    result = number * 0
    for bit_place in range(bit_count):
        result = result + (number >> bit_place & 1) * (1 << bit_count - 1 - bit_place)
    return result


def shift_parts(freq_ids, total_steps):
    phase_angle = freq_ids.astype(jnp.float32) * (2.0 * math.pi / total_steps)
    root_scale = alpha_wrap ** (1.0 / total_steps)
    return (
        step_rate * (1.0 - root_scale * jnp.cos(phase_angle)),
        step_rate * root_scale * jnp.sin(phase_angle),
    )


def halo_pair(block, axis, dim, width):
    count = lax.axis_size(axis)
    forward = [(i, i + 1) for i in range(count - 1)]
    backward = [(i + 1, i) for i in range(count - 1)]
    size = block.shape[dim]
    top = lax.ppermute(lax.slice_in_dim(block, size - width, size, axis=dim), axis, forward)
    bottom = lax.ppermute(lax.slice_in_dim(block, 0, width, axis=dim), axis, backward)
    return top, bottom


def edge_kernel(rhs_ref, top_ref, bot_ref):
    rows = rhs_ref.shape[2]
    for f in range(rhs_ref.shape[1]):
        for x in range(2):
            tile = rhs_ref[x, f]
            top_ref[x, f] = tile[rows - HALO:rows]
            bot_ref[x, f] = tile[0:HALO]


def edge_call(spectrum):
    _, count, rows, cols = spectrum.shape
    block = 8
    edge = pl.BlockSpec((2, block, HALO, cols), lambda g: (0, g, 0, 0))
    shape = jax.ShapeDtypeStruct((2, count, HALO, cols), jnp.float32)
    return pl.pallas_call(
        edge_kernel,
        out_shape=[shape, shape],
        grid=(count // block,),
        in_specs=[pl.BlockSpec((2, block, rows, cols), lambda g: (0, g, 0, 0))],
        out_specs=[edge, edge],
        compiler_params=pltpu.CompilerParams(dimension_semantics=("arbitrary",)),
    )(spectrum)


def sweep_kernel(dev_ref, lam_ref, rhs_ref, top_ref, bot_ref, diff_ref, mask_ref, table_ref, *rest):
    out_refs, field = rest[:-1], rest[-1]
    block = rhs_ref.shape[1]
    count = lam_ref.shape[1]
    cols = rhs_ref.shape[3]
    base = pl.program_id(0) * block
    diff = diff_ref[...]
    diag_base = 4.0 * diff + flow_speed
    keep = mask_ref[...]
    row8 = lax.broadcasted_iota(jnp.int32, (8, cols), 0)
    col = lax.broadcasted_iota(jnp.int32, (16, cols), 1)

    def frame(x, f):
        local = rhs_ref[x, f]
        bv = bot_ref[x, f]
        tv = top_ref[x, f]
        hi = jnp.where(row8 == 0, jnp.broadcast_to(bv[0:1], (8, cols)), 0.0)
        hi = jnp.where(row8 == 1, jnp.broadcast_to(bv[1:2], (8, cols)), hi)
        hi = jnp.where(row8 == 6, jnp.broadcast_to(tv[0:1], (8, cols)), hi)
        hi = jnp.where(row8 == 7, jnp.broadcast_to(tv[1:2], (8, cols)), hi)
        return jnp.concatenate([local, hi], axis=0)

    def around(v):
        north = pltpu.roll(v, 1, 0)
        south = pltpu.roll(v, 15, 0)
        west = jnp.where(col == 0, 0.0, pltpu.roll(v, 1, 1))
        east = jnp.where(col == cols - 1, 0.0, pltpu.roll(v, cols - 1, 1))
        return north, north + south + west + east

    def body(f, carry):
        lam_r = lam_ref[0, base + f]
        lam_i = lam_ref[1, base + f]
        dr = diag_base + lam_r
        inv_mag = 1.0 / (dr * dr + lam_i * lam_i)
        r_re = frame(0, f)
        r_im = frame(1, f)
        c_re = sweep_weights[0] * ((r_re * dr + r_im * lam_i) * inv_mag)
        c_im = sweep_weights[0] * ((r_im * dr - r_re * lam_i) * inv_mag)
        for order in (1, 2):
            n_re, b_re = around(c_re)
            n_im, b_im = around(c_im)
            a_re = dr * c_re - lam_i * c_im - diff * b_re - flow_speed * n_re
            a_im = dr * c_im + lam_i * c_re - diff * b_im - flow_speed * n_im
            s_re = r_re - a_re
            s_im = r_im - a_im
            c_re = c_re + sweep_weights[order] * ((s_re * dr + s_im * lam_i) * inv_mag)
            c_im = c_im + sweep_weights[order] * ((s_im * dr - s_re * lam_i) * inv_mag)
            if order == 1:
                c_re = c_re * keep
                c_im = c_im * keep
        width = field.shape[2]
        for blk in range(field.shape[0]):
            lanes = slice(blk * width, (blk + 1) * width)
            field[blk, pl.ds(pl.multiple_of((base + f) * 8, 8), 8), :] = c_re[0:8, lanes]
            field[blk, pl.ds(pl.multiple_of((count + base + f) * 8, 8), 8), :] = c_im[0:8, lanes]
        return carry

    lax.fori_loop(0, block, body, 0)

    @pl.when(pl.program_id(0) == pl.num_programs(0) - 1)
    def _():
        table = table_ref[...]
        device = dev_ref[0]
        for slot, o_ref in enumerate(out_refs):
            source = field.at[device ^ slot]
            for r in range(8):
                plane = source[pl.ds(r, 2 * count, stride=8), :]
                o_ref[pl.ds(r, 2 * count, stride=8), :] = jnp.dot(
                    table, plane, precision=lax.Precision.HIGHEST, preferred_element_type=jnp.float32
                )


def sweep_call(device, lam, spectrum, top, bottom, diff_frame, mask_frame, table, blocks):
    _, count, rows, cols = spectrum.shape
    block = F_BLOCK
    width = cols // blocks
    big = pl.BlockSpec((2, block, rows, cols), lambda g: (0, g, 0, 0))
    edge = pl.BlockSpec((2, block, HALO, cols), lambda g: (0, g, 0, 0))
    whole = pl.BlockSpec((16, cols), lambda g: (0, 0))
    square = pl.BlockSpec((2 * count, 2 * count), lambda g: (0, 0))
    out_rows = 2 * count * rows
    return pl.pallas_call(
        sweep_kernel,
        out_shape=[jax.ShapeDtypeStruct((out_rows, width), jnp.float32)] * blocks,
        grid=(count // block,),
        in_specs=[pl.BlockSpec(memory_space=pltpu.SMEM)] * 2 + [big, edge, edge, whole, whole, square],
        out_specs=[pl.BlockSpec((out_rows, width), lambda g: (0, 0))] * blocks,
        scratch_shapes=[pltpu.VMEM((blocks, out_rows, width), jnp.float32)],
        compiler_params=pltpu.CompilerParams(dimension_semantics=("arbitrary",)),
        cost_estimate=pl.CostEstimate(
            flops=200 * spectrum.size, transcendentals=0, bytes_accessed=8 * spectrum.size
        ),
    )(device, lam, spectrum, top, bottom, diff_frame, mask_frame, table)


def combine_kernel(w_ref, fac_ref, *refs):
    count = len(refs) // 2
    in_refs, out_refs = refs[:count], refs[count:]
    block = in_refs[0].shape[1] // 8
    base = pl.program_id(0) * block

    def body(qi, carry):
        rows = pl.ds(pl.multiple_of(qi * 8, 8), 8)
        parts = [(ref[0, rows, :], ref[1, rows, :]) for ref in in_refs]
        for so, o_ref in enumerate(out_refs):
            acc_re = None
            acc_im = None
            for si, (x_re, x_im) in enumerate(parts):
                c = w_ref[0, so, si]
                s = w_ref[1, so, si]
                t_re = c * x_re - s * x_im
                t_im = s * x_re + c * x_im
                acc_re = t_re if acc_re is None else acc_re + t_re
                acc_im = t_im if acc_im is None else acc_im + t_im
            scale = fac_ref[so, base + qi]
            o_ref[0, rows, :] = acc_re * scale
            o_ref[1, rows, :] = acc_im * scale
        return carry

    lax.fori_loop(0, block, body, 0)


def combine_call(weights, factor, slots, q_block):
    _, rows, width = slots[0].shape
    spec = pl.BlockSpec((2, q_block * 8, width), lambda g: (0, g, 0))
    count = len(slots)
    return pl.pallas_call(
        combine_kernel,
        out_shape=[jax.ShapeDtypeStruct(slots[0].shape, jnp.float32)] * count,
        grid=(rows // (q_block * 8),),
        in_specs=[pl.BlockSpec(memory_space=pltpu.SMEM)] * 2 + [spec] * count,
        out_specs=[spec] * count,
        compiler_params=pltpu.CompilerParams(dimension_semantics=("arbitrary",)),
        cost_estimate=pl.CostEstimate(
            flops=64 * count * slots[0].size, transcendentals=0, bytes_accessed=8 * count * slots[0].size
        ),
    )(weights, factor, *slots)


def place_kernel(dev_ref, *refs):
    count = len(refs) - 1
    in_refs, o_ref = refs[:count], refs[count]
    width = in_refs[0].shape[2]
    device = dev_ref[0]
    for slot, ref in enumerate(in_refs):
        start = pl.multiple_of((device ^ slot) * width, width)
        o_ref[:, :, pl.ds(start, width)] = ref[...]


def place_call(device, slots, q_block):
    _, rows, width = slots[0].shape
    count = len(slots)
    spec = pl.BlockSpec((2, q_block * 8, width), lambda g: (0, g, 0))
    return pl.pallas_call(
        place_kernel,
        out_shape=jax.ShapeDtypeStruct((2, rows, width * count), jnp.float32),
        grid=(rows // (q_block * 8),),
        in_specs=[pl.BlockSpec(memory_space=pltpu.SMEM)] + [spec] * count,
        out_specs=pl.BlockSpec((2, q_block * 8, width * count), lambda g: (0, g, 0)),
        compiler_params=pltpu.CompilerParams(dimension_semantics=("arbitrary",)),
    )(device, *slots)


def xor_exchange(slots, axis):
    received = [slots[0]] + [None] * (len(slots) - 1)
    for slot in XOR_ORDER:
        pairs = [(i, i ^ slot) for i in range(len(slots))]
        received[slot] = lax.ppermute(slots[slot], axis, pairs)
    return received


def frames(diffusivity, space_place, space_count):
    rows, cols = diffusivity.shape
    d_top, d_bot = halo_pair(diffusivity, "space", 0, HALO)
    gap = jnp.zeros((16 - rows - 2 * HALO, cols), jnp.float32)
    diff_frame = jnp.concatenate([diffusivity, d_bot, gap, d_top], axis=0)
    row = jnp.arange(16, dtype=jnp.int32)
    keep = (row < rows) | ((row == rows) & (space_place < space_count - 1)) | (
        (row == 15) & (space_place > 0)
    )
    mask_frame = jnp.broadcast_to(keep.astype(jnp.float32)[:, None], (16, cols))
    return diff_frame, mask_frame


def on_device(spectrum, diffusivity):
    local_count = spectrum.shape[1]
    row_count = spectrum.shape[2]
    col_count = spectrum.shape[3]
    tm_count = lax.axis_size("tm")
    space_count = lax.axis_size("space")
    bit_count = tm_count.bit_length() - 1
    total_steps = local_count * tm_count
    tm_place = lax.axis_index("tm")
    space_place = lax.axis_index("space")
    residue = reverse_bits(tm_place, bit_count)
    index_f = jnp.arange(local_count, dtype=jnp.int32)
    freq_ids = index_f * tm_count + residue
    lam = jnp.stack(shift_parts(freq_ids, total_steps))

    low_rows, high_rows = edge_call(spectrum)
    space_ring = lax.axis_size("space")
    top = lax.ppermute(low_rows, "space", [(i, i + 1) for i in range(space_ring - 1)])
    bottom = lax.ppermute(high_rows, "space", [(i + 1, i) for i in range(space_ring - 1)])
    diff_frame, mask_frame = frames(diffusivity, space_place, space_count)
    grid_angle = (index_f[:, None] * freq_ids[None, :] % total_steps).astype(jnp.float32) * (
        2.0 * math.pi / total_steps
    )
    cosine = jnp.cos(grid_angle)
    sine = jnp.sin(grid_angle)
    table = jnp.concatenate(
        [jnp.concatenate([cosine, -sine], 1), jnp.concatenate([sine, cosine], 1)], 0
    )
    device = jnp.reshape(tm_place, (1,)).astype(jnp.int32)
    outgoing = sweep_call(device, lam, spectrum, top, bottom, diff_frame, mask_frame, table, tm_count)
    col_block = col_count // tm_count
    outgoing = [piece.reshape(2, local_count * row_count, col_block) for piece in outgoing]
    arrived = xor_exchange(outgoing, "tm")

    slot = jnp.arange(tm_count, dtype=jnp.int32)
    target = tm_place ^ slot
    source_residue = reverse_bits(target, bit_count)
    class_angle = (target[:, None] * source_residue[None, :] % tm_count).astype(jnp.float32) * (
        2.0 * math.pi / tm_count
    )
    weights = jnp.stack([jnp.cos(class_angle), jnp.sin(class_angle)])
    step_ids = (target[:, None] * local_count + index_f[None, :]).astype(jnp.float32)
    factor = jnp.exp(step_ids * (-math.log(alpha_wrap) / total_steps)) / math.sqrt(total_steps)
    combined = combine_call(weights, factor, arrived, Q_BLOCK)
    returned = xor_exchange(combined, "tm")
    placed = place_call(device, returned, Q_BLOCK)
    return placed.reshape(2, local_count, row_count, col_count)


def solution(mesh):
    in_specs = (P(None, "tm", "space", None), P("space", None))
    out_specs = P(None, "tm", "space", None)
    return jax.shard_map(
        on_device, mesh=mesh, in_specs=in_specs, out_specs=out_specs, check_vma=False
    )
```

```python
import functools
import math

import jax
import jax.numpy as jnp
import numpy as np
from jax import lax
from jax.experimental import pallas as pl
from jax.experimental.pallas import tpu as pltpu
from jax.sharding import PartitionSpec as P

alpha_wrap = 0.25
step_rate = 0.5
flow_speed = 2.0
sweep_weights = [
    1.0 / (1.0 + 0.7 * math.cos(math.pi * (2 * order + 1) / 6.0)) for order in range(3)
]
Q_BLOCK = 16
F_BLOCK = 4
HALO = 2


def reverse_bits(number, bit_count):
    result = number * 0
    for bit_place in range(bit_count):
        result = result + (number >> bit_place & 1) * (1 << bit_count - 1 - bit_place)
    return result


def shift_parts(freq_ids, total_steps):
    phase_angle = freq_ids.astype(jnp.float32) * (2.0 * math.pi / total_steps)
    root_scale = alpha_wrap ** (1.0 / total_steps)
    return (
        step_rate * (1.0 - root_scale * jnp.cos(phase_angle)),
        step_rate * root_scale * jnp.sin(phase_angle),
    )


def halo_pair(block, axis, dim, width):
    count = lax.axis_size(axis)
    forward = [(i, i + 1) for i in range(count - 1)]
    backward = [(i + 1, i) for i in range(count - 1)]
    size = block.shape[dim]
    top = lax.ppermute(lax.slice_in_dim(block, size - width, size, axis=dim), axis, forward)
    bottom = lax.ppermute(lax.slice_in_dim(block, 0, width, axis=dim), axis, backward)
    return top, bottom


def sweep_kernel(dev_ref, lam_ref, rhs_ref, top_ref, bot_ref, diff_ref, mask_ref, table_ref, *rest):
    out_refs, field = rest[:-1], rest[-1]
    block = rhs_ref.shape[1]
    count = lam_ref.shape[1]
    cols = rhs_ref.shape[3]
    base = pl.program_id(0) * block
    diff = diff_ref[...]
    diag_base = 4.0 * diff + flow_speed
    keep = mask_ref[...]
    row8 = lax.broadcasted_iota(jnp.int32, (8, cols), 0)
    col = lax.broadcasted_iota(jnp.int32, (16, cols), 1)

    def frame(x, f):
        local = rhs_ref[x, f]
        bv = bot_ref[x, f]
        tv = top_ref[x, f]
        hi = jnp.where(row8 == 0, jnp.broadcast_to(bv[0:1], (8, cols)), 0.0)
        hi = jnp.where(row8 == 1, jnp.broadcast_to(bv[1:2], (8, cols)), hi)
        hi = jnp.where(row8 == 6, jnp.broadcast_to(tv[0:1], (8, cols)), hi)
        hi = jnp.where(row8 == 7, jnp.broadcast_to(tv[1:2], (8, cols)), hi)
        return jnp.concatenate([local, hi], axis=0)

    def around(v):
        north = pltpu.roll(v, 1, 0)
        south = pltpu.roll(v, 15, 0)
        west = jnp.where(col == 0, 0.0, pltpu.roll(v, 1, 1))
        east = jnp.where(col == cols - 1, 0.0, pltpu.roll(v, cols - 1, 1))
        return north, north + south + west + east

    def body(f, carry):
        lam_r = lam_ref[0, base + f]
        lam_i = lam_ref[1, base + f]
        dr = diag_base + lam_r
        inv_mag = 1.0 / (dr * dr + lam_i * lam_i)
        r_re = frame(0, f)
        r_im = frame(1, f)
        c_re = sweep_weights[0] * ((r_re * dr + r_im * lam_i) * inv_mag)
        c_im = sweep_weights[0] * ((r_im * dr - r_re * lam_i) * inv_mag)
        for order in (1, 2):
            n_re, b_re = around(c_re)
            n_im, b_im = around(c_im)
            a_re = dr * c_re - lam_i * c_im - diff * b_re - flow_speed * n_re
            a_im = dr * c_im + lam_i * c_re - diff * b_im - flow_speed * n_im
            s_re = r_re - a_re
            s_im = r_im - a_im
            c_re = c_re + sweep_weights[order] * ((s_re * dr + s_im * lam_i) * inv_mag)
            c_im = c_im + sweep_weights[order] * ((s_im * dr - s_re * lam_i) * inv_mag)
            if order == 1:
                c_re = c_re * keep
                c_im = c_im * keep
        width = field.shape[2]
        for blk in range(field.shape[0]):
            lanes = slice(blk * width, (blk + 1) * width)
            field[blk, pl.ds(pl.multiple_of((base + f) * 8, 8), 8), :] = c_re[0:8, lanes]
            field[blk, pl.ds(pl.multiple_of((count + base + f) * 8, 8), 8), :] = c_im[0:8, lanes]
        return carry

    lax.fori_loop(0, block, body, 0)

    @pl.when(pl.program_id(0) == pl.num_programs(0) - 1)
    def _():
        table = table_ref[...]
        device = dev_ref[0]
        for slot, o_ref in enumerate(out_refs):
            source = field.at[device ^ slot]
            for r in range(8):
                plane = source[pl.ds(r, 2 * count, stride=8), :]
                o_ref[pl.ds(r, 2 * count, stride=8), :] = jnp.dot(
                    table, plane, precision=lax.Precision.HIGHEST, preferred_element_type=jnp.float32
                )


def sweep_call(device, lam, spectrum, top, bottom, diff_frame, mask_frame, table, blocks):
    _, count, rows, cols = spectrum.shape
    block = F_BLOCK
    width = cols // blocks
    big = pl.BlockSpec((2, block, rows, cols), lambda g: (0, g, 0, 0))
    edge = pl.BlockSpec((2, block, HALO, cols), lambda g: (0, g, 0, 0))
    whole = pl.BlockSpec((16, cols), lambda g: (0, 0))
    square = pl.BlockSpec((2 * count, 2 * count), lambda g: (0, 0))
    out_rows = 2 * count * rows
    return pl.pallas_call(
        sweep_kernel,
        out_shape=[jax.ShapeDtypeStruct((out_rows, width), jnp.float32)] * blocks,
        grid=(count // block,),
        in_specs=[pl.BlockSpec(memory_space=pltpu.SMEM)] * 2 + [big, edge, edge, whole, whole, square],
        out_specs=[pl.BlockSpec((out_rows, width), lambda g: (0, 0))] * blocks,
        scratch_shapes=[pltpu.VMEM((blocks, out_rows, width), jnp.float32)],
        compiler_params=pltpu.CompilerParams(dimension_semantics=("arbitrary",)),
        cost_estimate=pl.CostEstimate(
            flops=200 * spectrum.size, transcendentals=0, bytes_accessed=8 * spectrum.size
        ),
    )(device, lam, spectrum, top, bottom, diff_frame, mask_frame, table)


def combine_kernel(w_ref, fac_ref, *refs):
    count = len(refs) // 2
    in_refs, out_refs = refs[:count], refs[count:]
    block = in_refs[0].shape[1] // 8
    base = pl.program_id(0) * block

    def body(qi, carry):
        rows = pl.ds(pl.multiple_of(qi * 8, 8), 8)
        parts = [(ref[0, rows, :], ref[1, rows, :]) for ref in in_refs]
        for so, o_ref in enumerate(out_refs):
            acc_re = None
            acc_im = None
            for si, (x_re, x_im) in enumerate(parts):
                c = w_ref[0, so, si]
                s = w_ref[1, so, si]
                t_re = c * x_re - s * x_im
                t_im = s * x_re + c * x_im
                acc_re = t_re if acc_re is None else acc_re + t_re
                acc_im = t_im if acc_im is None else acc_im + t_im
            scale = fac_ref[so, base + qi]
            o_ref[0, rows, :] = acc_re * scale
            o_ref[1, rows, :] = acc_im * scale
        return carry

    lax.fori_loop(0, block, body, 0)


def combine_call(weights, factor, slots, q_block):
    _, rows, width = slots[0].shape
    spec = pl.BlockSpec((2, q_block * 8, width), lambda g: (0, g, 0))
    count = len(slots)
    return pl.pallas_call(
        combine_kernel,
        out_shape=[jax.ShapeDtypeStruct(slots[0].shape, jnp.float32)] * count,
        grid=(rows // (q_block * 8),),
        in_specs=[pl.BlockSpec(memory_space=pltpu.SMEM)] * 2 + [spec] * count,
        out_specs=[spec] * count,
        compiler_params=pltpu.CompilerParams(dimension_semantics=("arbitrary",)),
        cost_estimate=pl.CostEstimate(
            flops=64 * count * slots[0].size, transcendentals=0, bytes_accessed=8 * count * slots[0].size
        ),
    )(weights, factor, *slots)


def place_kernel(dev_ref, *refs):
    count = len(refs) - 1
    in_refs, o_ref = refs[:count], refs[count]
    width = in_refs[0].shape[2]
    device = dev_ref[0]
    for slot, ref in enumerate(in_refs):
        start = pl.multiple_of((device ^ slot) * width, width)
        o_ref[:, :, pl.ds(start, width)] = ref[...]


def place_call(device, slots, q_block):
    _, rows, width = slots[0].shape
    count = len(slots)
    spec = pl.BlockSpec((2, q_block * 8, width), lambda g: (0, g, 0))
    return pl.pallas_call(
        place_kernel,
        out_shape=jax.ShapeDtypeStruct((2, rows, width * count), jnp.float32),
        grid=(rows // (q_block * 8),),
        in_specs=[pl.BlockSpec(memory_space=pltpu.SMEM)] + [spec] * count,
        out_specs=pl.BlockSpec((2, q_block * 8, width * count), lambda g: (0, g, 0)),
        compiler_params=pltpu.CompilerParams(dimension_semantics=("arbitrary",)),
    )(device, *slots)


def xor_exchange(slots, axis):
    count = len(slots)
    ring = 4

    def along(step, flip):
        return [(i, ((i & ring) ^ flip) | ((i + step) % ring)) for i in range(count)]

    received = [slots[0]] + [None] * (count - 1)
    for slot in range(1, count):
        if slot & 3 != 2:
            received[slot] = lax.ppermute(slots[slot], axis, [(i, i ^ slot) for i in range(count)])
            continue
        flip = slot & ring
        halves = []
        for step, piece in ((1, slots[slot][0:1]), (ring - 1, slots[slot][1:2])):
            hop = lax.ppermute(piece, axis, along(step, 0))
            halves.append(lax.ppermute(hop, axis, along(step, flip)))
        received[slot] = jnp.concatenate(halves, axis=0)
    return received


def frames(diffusivity, space_place, space_count):
    rows, cols = diffusivity.shape
    d_top, d_bot = halo_pair(diffusivity, "space", 0, HALO)
    gap = jnp.zeros((16 - rows - 2 * HALO, cols), jnp.float32)
    diff_frame = jnp.concatenate([diffusivity, d_bot, gap, d_top], axis=0)
    row = jnp.arange(16, dtype=jnp.int32)
    keep = (row < rows) | ((row == rows) & (space_place < space_count - 1)) | (
        (row == 15) & (space_place > 0)
    )
    mask_frame = jnp.broadcast_to(keep.astype(jnp.float32)[:, None], (16, cols))
    return diff_frame, mask_frame


def on_device(spectrum, diffusivity):
    local_count = spectrum.shape[1]
    row_count = spectrum.shape[2]
    col_count = spectrum.shape[3]
    tm_count = lax.axis_size("tm")
    space_count = lax.axis_size("space")
    bit_count = tm_count.bit_length() - 1
    total_steps = local_count * tm_count
    tm_place = lax.axis_index("tm")
    space_place = lax.axis_index("space")
    residue = reverse_bits(tm_place, bit_count)
    index_f = jnp.arange(local_count, dtype=jnp.int32)
    freq_ids = index_f * tm_count + residue
    lam = jnp.stack(shift_parts(freq_ids, total_steps))

    top, bottom = halo_pair(spectrum, "space", 2, HALO)
    diff_frame, mask_frame = frames(diffusivity, space_place, space_count)
    grid_angle = (index_f[:, None] * freq_ids[None, :] % total_steps).astype(jnp.float32) * (
        2.0 * math.pi / total_steps
    )
    cosine = jnp.cos(grid_angle)
    sine = jnp.sin(grid_angle)
    table = jnp.concatenate(
        [jnp.concatenate([cosine, -sine], 1), jnp.concatenate([sine, cosine], 1)], 0
    )
    device = jnp.reshape(tm_place, (1,)).astype(jnp.int32)
    outgoing = sweep_call(device, lam, spectrum, top, bottom, diff_frame, mask_frame, table, tm_count)
    col_block = col_count // tm_count
    outgoing = [piece.reshape(2, local_count * row_count, col_block) for piece in outgoing]
    arrived = xor_exchange(outgoing, "tm")

    slot = jnp.arange(tm_count, dtype=jnp.int32)
    target = tm_place ^ slot
    source_residue = reverse_bits(target, bit_count)
    class_angle = (target[:, None] * source_residue[None, :] % tm_count).astype(jnp.float32) * (
        2.0 * math.pi / tm_count
    )
    weights = jnp.stack([jnp.cos(class_angle), jnp.sin(class_angle)])
    step_ids = (target[:, None] * local_count + index_f[None, :]).astype(jnp.float32)
    factor = jnp.exp(step_ids * (-math.log(alpha_wrap) / total_steps)) / math.sqrt(total_steps)
    combined = combine_call(weights, factor, arrived, Q_BLOCK)
    returned = xor_exchange(combined, "tm")
    placed = place_call(device, returned, Q_BLOCK)
    return placed.reshape(2, local_count, row_count, col_count)


def solution(mesh):
    in_specs = (P(None, "tm", "space", None), P("space", None))
    out_specs = P(None, "tm", "space", None)
    return jax.shard_map(
        on_device, mesh=mesh, in_specs=in_specs, out_specs=out_specs, check_vma=False
    )
```

```python
import functools
import math

import jax
import jax.numpy as jnp
import numpy as np
from jax import lax
from jax.experimental import pallas as pl
from jax.experimental.pallas import tpu as pltpu
from jax.sharding import PartitionSpec as P

alpha_wrap = 0.25
step_rate = 0.5
flow_speed = 2.0
sweep_weights = [
    1.0 / (1.0 + 0.7 * math.cos(math.pi * (2 * order + 1) / 6.0)) for order in range(3)
]
Q_BLOCK = 16
F_BLOCK = 4
HALO = 2


def reverse_bits(number, bit_count):
    result = number * 0
    for bit_place in range(bit_count):
        result = result + (number >> bit_place & 1) * (1 << bit_count - 1 - bit_place)
    return result


def shift_parts(freq_ids, total_steps):
    phase_angle = freq_ids.astype(jnp.float32) * (2.0 * math.pi / total_steps)
    root_scale = alpha_wrap ** (1.0 / total_steps)
    return (
        step_rate * (1.0 - root_scale * jnp.cos(phase_angle)),
        step_rate * root_scale * jnp.sin(phase_angle),
    )


def halo_pair(block, axis, dim, width):
    count = lax.axis_size(axis)
    forward = [(i, i + 1) for i in range(count - 1)]
    backward = [(i + 1, i) for i in range(count - 1)]
    size = block.shape[dim]
    top = lax.ppermute(lax.slice_in_dim(block, size - width, size, axis=dim), axis, forward)
    bottom = lax.ppermute(lax.slice_in_dim(block, 0, width, axis=dim), axis, backward)
    return top, bottom


def sweep_kernel(lam_ref, rhs_ref, top_ref, bot_ref, diff_ref, mask_ref, table_ref, o_ref, field):
    block = rhs_ref.shape[1]
    count = lam_ref.shape[1]
    cols = rhs_ref.shape[3]
    base = pl.program_id(0) * block
    diff = diff_ref[...]
    diag_base = 4.0 * diff + flow_speed
    keep = mask_ref[...]
    row8 = lax.broadcasted_iota(jnp.int32, (8, cols), 0)
    col = lax.broadcasted_iota(jnp.int32, (16, cols), 1)

    def frame(x, f):
        local = rhs_ref[x, f]
        bv = bot_ref[x, f]
        tv = top_ref[x, f]
        hi = jnp.where(row8 == 0, jnp.broadcast_to(bv[0:1], (8, cols)), 0.0)
        hi = jnp.where(row8 == 1, jnp.broadcast_to(bv[1:2], (8, cols)), hi)
        hi = jnp.where(row8 == 6, jnp.broadcast_to(tv[0:1], (8, cols)), hi)
        hi = jnp.where(row8 == 7, jnp.broadcast_to(tv[1:2], (8, cols)), hi)
        return jnp.concatenate([local, hi], axis=0)

    def around(v):
        north = pltpu.roll(v, 1, 0)
        south = pltpu.roll(v, 15, 0)
        west = jnp.where(col == 0, 0.0, pltpu.roll(v, 1, 1))
        east = jnp.where(col == cols - 1, 0.0, pltpu.roll(v, cols - 1, 1))
        return north, north + south + west + east

    def body(f, carry):
        lam_r = lam_ref[0, base + f]
        lam_i = lam_ref[1, base + f]
        dr = diag_base + lam_r
        inv_mag = 1.0 / (dr * dr + lam_i * lam_i)
        r_re = frame(0, f)
        r_im = frame(1, f)
        c_re = sweep_weights[0] * ((r_re * dr + r_im * lam_i) * inv_mag)
        c_im = sweep_weights[0] * ((r_im * dr - r_re * lam_i) * inv_mag)
        for order in (1, 2):
            n_re, b_re = around(c_re)
            n_im, b_im = around(c_im)
            if order == 2:
                n_re, b_re, n_im, b_im = n_re[0:8], b_re[0:8], n_im[0:8], b_im[0:8]
                c_re, c_im, r_re, r_im = c_re[0:8], c_im[0:8], r_re[0:8], r_im[0:8]
                dr, inv_mag, d = dr[0:8], inv_mag[0:8], diff[0:8]
            else:
                d = diff
            a_re = dr * c_re - lam_i * c_im - d * b_re - flow_speed * n_re
            a_im = dr * c_im + lam_i * c_re - d * b_im - flow_speed * n_im
            s_re = r_re - a_re
            s_im = r_im - a_im
            c_re = c_re + sweep_weights[order] * ((s_re * dr + s_im * lam_i) * inv_mag)
            c_im = c_im + sweep_weights[order] * ((s_im * dr - s_re * lam_i) * inv_mag)
            if order == 1:
                c_re = c_re * keep
                c_im = c_im * keep
        width = field.shape[2]
        for blk in range(field.shape[0]):
            lanes = slice(blk * width, (blk + 1) * width)
            field[blk, pl.ds(pl.multiple_of((base + f) * 8, 8), 8), :] = c_re[0:8, lanes]
            field[blk, pl.ds(pl.multiple_of((count + base + f) * 8, 8), 8), :] = c_im[0:8, lanes]
        return carry

    lax.fori_loop(0, block, body, 0)

    @pl.when(pl.program_id(0) == pl.num_programs(0) - 1)
    def _():
        table = table_ref[...]
        for blk in range(o_ref.shape[0]):
            for r in range(8):
                plane = field[blk, pl.ds(r, 2 * count, stride=8), :]
                o_ref[blk, pl.ds(r, 2 * count, stride=8), :] = jnp.dot(
                    table, plane, precision=lax.Precision.HIGHEST, preferred_element_type=jnp.float32
                )


def sweep_call(lam, spectrum, top, bottom, diff_frame, mask_frame, table, blocks):
    _, count, rows, cols = spectrum.shape
    block = F_BLOCK
    width = cols // blocks
    big = pl.BlockSpec((2, block, rows, cols), lambda g: (0, g, 0, 0))
    edge = pl.BlockSpec((2, block, HALO, cols), lambda g: (0, g, 0, 0))
    whole = pl.BlockSpec((16, cols), lambda g: (0, 0))
    square = pl.BlockSpec((2 * count, 2 * count), lambda g: (0, 0))
    out_rows = 2 * count * rows
    return pl.pallas_call(
        sweep_kernel,
        out_shape=jax.ShapeDtypeStruct((blocks, out_rows, width), jnp.float32),
        grid=(count // block,),
        in_specs=[pl.BlockSpec(memory_space=pltpu.SMEM), big, edge, edge, whole, whole, square],
        out_specs=pl.BlockSpec((blocks, out_rows, width), lambda g: (0, 0, 0)),
        scratch_shapes=[pltpu.VMEM((blocks, out_rows, width), jnp.float32)],
        compiler_params=pltpu.CompilerParams(dimension_semantics=("arbitrary",)),
        cost_estimate=pl.CostEstimate(
            flops=200 * spectrum.size, transcendentals=0, bytes_accessed=8 * spectrum.size
        ),
    )(lam, spectrum, top, bottom, diff_frame, mask_frame, table)


def combine_kernel(weights, fac_ref, a_ref, o_ref):
    block = a_ref.shape[2] // 8
    base = pl.program_id(0) * block

    def body(qi, carry):
        rows = pl.ds(pl.multiple_of(qi * 8, 8), 8)
        parts = [(a_ref[s, 0, rows, :], a_ref[s, 1, rows, :]) for s in range(a_ref.shape[0])]
        for m, row in enumerate(weights):
            acc_re = []
            acc_im = []
            for (c, s), (x_re, x_im) in zip(row, parts):
                for coef, val, acc in ((c, x_re, acc_re), (-s, x_im, acc_re), (s, x_re, acc_im), (c, x_im, acc_im)):
                    if coef == 1.0:
                        acc.append(val)
                    elif coef == -1.0:
                        acc.append(-val)
                    elif coef != 0.0:
                        acc.append(coef * val)
            scale = fac_ref[m, base + qi]
            o_ref[m, 0, rows, :] = sum(acc_re[1:], acc_re[0]) * scale
            o_ref[m, 1, rows, :] = sum(acc_im[1:], acc_im[0]) * scale
        return carry

    lax.fori_loop(0, block, body, 0)


def combine_call(weights, factor, arrived, q_block):
    blocks, _, rows, width = arrived.shape
    spec = pl.BlockSpec((blocks, 2, q_block * 8, width), lambda g: (0, 0, g, 0))
    return pl.pallas_call(
        functools.partial(combine_kernel, weights),
        out_shape=jax.ShapeDtypeStruct(arrived.shape, jnp.float32),
        grid=(rows // (q_block * 8),),
        in_specs=[pl.BlockSpec(memory_space=pltpu.SMEM), spec],
        out_specs=spec,
        compiler_params=pltpu.CompilerParams(dimension_semantics=("arbitrary",)),
        cost_estimate=pl.CostEstimate(
            flops=40 * arrived.size, transcendentals=0, bytes_accessed=8 * arrived.size
        ),
    )(factor, arrived)


def class_weights(tm_count, bit_count):
    rows = []
    for m in range(tm_count):
        row = []
        for source in range(tm_count):
            angle = 2.0 * math.pi * ((m * reverse_bits(source, bit_count)) % tm_count) / tm_count
            c, s = math.cos(angle), math.sin(angle)
            c = float(np.float32(0.0 if abs(c) < 1e-9 else c))
            s = float(np.float32(0.0 if abs(s) < 1e-9 else s))
            row.append((c, s))
        rows.append(tuple(row))
    return tuple(rows)


def frames(diffusivity, space_place, space_count):
    rows, cols = diffusivity.shape
    d_top, d_bot = halo_pair(diffusivity, "space", 0, HALO)
    gap = jnp.zeros((16 - rows - 2 * HALO, cols), jnp.float32)
    diff_frame = jnp.concatenate([diffusivity, d_bot, gap, d_top], axis=0)
    row = jnp.arange(16, dtype=jnp.int32)
    keep = (row < rows) | ((row == rows) & (space_place < space_count - 1)) | (
        (row == 15) & (space_place > 0)
    )
    mask_frame = jnp.broadcast_to(keep.astype(jnp.float32)[:, None], (16, cols))
    return diff_frame, mask_frame


def on_device(spectrum, diffusivity):
    local_count = spectrum.shape[1]
    row_count = spectrum.shape[2]
    col_count = spectrum.shape[3]
    tm_count = lax.axis_size("tm")
    space_count = lax.axis_size("space")
    bit_count = tm_count.bit_length() - 1
    total_steps = local_count * tm_count
    tm_place = lax.axis_index("tm")
    space_place = lax.axis_index("space")
    residue = reverse_bits(tm_place, bit_count)
    index_f = jnp.arange(local_count, dtype=jnp.int32)
    freq_ids = index_f * tm_count + residue
    lam = jnp.stack(shift_parts(freq_ids, total_steps))

    top, bottom = halo_pair(spectrum, "space", 2, HALO)
    diff_frame, mask_frame = frames(diffusivity, space_place, space_count)
    grid_angle = (index_f[:, None] * freq_ids[None, :] % total_steps).astype(jnp.float32) * (
        2.0 * math.pi / total_steps
    )
    cosine = jnp.cos(grid_angle)
    sine = jnp.sin(grid_angle)
    table = jnp.concatenate(
        [jnp.concatenate([cosine, -sine], 1), jnp.concatenate([sine, cosine], 1)], 0
    )
    outgoing = sweep_call(lam, spectrum, top, bottom, diff_frame, mask_frame, table, tm_count)
    col_block = col_count // tm_count
    outgoing = outgoing.reshape(tm_count, 2, local_count * row_count, col_block)
    arrived = lax.all_to_all(outgoing, "tm", 0, 0, tiled=True)

    step_ids = (
        jnp.arange(tm_count, dtype=jnp.int32)[:, None] * local_count
        + jnp.arange(local_count, dtype=jnp.int32)[None, :]
    ).astype(jnp.float32)
    factor = jnp.exp(step_ids * (-math.log(alpha_wrap) / total_steps)) / math.sqrt(total_steps)
    combined = combine_call(class_weights(tm_count, bit_count), factor, arrived, Q_BLOCK)
    returned = lax.all_to_all(combined, "tm", 0, 0, tiled=True)
    returned = returned.reshape(tm_count, 2, local_count, row_count, col_block)
    return jnp.moveaxis(returned, 0, 3).reshape(2, local_count, row_count, col_count)


def solution(mesh):
    in_specs = (P(None, "tm", "space", None), P("space", None))
    out_specs = P(None, "tm", "space", None)
    return jax.shard_map(
        on_device, mesh=mesh, in_specs=in_specs, out_specs=out_specs, check_vma=False
    )
```

```python
import functools
import math

import jax
import jax.numpy as jnp
import numpy as np
from jax import lax
from jax.experimental import pallas as pl
from jax.experimental.pallas import tpu as pltpu
from jax.sharding import PartitionSpec as P

alpha_wrap = 0.25
step_rate = 0.5
flow_speed = 2.0
sweep_weights = [
    1.0 / (1.0 + 0.7 * math.cos(math.pi * (2 * order + 1) / 6.0)) for order in range(3)
]
Q_BLOCK = 16
F_BLOCK = 16
HALO = 2


def reverse_bits(number, bit_count):
    result = number * 0
    for bit_place in range(bit_count):
        result = result + (number >> bit_place & 1) * (1 << bit_count - 1 - bit_place)
    return result


def shift_parts(freq_ids, total_steps):
    phase_angle = freq_ids.astype(jnp.float32) * (2.0 * math.pi / total_steps)
    root_scale = alpha_wrap ** (1.0 / total_steps)
    return (
        step_rate * (1.0 - root_scale * jnp.cos(phase_angle)),
        step_rate * root_scale * jnp.sin(phase_angle),
    )


def halo_pair(block, axis, dim, width):
    count = lax.axis_size(axis)
    forward = [(i, i + 1) for i in range(count - 1)]
    backward = [(i + 1, i) for i in range(count - 1)]
    size = block.shape[dim]
    top = lax.ppermute(lax.slice_in_dim(block, size - width, size, axis=dim), axis, forward)
    bottom = lax.ppermute(lax.slice_in_dim(block, 0, width, axis=dim), axis, backward)
    return top, bottom


def sweep_kernel(lam_ref, rhs_ref, top_ref, bot_ref, diff_ref, mask_ref, table_ref, o_ref, field):
    block = rhs_ref.shape[1]
    count = lam_ref.shape[1]
    cols = rhs_ref.shape[3]
    base = pl.program_id(0) * block
    diff = diff_ref[...]
    diag_base = 4.0 * diff + flow_speed
    keep = mask_ref[...]
    row8 = lax.broadcasted_iota(jnp.int32, (8, cols), 0)
    col = lax.broadcasted_iota(jnp.int32, (16, cols), 1)

    def frame(x, f):
        local = rhs_ref[x, f]
        bv = bot_ref[x, f]
        tv = top_ref[x, f]
        hi = jnp.where(row8 == 0, jnp.broadcast_to(bv[0:1], (8, cols)), 0.0)
        hi = jnp.where(row8 == 1, jnp.broadcast_to(bv[1:2], (8, cols)), hi)
        hi = jnp.where(row8 == 6, jnp.broadcast_to(tv[0:1], (8, cols)), hi)
        hi = jnp.where(row8 == 7, jnp.broadcast_to(tv[1:2], (8, cols)), hi)
        return jnp.concatenate([local, hi], axis=0)

    def around(v):
        north = pltpu.roll(v, 1, 0)
        south = pltpu.roll(v, 15, 0)
        west = jnp.where(col == 0, 0.0, pltpu.roll(v, 1, 1))
        east = jnp.where(col == cols - 1, 0.0, pltpu.roll(v, cols - 1, 1))
        return north, north + south + west + east

    def body(f, carry):
        lam_r = lam_ref[0, base + f]
        lam_i = lam_ref[1, base + f]
        dr = diag_base + lam_r
        inv_mag = 1.0 / (dr * dr + lam_i * lam_i)
        r_re = frame(0, f)
        r_im = frame(1, f)
        c_re = sweep_weights[0] * ((r_re * dr + r_im * lam_i) * inv_mag)
        c_im = sweep_weights[0] * ((r_im * dr - r_re * lam_i) * inv_mag)
        for order in (1, 2):
            n_re, b_re = around(c_re)
            n_im, b_im = around(c_im)
            if order == 2:
                n_re, b_re, n_im, b_im = n_re[0:8], b_re[0:8], n_im[0:8], b_im[0:8]
                c_re, c_im, r_re, r_im = c_re[0:8], c_im[0:8], r_re[0:8], r_im[0:8]
                dr, inv_mag, d = dr[0:8], inv_mag[0:8], diff[0:8]
            else:
                d = diff
            a_re = dr * c_re - lam_i * c_im - d * b_re - flow_speed * n_re
            a_im = dr * c_im + lam_i * c_re - d * b_im - flow_speed * n_im
            s_re = r_re - a_re
            s_im = r_im - a_im
            c_re = c_re + sweep_weights[order] * ((s_re * dr + s_im * lam_i) * inv_mag)
            c_im = c_im + sweep_weights[order] * ((s_im * dr - s_re * lam_i) * inv_mag)
            if order == 1:
                c_re = c_re * keep
                c_im = c_im * keep
        width = field.shape[2]
        for blk in range(field.shape[0]):
            lanes = slice(blk * width, (blk + 1) * width)
            field[blk, pl.ds(pl.multiple_of((base + f) * 8, 8), 8), :] = c_re[0:8, lanes]
            field[blk, pl.ds(pl.multiple_of((count + base + f) * 8, 8), 8), :] = c_im[0:8, lanes]
        return carry

    lax.fori_loop(0, block, body, 0)

    @pl.when(pl.program_id(0) == pl.num_programs(0) - 1)
    def _():
        table = table_ref[...]
        for blk in range(o_ref.shape[0]):
            for r in range(8):
                plane = field[blk, pl.ds(r, 2 * count, stride=8), :]
                o_ref[blk, pl.ds(r, 2 * count, stride=8), :] = jnp.dot(
                    table, plane, precision=lax.Precision.HIGHEST, preferred_element_type=jnp.float32
                )


def sweep_call(lam, spectrum, top, bottom, diff_frame, mask_frame, table, blocks):
    _, count, rows, cols = spectrum.shape
    block = F_BLOCK
    width = cols // blocks
    big = pl.BlockSpec((2, block, rows, cols), lambda g: (0, g, 0, 0))
    edge = pl.BlockSpec((2, block, HALO, cols), lambda g: (0, g, 0, 0))
    whole = pl.BlockSpec((16, cols), lambda g: (0, 0))
    square = pl.BlockSpec((2 * count, 2 * count), lambda g: (0, 0))
    out_rows = 2 * count * rows
    return pl.pallas_call(
        sweep_kernel,
        out_shape=jax.ShapeDtypeStruct((blocks, out_rows, width), jnp.float32),
        grid=(count // block,),
        in_specs=[pl.BlockSpec(memory_space=pltpu.SMEM), big, edge, edge, whole, whole, square],
        out_specs=pl.BlockSpec((blocks, out_rows, width), lambda g: (0, 0, 0)),
        scratch_shapes=[pltpu.VMEM((blocks, out_rows, width), jnp.float32)],
        compiler_params=pltpu.CompilerParams(dimension_semantics=("arbitrary",)),
        cost_estimate=pl.CostEstimate(
            flops=200 * spectrum.size, transcendentals=0, bytes_accessed=8 * spectrum.size
        ),
    )(lam, spectrum, top, bottom, diff_frame, mask_frame, table)


def combine_kernel(weights, fac_ref, a_ref, o_ref):
    block = a_ref.shape[2] // 8
    base = pl.program_id(0) * block

    def body(qi, carry):
        rows = pl.ds(pl.multiple_of(qi * 8, 8), 8)
        parts = [(a_ref[s, 0, rows, :], a_ref[s, 1, rows, :]) for s in range(a_ref.shape[0])]
        for m, row in enumerate(weights):
            acc_re = []
            acc_im = []
            for (c, s), (x_re, x_im) in zip(row, parts):
                for coef, val, acc in ((c, x_re, acc_re), (-s, x_im, acc_re), (s, x_re, acc_im), (c, x_im, acc_im)):
                    if coef == 1.0:
                        acc.append(val)
                    elif coef == -1.0:
                        acc.append(-val)
                    elif coef != 0.0:
                        acc.append(coef * val)
            scale = fac_ref[m, base + qi]
            o_ref[m, 0, rows, :] = sum(acc_re[1:], acc_re[0]) * scale
            o_ref[m, 1, rows, :] = sum(acc_im[1:], acc_im[0]) * scale
        return carry

    lax.fori_loop(0, block, body, 0)


def combine_call(weights, factor, arrived, q_block):
    blocks, _, rows, width = arrived.shape
    spec = pl.BlockSpec((blocks, 2, q_block * 8, width), lambda g: (0, 0, g, 0))
    return pl.pallas_call(
        functools.partial(combine_kernel, weights),
        out_shape=jax.ShapeDtypeStruct(arrived.shape, jnp.float32),
        grid=(rows // (q_block * 8),),
        in_specs=[pl.BlockSpec(memory_space=pltpu.SMEM), spec],
        out_specs=spec,
        compiler_params=pltpu.CompilerParams(dimension_semantics=("arbitrary",)),
        cost_estimate=pl.CostEstimate(
            flops=40 * arrived.size, transcendentals=0, bytes_accessed=8 * arrived.size
        ),
    )(factor, arrived)


def class_weights(tm_count, bit_count):
    rows = []
    for m in range(tm_count):
        row = []
        for source in range(tm_count):
            angle = 2.0 * math.pi * ((m * reverse_bits(source, bit_count)) % tm_count) / tm_count
            c, s = math.cos(angle), math.sin(angle)
            c = float(np.float32(0.0 if abs(c) < 1e-9 else c))
            s = float(np.float32(0.0 if abs(s) < 1e-9 else s))
            row.append((c, s))
        rows.append(tuple(row))
    return tuple(rows)


def frames(diffusivity, d_top, d_bot, space_place, space_count):
    rows, cols = diffusivity.shape
    gap = jnp.zeros((16 - rows - 2 * HALO, cols), jnp.float32)
    diff_frame = jnp.concatenate([diffusivity, d_bot, gap, d_top], axis=0)
    row = jnp.arange(16, dtype=jnp.int32)
    keep = (row < rows) | ((row == rows) & (space_place < space_count - 1)) | (
        (row == 15) & (space_place > 0)
    )
    mask_frame = jnp.broadcast_to(keep.astype(jnp.float32)[:, None], (16, cols))
    return diff_frame, mask_frame


def on_device(spectrum, diffusivity):
    local_count = spectrum.shape[1]
    row_count = spectrum.shape[2]
    col_count = spectrum.shape[3]
    tm_count = lax.axis_size("tm")
    space_count = lax.axis_size("space")
    bit_count = tm_count.bit_length() - 1
    total_steps = local_count * tm_count
    tm_place = lax.axis_index("tm")
    space_place = lax.axis_index("space")
    residue = reverse_bits(tm_place, bit_count)
    index_f = jnp.arange(local_count, dtype=jnp.int32)
    freq_ids = index_f * tm_count + residue
    lam = jnp.stack(shift_parts(freq_ids, total_steps))

    diff_slot = jnp.broadcast_to(diffusivity[None, None], (2, 1, row_count, col_count))
    top, bottom = halo_pair(jnp.concatenate([spectrum, diff_slot], axis=1), "space", 2, HALO)
    diff_frame, mask_frame = frames(diffusivity, top[0, local_count], bottom[0, local_count], space_place, space_count)
    grid_angle = (index_f[:, None] * freq_ids[None, :] % total_steps).astype(jnp.float32) * (
        2.0 * math.pi / total_steps
    )
    cosine = jnp.cos(grid_angle)
    sine = jnp.sin(grid_angle)
    table = jnp.concatenate(
        [jnp.concatenate([cosine, -sine], 1), jnp.concatenate([sine, cosine], 1)], 0
    )
    outgoing = sweep_call(lam, spectrum, top, bottom, diff_frame, mask_frame, table, tm_count)
    col_block = col_count // tm_count
    outgoing = outgoing.reshape(tm_count, 2, local_count * row_count, col_block)
    arrived = lax.all_to_all(outgoing, "tm", 0, 0, tiled=True)

    step_ids = (
        jnp.arange(tm_count, dtype=jnp.int32)[:, None] * local_count
        + jnp.arange(local_count, dtype=jnp.int32)[None, :]
    ).astype(jnp.float32)
    factor = jnp.exp(step_ids * (-math.log(alpha_wrap) / total_steps)) / math.sqrt(total_steps)
    combined = combine_call(class_weights(tm_count, bit_count), factor, arrived, Q_BLOCK)
    returned = lax.all_to_all(combined, "tm", 0, 0, tiled=True)
    returned = returned.reshape(tm_count, 2, local_count, row_count, col_block)
    return jnp.moveaxis(returned, 0, 3).reshape(2, local_count, row_count, col_count)


def solution(mesh):
    in_specs = (P(None, "tm", "space", None), P("space", None))
    out_specs = P(None, "tm", "space", None)
    return jax.shard_map(
        on_device, mesh=mesh, in_specs=in_specs, out_specs=out_specs, check_vma=False
    )
```

```python
import functools
import math

import jax
import jax.numpy as jnp
import numpy as np
from jax import lax
from jax.experimental import pallas as pl
from jax.experimental.pallas import tpu as pltpu
from jax.sharding import PartitionSpec as P

alpha_wrap = 0.25
step_rate = 0.5
flow_speed = 2.0
sweep_weights = [
    1.0 / (1.0 + 0.7 * math.cos(math.pi * (2 * order + 1) / 6.0)) for order in range(3)
]
Q_BLOCK = 16
F_BLOCK = 4
HALO = 2


def reverse_bits(number, bit_count):
    result = number * 0
    for bit_place in range(bit_count):
        result = result + (number >> bit_place & 1) * (1 << bit_count - 1 - bit_place)
    return result


def shift_parts(freq_ids, total_steps):
    phase_angle = freq_ids.astype(jnp.float32) * (2.0 * math.pi / total_steps)
    root_scale = alpha_wrap ** (1.0 / total_steps)
    return (
        step_rate * (1.0 - root_scale * jnp.cos(phase_angle)),
        step_rate * root_scale * jnp.sin(phase_angle),
    )


def halo_pair(block, axis, dim, width):
    count = lax.axis_size(axis)
    forward = [(i, i + 1) for i in range(count - 1)]
    backward = [(i + 1, i) for i in range(count - 1)]
    size = block.shape[dim]
    top = lax.ppermute(lax.slice_in_dim(block, size - width, size, axis=dim), axis, forward)
    bottom = lax.ppermute(lax.slice_in_dim(block, 0, width, axis=dim), axis, backward)
    return top, bottom


def sweep_kernel(half, lam_ref, rhs_ref, edge_ref, diff_ref, mask_ref, table_ref, o_ref, field):
    block = rhs_ref.shape[1]
    count = lam_ref.shape[1]
    cols = rhs_ref.shape[3]
    base = pl.program_id(0) * block
    diff = diff_ref[...]
    diag_base = 4.0 * diff + flow_speed
    keep = mask_ref[...]
    row = lax.broadcasted_iota(jnp.int32, (8, cols), 0)
    col = lax.broadcasted_iota(jnp.int32, (8, cols), 1)
    first = 6 if half == 0 else 4

    def frame(x, f):
        local = rhs_ref[x, f]
        if half == 1:
            local = pltpu.roll(local, 4, 0)
        ev = edge_ref[x, f]
        out = jnp.where(row == first, jnp.broadcast_to(ev[0:1], (8, cols)), local)
        return jnp.where(row == first + 1, jnp.broadcast_to(ev[1:2], (8, cols)), out)

    def around(v):
        north = pltpu.roll(v, 1, 0)
        south = pltpu.roll(v, 7, 0)
        west = jnp.where(col == 0, 0.0, pltpu.roll(v, 1, 1))
        east = jnp.where(col == cols - 1, 0.0, pltpu.roll(v, cols - 1, 1))
        return north, north + south + west + east

    def body(f, carry):
        lam_r = lam_ref[0, base + f]
        lam_i = lam_ref[1, base + f]
        dr = diag_base + lam_r
        inv_mag = 1.0 / (dr * dr + lam_i * lam_i)
        r_re = frame(0, f)
        r_im = frame(1, f)
        c_re = sweep_weights[0] * ((r_re * dr + r_im * lam_i) * inv_mag)
        c_im = sweep_weights[0] * ((r_im * dr - r_re * lam_i) * inv_mag)
        for order in (1, 2):
            n_re, b_re = around(c_re)
            n_im, b_im = around(c_im)
            a_re = dr * c_re - lam_i * c_im - diff * b_re - flow_speed * n_re
            a_im = dr * c_im + lam_i * c_re - diff * b_im - flow_speed * n_im
            s_re = r_re - a_re
            s_im = r_im - a_im
            c_re = c_re + sweep_weights[order] * ((s_re * dr + s_im * lam_i) * inv_mag)
            c_im = c_im + sweep_weights[order] * ((s_im * dr - s_re * lam_i) * inv_mag)
            if order == 1:
                c_re = c_re * keep
                c_im = c_im * keep
        width = field.shape[2]
        for blk in range(field.shape[0]):
            lanes = slice(blk * width, (blk + 1) * width)
            field[blk, pl.ds(pl.multiple_of((base + f) * 4, 4), 4), :] = c_re[0:4, lanes]
            field[blk, pl.ds(pl.multiple_of((count + base + f) * 4, 4), 4), :] = c_im[0:4, lanes]
        return carry

    lax.fori_loop(0, block, body, 0)

    @pl.when(pl.program_id(0) == pl.num_programs(0) - 1)
    def _():
        table = table_ref[...]
        for blk in range(o_ref.shape[0]):
            for r in range(4):
                plane = field[blk, pl.ds(r, 2 * count, stride=4), :]
                o_ref[blk, pl.ds(r, 2 * count, stride=4), :] = jnp.dot(
                    table, plane, precision=lax.Precision.HIGHEST, preferred_element_type=jnp.float32
                )


def sweep_call(half, lam, spectrum, edge, diff_frame, mask_frame, table, blocks):
    _, count, rows, cols = spectrum.shape
    block = F_BLOCK
    width = cols // blocks
    big = pl.BlockSpec((2, block, rows, cols), lambda g: (0, g, 0, 0))
    edges = pl.BlockSpec((2, block, HALO, cols), lambda g: (0, g, 0, 0))
    whole = pl.BlockSpec((8, cols), lambda g: (0, 0))
    square = pl.BlockSpec((2 * count, 2 * count), lambda g: (0, 0))
    out_rows = 2 * count * 4
    return pl.pallas_call(
        functools.partial(sweep_kernel, half),
        out_shape=jax.ShapeDtypeStruct((blocks, out_rows, width), jnp.float32),
        grid=(count // block,),
        in_specs=[pl.BlockSpec(memory_space=pltpu.SMEM), big, edges, whole, whole, square],
        out_specs=pl.BlockSpec((blocks, out_rows, width), lambda g: (0, 0, 0)),
        scratch_shapes=[pltpu.VMEM((blocks, out_rows, width), jnp.float32)],
        compiler_params=pltpu.CompilerParams(dimension_semantics=("arbitrary",)),
        cost_estimate=pl.CostEstimate(
            flops=100 * spectrum.size, transcendentals=0, bytes_accessed=6 * spectrum.size
        ),
    )(lam, spectrum, edge, diff_frame, mask_frame, table)


def combine_kernel(weights, fac_ref, a_ref, o_ref):
    block = a_ref.shape[2] // 8
    base = pl.program_id(0) * block
    sub = lax.broadcasted_iota(jnp.int32, (8, a_ref.shape[3]), 0)

    def body(qi, carry):
        rows = pl.ds(pl.multiple_of(qi * 8, 8), 8)
        parts = [(a_ref[s, 0, rows, :], a_ref[s, 1, rows, :]) for s in range(a_ref.shape[0])]
        for m, row in enumerate(weights):
            acc_re = []
            acc_im = []
            for (c, s), (x_re, x_im) in zip(row, parts):
                for coef, val, acc in ((c, x_re, acc_re), (-s, x_im, acc_re), (s, x_re, acc_im), (c, x_im, acc_im)):
                    if coef == 1.0:
                        acc.append(val)
                    elif coef == -1.0:
                        acc.append(-val)
                    elif coef != 0.0:
                        acc.append(coef * val)
            q0 = (base + qi) * 2
            scale = jnp.where(sub < 4, fac_ref[m, q0], fac_ref[m, q0 + 1])
            o_ref[m, 0, rows, :] = sum(acc_re[1:], acc_re[0]) * scale
            o_ref[m, 1, rows, :] = sum(acc_im[1:], acc_im[0]) * scale
        return carry

    lax.fori_loop(0, block, body, 0)


def combine_call(weights, factor, arrived, q_block):
    blocks, _, rows, width = arrived.shape
    spec = pl.BlockSpec((blocks, 2, q_block * 8, width), lambda g: (0, 0, g, 0))
    return pl.pallas_call(
        functools.partial(combine_kernel, weights),
        out_shape=jax.ShapeDtypeStruct(arrived.shape, jnp.float32),
        grid=(rows // (q_block * 8),),
        in_specs=[pl.BlockSpec(memory_space=pltpu.SMEM), spec],
        out_specs=spec,
        compiler_params=pltpu.CompilerParams(dimension_semantics=("arbitrary",)),
        cost_estimate=pl.CostEstimate(
            flops=40 * arrived.size, transcendentals=0, bytes_accessed=8 * arrived.size
        ),
    )(factor, arrived)


def class_weights(tm_count, bit_count):
    rows = []
    for m in range(tm_count):
        row = []
        for source in range(tm_count):
            angle = 2.0 * math.pi * ((m * reverse_bits(source, bit_count)) % tm_count) / tm_count
            c, s = math.cos(angle), math.sin(angle)
            c = float(np.float32(0.0 if abs(c) < 1e-9 else c))
            s = float(np.float32(0.0 if abs(s) < 1e-9 else s))
            row.append((c, s))
        rows.append(tuple(row))
    return tuple(rows)


def frames(diffusivity, space_place, space_count):
    rows, cols = diffusivity.shape
    d_top, d_bot = halo_pair(diffusivity, "space", 0, HALO)
    diff_frames = (
        jnp.concatenate([diffusivity[0:6], d_top], axis=0),
        jnp.concatenate([diffusivity[4:8], d_bot, diffusivity[2:4]], axis=0),
    )
    row = jnp.arange(8, dtype=jnp.int32)
    keeps = (
        (row != 7) | (space_place > 0),
        (row != 4) | (space_place < space_count - 1),
    )
    mask_frames = tuple(jnp.broadcast_to(k.astype(jnp.float32)[:, None], (8, cols)) for k in keeps)
    return diff_frames, mask_frames


def on_device(spectrum, diffusivity):
    local_count = spectrum.shape[1]
    row_count = spectrum.shape[2]
    col_count = spectrum.shape[3]
    tm_count = lax.axis_size("tm")
    space_count = lax.axis_size("space")
    bit_count = tm_count.bit_length() - 1
    total_steps = local_count * tm_count
    tm_place = lax.axis_index("tm")
    space_place = lax.axis_index("space")
    residue = reverse_bits(tm_place, bit_count)
    index_f = jnp.arange(local_count, dtype=jnp.int32)
    freq_ids = index_f * tm_count + residue
    lam = jnp.stack(shift_parts(freq_ids, total_steps))

    top, bottom = halo_pair(spectrum, "space", 2, HALO)
    diff_frames, mask_frames = frames(diffusivity, space_place, space_count)

    grid_angle = (index_f[:, None] * freq_ids[None, :] % total_steps).astype(jnp.float32) * (
        2.0 * math.pi / total_steps
    )
    cosine = jnp.cos(grid_angle)
    sine = jnp.sin(grid_angle)
    table = jnp.concatenate(
        [jnp.concatenate([cosine, -sine], 1), jnp.concatenate([sine, cosine], 1)], 0
    )
    col_block = col_count // tm_count
    step_ids = (
        jnp.arange(tm_count, dtype=jnp.int32)[:, None] * local_count
        + jnp.arange(local_count, dtype=jnp.int32)[None, :]
    ).astype(jnp.float32)
    factor = jnp.exp(step_ids * (-math.log(alpha_wrap) / total_steps)) / math.sqrt(total_steps)
    weights = class_weights(tm_count, bit_count)

    arrived = []
    for half, edge in ((0, top), (1, bottom)):
        outgoing = sweep_call(half, lam, spectrum, edge, diff_frames[half], mask_frames[half], table, tm_count)
        outgoing = outgoing.reshape(tm_count, 2, local_count * 4, col_block)
        arrived.append(lax.all_to_all(outgoing, "tm", 0, 0, tiled=True))
    returned = []
    for piece in arrived:
        combined = combine_call(weights, factor, piece, Q_BLOCK)
        returned.append(lax.all_to_all(combined, "tm", 0, 0, tiled=True).reshape(tm_count, 2, local_count, 4, col_block))
    joined = jnp.concatenate(returned, axis=3)
    return jnp.moveaxis(joined, 0, 3).reshape(2, local_count, row_count, col_count)


def solution(mesh):
    in_specs = (P(None, "tm", "space", None), P("space", None))
    out_specs = P(None, "tm", "space", None)
    return jax.shard_map(
        on_device, mesh=mesh, in_specs=in_specs, out_specs=out_specs, check_vma=False
    )
```

```python
import functools
import math

import jax
import jax.numpy as jnp
import numpy as np
from jax import lax
from jax.experimental import pallas as pl
from jax.experimental.pallas import tpu as pltpu
from jax.sharding import PartitionSpec as P

alpha_wrap = 0.25
step_rate = 0.5
flow_speed = 2.0
sweep_weights = [
    1.0 / (1.0 + 0.7 * math.cos(math.pi * (2 * order + 1) / 6.0)) for order in range(3)
]
Q_BLOCK = 16
F_BLOCK = 16
SWEEP_UNROLL = 2
HALO = 2


def reverse_bits(number, bit_count):
    result = number * 0
    for bit_place in range(bit_count):
        result = result + (number >> bit_place & 1) * (1 << bit_count - 1 - bit_place)
    return result


def shift_parts(freq_ids, total_steps):
    phase_angle = freq_ids.astype(jnp.float32) * (2.0 * math.pi / total_steps)
    root_scale = alpha_wrap ** (1.0 / total_steps)
    return (
        step_rate * (1.0 - root_scale * jnp.cos(phase_angle)),
        step_rate * root_scale * jnp.sin(phase_angle),
    )


def halo_pair(block, axis, dim, width):
    count = lax.axis_size(axis)
    forward = [(i, i + 1) for i in range(count - 1)]
    backward = [(i + 1, i) for i in range(count - 1)]
    size = block.shape[dim]
    top = lax.ppermute(lax.slice_in_dim(block, size - width, size, axis=dim), axis, forward)
    bottom = lax.ppermute(lax.slice_in_dim(block, 0, width, axis=dim), axis, backward)
    return top, bottom


def sweep_kernel(lam_ref, rhs_ref, top_ref, bot_ref, diff_ref, mask_ref, table_ref, o_ref, field):
    block = rhs_ref.shape[1]
    count = lam_ref.shape[1]
    cols = rhs_ref.shape[3]
    base = pl.program_id(0) * block
    diff = diff_ref[...]
    diag_base = 4.0 * diff + flow_speed
    keep = mask_ref[...]
    row8 = lax.broadcasted_iota(jnp.int32, (8, cols), 0)
    col = lax.broadcasted_iota(jnp.int32, (16, cols), 1)

    def frame(x, f):
        local = rhs_ref[x, f]
        bv = bot_ref[x, f]
        tv = top_ref[x, f]
        hi = jnp.where(row8 == 0, jnp.broadcast_to(bv[0:1], (8, cols)), 0.0)
        hi = jnp.where(row8 == 1, jnp.broadcast_to(bv[1:2], (8, cols)), hi)
        hi = jnp.where(row8 == 6, jnp.broadcast_to(tv[0:1], (8, cols)), hi)
        hi = jnp.where(row8 == 7, jnp.broadcast_to(tv[1:2], (8, cols)), hi)
        return jnp.concatenate([local, hi], axis=0)

    def around(v):
        north = pltpu.roll(v, 1, 0)
        south = pltpu.roll(v, 15, 0)
        west = jnp.where(col == 0, 0.0, pltpu.roll(v, 1, 1))
        east = jnp.where(col == cols - 1, 0.0, pltpu.roll(v, cols - 1, 1))
        return north, north + south + west + east

    def body(f, carry):
        lam_r = lam_ref[0, base + f]
        lam_i = lam_ref[1, base + f]
        dr = diag_base + lam_r
        inv_mag = 1.0 / (dr * dr + lam_i * lam_i)
        r_re = frame(0, f)
        r_im = frame(1, f)
        c_re = sweep_weights[0] * ((r_re * dr + r_im * lam_i) * inv_mag)
        c_im = sweep_weights[0] * ((r_im * dr - r_re * lam_i) * inv_mag)
        for order in (1, 2):
            n_re, b_re = around(c_re)
            n_im, b_im = around(c_im)
            if order == 2:
                n_re, b_re, n_im, b_im = n_re[0:8], b_re[0:8], n_im[0:8], b_im[0:8]
                c_re, c_im, r_re, r_im = c_re[0:8], c_im[0:8], r_re[0:8], r_im[0:8]
                dr, inv_mag, d = dr[0:8], inv_mag[0:8], diff[0:8]
            else:
                d = diff
            a_re = dr * c_re - lam_i * c_im - d * b_re - flow_speed * n_re
            a_im = dr * c_im + lam_i * c_re - d * b_im - flow_speed * n_im
            s_re = r_re - a_re
            s_im = r_im - a_im
            c_re = c_re + sweep_weights[order] * ((s_re * dr + s_im * lam_i) * inv_mag)
            c_im = c_im + sweep_weights[order] * ((s_im * dr - s_re * lam_i) * inv_mag)
            if order == 1:
                c_re = c_re * keep
                c_im = c_im * keep
        width = field.shape[2]
        for blk in range(field.shape[0]):
            lanes = slice(blk * width, (blk + 1) * width)
            field[blk, pl.ds(pl.multiple_of((base + f) * 8, 8), 8), :] = c_re[0:8, lanes]
            field[blk, pl.ds(pl.multiple_of((count + base + f) * 8, 8), 8), :] = c_im[0:8, lanes]
        return carry

    lax.fori_loop(0, block, body, 0, unroll=SWEEP_UNROLL)

    @pl.when(pl.program_id(0) == pl.num_programs(0) - 1)
    def _():
        table = table_ref[...]
        for blk in range(o_ref.shape[0]):
            for r in range(8):
                plane = field[blk, pl.ds(r, 2 * count, stride=8), :]
                o_ref[blk, pl.ds(r, 2 * count, stride=8), :] = jnp.dot(
                    table, plane, precision=lax.Precision.HIGHEST, preferred_element_type=jnp.float32
                )


def sweep_call(lam, spectrum, top, bottom, diff_frame, mask_frame, table, blocks):
    _, count, rows, cols = spectrum.shape
    block = F_BLOCK
    width = cols // blocks
    big = pl.BlockSpec((2, block, rows, cols), lambda g: (0, g, 0, 0))
    edge = pl.BlockSpec((2, block, HALO, cols), lambda g: (0, g, 0, 0))
    whole = pl.BlockSpec((16, cols), lambda g: (0, 0))
    square = pl.BlockSpec((2 * count, 2 * count), lambda g: (0, 0))
    out_rows = 2 * count * rows
    return pl.pallas_call(
        sweep_kernel,
        out_shape=jax.ShapeDtypeStruct((blocks, out_rows, width), jnp.float32),
        grid=(count // block,),
        in_specs=[pl.BlockSpec(memory_space=pltpu.SMEM), big, edge, edge, whole, whole, square],
        out_specs=pl.BlockSpec((blocks, out_rows, width), lambda g: (0, 0, 0)),
        scratch_shapes=[pltpu.VMEM((blocks, out_rows, width), jnp.float32)],
        compiler_params=pltpu.CompilerParams(dimension_semantics=("arbitrary",)),
        cost_estimate=pl.CostEstimate(
            flops=200 * spectrum.size, transcendentals=0, bytes_accessed=8 * spectrum.size
        ),
    )(lam, spectrum, top, bottom, diff_frame, mask_frame, table)


def combine_kernel(weights, fac_ref, a_ref, o_ref):
    block = a_ref.shape[2] // 8
    base = pl.program_id(0) * block

    def body(qi, carry):
        rows = pl.ds(pl.multiple_of(qi * 8, 8), 8)
        parts = [(a_ref[s, 0, rows, :], a_ref[s, 1, rows, :]) for s in range(a_ref.shape[0])]
        for m, row in enumerate(weights):
            acc_re = []
            acc_im = []
            for (c, s), (x_re, x_im) in zip(row, parts):
                for coef, val, acc in ((c, x_re, acc_re), (-s, x_im, acc_re), (s, x_re, acc_im), (c, x_im, acc_im)):
                    if coef == 1.0:
                        acc.append(val)
                    elif coef == -1.0:
                        acc.append(-val)
                    elif coef != 0.0:
                        acc.append(coef * val)
            scale = fac_ref[m, base + qi]
            o_ref[m, 0, rows, :] = sum(acc_re[1:], acc_re[0]) * scale
            o_ref[m, 1, rows, :] = sum(acc_im[1:], acc_im[0]) * scale
        return carry

    lax.fori_loop(0, block, body, 0, unroll=SWEEP_UNROLL)


def combine_call(weights, factor, arrived, q_block):
    blocks, _, rows, width = arrived.shape
    spec = pl.BlockSpec((blocks, 2, q_block * 8, width), lambda g: (0, 0, g, 0))
    return pl.pallas_call(
        functools.partial(combine_kernel, weights),
        out_shape=jax.ShapeDtypeStruct(arrived.shape, jnp.float32),
        grid=(rows // (q_block * 8),),
        in_specs=[pl.BlockSpec(memory_space=pltpu.SMEM), spec],
        out_specs=spec,
        compiler_params=pltpu.CompilerParams(dimension_semantics=("arbitrary",)),
        cost_estimate=pl.CostEstimate(
            flops=40 * arrived.size, transcendentals=0, bytes_accessed=8 * arrived.size
        ),
    )(factor, arrived)


def class_weights(tm_count, bit_count):
    rows = []
    for m in range(tm_count):
        row = []
        for source in range(tm_count):
            angle = 2.0 * math.pi * ((m * reverse_bits(source, bit_count)) % tm_count) / tm_count
            c, s = math.cos(angle), math.sin(angle)
            c = float(np.float32(0.0 if abs(c) < 1e-9 else c))
            s = float(np.float32(0.0 if abs(s) < 1e-9 else s))
            row.append((c, s))
        rows.append(tuple(row))
    return tuple(rows)


def frames(diffusivity, d_top, d_bot, space_place, space_count):
    rows, cols = diffusivity.shape
    gap = jnp.zeros((16 - rows - 2 * HALO, cols), jnp.float32)
    diff_frame = jnp.concatenate([diffusivity, d_bot, gap, d_top], axis=0)
    row = jnp.arange(16, dtype=jnp.int32)
    keep = (row < rows) | ((row == rows) & (space_place < space_count - 1)) | (
        (row == 15) & (space_place > 0)
    )
    mask_frame = jnp.broadcast_to(keep.astype(jnp.float32)[:, None], (16, cols))
    return diff_frame, mask_frame


def on_device(spectrum, diffusivity):
    local_count = spectrum.shape[1]
    row_count = spectrum.shape[2]
    col_count = spectrum.shape[3]
    tm_count = lax.axis_size("tm")
    space_count = lax.axis_size("space")
    bit_count = tm_count.bit_length() - 1
    total_steps = local_count * tm_count
    tm_place = lax.axis_index("tm")
    space_place = lax.axis_index("space")
    residue = reverse_bits(tm_place, bit_count)
    index_f = jnp.arange(local_count, dtype=jnp.int32)
    freq_ids = index_f * tm_count + residue
    lam = jnp.stack(shift_parts(freq_ids, total_steps))

    diff_slot = jnp.broadcast_to(diffusivity[None, None], (2, 1, row_count, col_count))
    top, bottom = halo_pair(jnp.concatenate([spectrum, diff_slot], axis=1), "space", 2, HALO)
    diff_frame, mask_frame = frames(diffusivity, top[0, local_count], bottom[0, local_count], space_place, space_count)
    grid_angle = (index_f[:, None] * freq_ids[None, :] % total_steps).astype(jnp.float32) * (
        2.0 * math.pi / total_steps
    )
    cosine = jnp.cos(grid_angle)
    sine = jnp.sin(grid_angle)
    table = jnp.concatenate(
        [jnp.concatenate([cosine, -sine], 1), jnp.concatenate([sine, cosine], 1)], 0
    )
    outgoing = sweep_call(lam, spectrum, top, bottom, diff_frame, mask_frame, table, tm_count)
    col_block = col_count // tm_count
    outgoing = outgoing.reshape(tm_count, 2, local_count * row_count, col_block)
    arrived = lax.all_to_all(outgoing, "tm", 0, 0, tiled=True)

    step_ids = (
        jnp.arange(tm_count, dtype=jnp.int32)[:, None] * local_count
        + jnp.arange(local_count, dtype=jnp.int32)[None, :]
    ).astype(jnp.float32)
    factor = jnp.exp(step_ids * (-math.log(alpha_wrap) / total_steps)) / math.sqrt(total_steps)
    combined = combine_call(class_weights(tm_count, bit_count), factor, arrived, Q_BLOCK)
    returned = lax.all_to_all(combined, "tm", 0, 0, tiled=True)
    returned = returned.reshape(tm_count, 2, local_count, row_count, col_block)
    return jnp.moveaxis(returned, 0, 3).reshape(2, local_count, row_count, col_count)


def solution(mesh):
    in_specs = (P(None, "tm", "space", None), P("space", None))
    out_specs = P(None, "tm", "space", None)
    return jax.shard_map(
        on_device, mesh=mesh, in_specs=in_specs, out_specs=out_specs, check_vma=False
    )
```

```python
import functools
import math

import jax
import jax.numpy as jnp
import numpy as np
from jax import lax
from jax.experimental import pallas as pl
from jax.experimental.pallas import tpu as pltpu
from jax.sharding import PartitionSpec as P

alpha_wrap = 0.25
step_rate = 0.5
flow_speed = 2.0
sweep_weights = [
    1.0 / (1.0 + 0.7 * math.cos(math.pi * (2 * order + 1) / 6.0)) for order in range(3)
]
Q_BLOCK = 16
F_BLOCK = 16
SWEEP_UNROLL = 2
HALO = 2


def reverse_bits(number, bit_count):
    result = number * 0
    for bit_place in range(bit_count):
        result = result + (number >> bit_place & 1) * (1 << bit_count - 1 - bit_place)
    return result


def shift_parts(freq_ids, total_steps):
    phase_angle = freq_ids.astype(jnp.float32) * (2.0 * math.pi / total_steps)
    root_scale = alpha_wrap ** (1.0 / total_steps)
    return (
        step_rate * (1.0 - root_scale * jnp.cos(phase_angle)),
        step_rate * root_scale * jnp.sin(phase_angle),
    )


def halo_pair(block, axis, dim, width):
    count = lax.axis_size(axis)
    forward = [(i, i + 1) for i in range(count - 1)]
    backward = [(i + 1, i) for i in range(count - 1)]
    size = block.shape[dim]
    top = lax.ppermute(lax.slice_in_dim(block, size - width, size, axis=dim), axis, forward)
    bottom = lax.ppermute(lax.slice_in_dim(block, 0, width, axis=dim), axis, backward)
    return top, bottom


def sweep_kernel(lam_ref, rhs_ref, top_ref, bot_ref, diff_ref, mask_ref, table_ref, o_ref, field):
    block = rhs_ref.shape[1]
    count = lam_ref.shape[1]
    cols = rhs_ref.shape[3]
    base = pl.program_id(0) * block
    diff = diff_ref[...]
    diag_base = 4.0 * diff + flow_speed
    keep = mask_ref[...]
    row8 = lax.broadcasted_iota(jnp.int32, (8, cols), 0)
    col = lax.broadcasted_iota(jnp.int32, (16, cols), 1)

    def frame(x, f):
        local = rhs_ref[x, f]
        bv = bot_ref[x, f]
        tv = top_ref[x, f]
        hi = jnp.where(row8 == 0, jnp.broadcast_to(bv[0:1], (8, cols)), 0.0)
        hi = jnp.where(row8 == 1, jnp.broadcast_to(bv[1:2], (8, cols)), hi)
        hi = jnp.where(row8 == 6, jnp.broadcast_to(tv[0:1], (8, cols)), hi)
        hi = jnp.where(row8 == 7, jnp.broadcast_to(tv[1:2], (8, cols)), hi)
        return jnp.concatenate([local, hi], axis=0)

    def around(v):
        north = pltpu.roll(v, 1, 0)
        south = pltpu.roll(v, 15, 0)
        west = jnp.where(col == 0, 0.0, pltpu.roll(v, 1, 1))
        east = jnp.where(col == cols - 1, 0.0, pltpu.roll(v, cols - 1, 1))
        return north, north + south + west + east

    def body(f, carry):
        lam_r = lam_ref[0, base + f]
        lam_i = lam_ref[1, base + f]
        dr = diag_base + lam_r
        inv_mag = 1.0 / (dr * dr + lam_i * lam_i)
        r_re = frame(0, f)
        r_im = frame(1, f)
        c_re = sweep_weights[0] * ((r_re * dr + r_im * lam_i) * inv_mag)
        c_im = sweep_weights[0] * ((r_im * dr - r_re * lam_i) * inv_mag)
        for order in (1, 2):
            n_re, b_re = around(c_re)
            n_im, b_im = around(c_im)
            if order == 2:
                n_re, b_re, n_im, b_im = n_re[0:8], b_re[0:8], n_im[0:8], b_im[0:8]
                c_re, c_im, r_re, r_im = c_re[0:8], c_im[0:8], r_re[0:8], r_im[0:8]
                dr, inv_mag, d = dr[0:8], inv_mag[0:8], diff[0:8]
            else:
                d = diff
            a_re = dr * c_re - lam_i * c_im - d * b_re - flow_speed * n_re
            a_im = dr * c_im + lam_i * c_re - d * b_im - flow_speed * n_im
            s_re = r_re - a_re
            s_im = r_im - a_im
            c_re = c_re + sweep_weights[order] * ((s_re * dr + s_im * lam_i) * inv_mag)
            c_im = c_im + sweep_weights[order] * ((s_im * dr - s_re * lam_i) * inv_mag)
            if order == 1:
                c_re = c_re * keep
                c_im = c_im * keep
        width = field.shape[2]
        for blk in range(field.shape[0]):
            lanes = slice(blk * width, (blk + 1) * width)
            field[blk, pl.ds(pl.multiple_of((base + f) * 8, 8), 8), :] = c_re[0:8, lanes]
            field[blk, pl.ds(pl.multiple_of((count + base + f) * 8, 8), 8), :] = c_im[0:8, lanes]
        return carry

    lax.fori_loop(0, block, body, 0, unroll=SWEEP_UNROLL)

    @pl.when(pl.program_id(0) == pl.num_programs(0) - 1)
    def _():
        table = table_ref[...]
        for blk in range(o_ref.shape[0]):
            for r in range(8):
                plane = field[blk, pl.ds(r, 2 * count, stride=8), :]
                o_ref[blk, pl.ds(r, 2 * count, stride=8), :] = jnp.dot(
                    table, plane, precision=lax.Precision.HIGHEST, preferred_element_type=jnp.float32
                )


def sweep_call(lam, spectrum, top, bottom, diff_frame, mask_frame, table, blocks):
    _, count, rows, cols = spectrum.shape
    block = F_BLOCK
    width = cols // blocks
    big = pl.BlockSpec((2, block, rows, cols), lambda g: (0, g, 0, 0))
    edge = pl.BlockSpec((2, block, HALO, cols), lambda g: (0, g, 0, 0))
    whole = pl.BlockSpec((16, cols), lambda g: (0, 0))
    square = pl.BlockSpec((2 * count, 2 * count), lambda g: (0, 0))
    out_rows = 2 * count * rows
    return pl.pallas_call(
        sweep_kernel,
        out_shape=jax.ShapeDtypeStruct((blocks, out_rows, width), jnp.float32),
        grid=(count // block,),
        in_specs=[pl.BlockSpec(memory_space=pltpu.SMEM), big, edge, edge, whole, whole, square],
        out_specs=pl.BlockSpec((blocks, out_rows, width), lambda g: (0, 0, 0)),
        scratch_shapes=[pltpu.VMEM((blocks, out_rows, width), jnp.float32)],
        compiler_params=pltpu.CompilerParams(dimension_semantics=("arbitrary",)),
        cost_estimate=pl.CostEstimate(
            flops=200 * spectrum.size, transcendentals=0, bytes_accessed=8 * spectrum.size
        ),
    )(lam, spectrum, top, bottom, diff_frame, mask_frame, table)


def combine_kernel(weights, fac_ref, a_ref, o_ref):
    block = a_ref.shape[2] // 8
    base = pl.program_id(0) * block
    half = float(np.float32(1.0 / math.sqrt(2.0)))

    def turn(p, eighths):
        re, im = p
        if eighths == 0:
            return p
        if eighths == 2:
            return -im, re
        if eighths == 1:
            return half * (re - im), half * (re + im)
        return -half * (re + im), half * (re - im)

    def body(qi, carry):
        rows = pl.ds(pl.multiple_of(qi * 8, 8), 8)
        x = [(a_ref[s, 0, rows, :], a_ref[s, 1, rows, :]) for s in range(a_ref.shape[0])]
        span = 1
        while span < len(x):
            y = list(x)
            for start in range(0, len(x), 2 * span):
                for j in range(span):
                    u = x[start + j]
                    v = turn(x[start + j + span], j * len(x) // (2 * span))
                    y[start + j] = (u[0] + v[0], u[1] + v[1])
                    y[start + j + span] = (u[0] - v[0], u[1] - v[1])
            x = y
            span *= 2
        for m, (re, im) in enumerate(x):
            scale = fac_ref[m, base + qi]
            o_ref[m, 0, rows, :] = re * scale
            o_ref[m, 1, rows, :] = im * scale
        return carry

    lax.fori_loop(0, block, body, 0, unroll=SWEEP_UNROLL)


def combine_call(weights, factor, arrived, q_block):
    blocks, _, rows, width = arrived.shape
    spec = pl.BlockSpec((blocks, 2, q_block * 8, width), lambda g: (0, 0, g, 0))
    return pl.pallas_call(
        functools.partial(combine_kernel, weights),
        out_shape=jax.ShapeDtypeStruct(arrived.shape, jnp.float32),
        grid=(rows // (q_block * 8),),
        in_specs=[pl.BlockSpec(memory_space=pltpu.SMEM), spec],
        out_specs=spec,
        compiler_params=pltpu.CompilerParams(dimension_semantics=("arbitrary",)),
        cost_estimate=pl.CostEstimate(
            flops=40 * arrived.size, transcendentals=0, bytes_accessed=8 * arrived.size
        ),
    )(factor, arrived)


def class_weights(tm_count, bit_count):
    rows = []
    for m in range(tm_count):
        row = []
        for source in range(tm_count):
            angle = 2.0 * math.pi * ((m * reverse_bits(source, bit_count)) % tm_count) / tm_count
            c, s = math.cos(angle), math.sin(angle)
            c = float(np.float32(0.0 if abs(c) < 1e-9 else c))
            s = float(np.float32(0.0 if abs(s) < 1e-9 else s))
            row.append((c, s))
        rows.append(tuple(row))
    return tuple(rows)


def frames(diffusivity, d_top, d_bot, space_place, space_count):
    rows, cols = diffusivity.shape
    gap = jnp.zeros((16 - rows - 2 * HALO, cols), jnp.float32)
    diff_frame = jnp.concatenate([diffusivity, d_bot, gap, d_top], axis=0)
    row = jnp.arange(16, dtype=jnp.int32)
    keep = (row < rows) | ((row == rows) & (space_place < space_count - 1)) | (
        (row == 15) & (space_place > 0)
    )
    mask_frame = jnp.broadcast_to(keep.astype(jnp.float32)[:, None], (16, cols))
    return diff_frame, mask_frame


def on_device(spectrum, diffusivity):
    local_count = spectrum.shape[1]
    row_count = spectrum.shape[2]
    col_count = spectrum.shape[3]
    tm_count = lax.axis_size("tm")
    space_count = lax.axis_size("space")
    bit_count = tm_count.bit_length() - 1
    total_steps = local_count * tm_count
    tm_place = lax.axis_index("tm")
    space_place = lax.axis_index("space")
    residue = reverse_bits(tm_place, bit_count)
    index_f = jnp.arange(local_count, dtype=jnp.int32)
    freq_ids = index_f * tm_count + residue
    lam = jnp.stack(shift_parts(freq_ids, total_steps))

    diff_slot = jnp.broadcast_to(diffusivity[None, None], (2, 1, row_count, col_count))
    top, bottom = halo_pair(jnp.concatenate([spectrum, diff_slot], axis=1), "space", 2, HALO)
    diff_frame, mask_frame = frames(diffusivity, top[0, local_count], bottom[0, local_count], space_place, space_count)
    grid_angle = (index_f[:, None] * freq_ids[None, :] % total_steps).astype(jnp.float32) * (
        2.0 * math.pi / total_steps
    )
    cosine = jnp.cos(grid_angle)
    sine = jnp.sin(grid_angle)
    table = jnp.concatenate(
        [jnp.concatenate([cosine, -sine], 1), jnp.concatenate([sine, cosine], 1)], 0
    )
    outgoing = sweep_call(lam, spectrum, top, bottom, diff_frame, mask_frame, table, tm_count)
    col_block = col_count // tm_count
    outgoing = outgoing.reshape(tm_count, 2, local_count * row_count, col_block)
    arrived = lax.all_to_all(outgoing, "tm", 0, 0, tiled=True)

    step_ids = (
        jnp.arange(tm_count, dtype=jnp.int32)[:, None] * local_count
        + jnp.arange(local_count, dtype=jnp.int32)[None, :]
    ).astype(jnp.float32)
    factor = jnp.exp(step_ids * (-math.log(alpha_wrap) / total_steps)) / math.sqrt(total_steps)
    combined = combine_call(class_weights(tm_count, bit_count), factor, arrived, Q_BLOCK)
    returned = lax.all_to_all(combined, "tm", 0, 0, tiled=True)
    returned = returned.reshape(tm_count, 2, local_count, row_count, col_block)
    return jnp.moveaxis(returned, 0, 3).reshape(2, local_count, row_count, col_count)


def solution(mesh):
    in_specs = (P(None, "tm", "space", None), P("space", None))
    out_specs = P(None, "tm", "space", None)
    return jax.shard_map(
        on_device, mesh=mesh, in_specs=in_specs, out_specs=out_specs, check_vma=False
    )
```

```python
import functools
import math

import jax
import jax.numpy as jnp
import numpy as np
from jax import lax
from jax.experimental import pallas as pl
from jax.experimental.pallas import tpu as pltpu
from jax.sharding import PartitionSpec as P

alpha_wrap = 0.25
step_rate = 0.5
flow_speed = 2.0
sweep_weights = [
    1.0 / (1.0 + 0.7 * math.cos(math.pi * (2 * order + 1) / 6.0)) for order in range(3)
]
Q_BLOCK = 16
F_BLOCK = 16
SWEEP_UNROLL = 2
HALO = 2


def reverse_bits(number, bit_count):
    result = number * 0
    for bit_place in range(bit_count):
        result = result + (number >> bit_place & 1) * (1 << bit_count - 1 - bit_place)
    return result


def shift_parts(freq_ids, total_steps):
    phase_angle = freq_ids.astype(jnp.float32) * (2.0 * math.pi / total_steps)
    root_scale = alpha_wrap ** (1.0 / total_steps)
    return (
        step_rate * (1.0 - root_scale * jnp.cos(phase_angle)),
        step_rate * root_scale * jnp.sin(phase_angle),
    )


def halo_pair(block, axis, dim, width):
    count = lax.axis_size(axis)
    forward = [(i, i + 1) for i in range(count - 1)]
    backward = [(i + 1, i) for i in range(count - 1)]
    size = block.shape[dim]
    top = lax.ppermute(lax.slice_in_dim(block, size - width, size, axis=dim), axis, forward)
    bottom = lax.ppermute(lax.slice_in_dim(block, 0, width, axis=dim), axis, backward)
    return top, bottom


def sweep_kernel(lam_ref, rhs_ref, top_ref, bot_ref, diff_ref, mask_ref, table_ref, o_ref, field):
    block = rhs_ref.shape[1]
    count = lam_ref.shape[1]
    cols = rhs_ref.shape[3]
    base = pl.program_id(0) * block
    diff = diff_ref[...]
    diag_base = 4.0 * diff + flow_speed
    keep = mask_ref[...]
    row8 = lax.broadcasted_iota(jnp.int32, (8, cols), 0)
    col = lax.broadcasted_iota(jnp.int32, (16, cols), 1)

    def frame(x, f):
        local = rhs_ref[x, f]
        bv = bot_ref[x, f]
        tv = top_ref[x, f]
        hi = jnp.where(row8 == 0, jnp.broadcast_to(bv[0:1], (8, cols)), 0.0)
        hi = jnp.where(row8 == 1, jnp.broadcast_to(bv[1:2], (8, cols)), hi)
        hi = jnp.where(row8 == 6, jnp.broadcast_to(tv[0:1], (8, cols)), hi)
        hi = jnp.where(row8 == 7, jnp.broadcast_to(tv[1:2], (8, cols)), hi)
        return jnp.concatenate([local, hi], axis=0)

    def around(v):
        north = pltpu.roll(v, 1, 0)
        south = pltpu.roll(v, 15, 0)
        west = jnp.where(col == 0, 0.0, pltpu.roll(v, 1, 1))
        east = jnp.where(col == cols - 1, 0.0, pltpu.roll(v, cols - 1, 1))
        return north, north + south + west + east

    def body(f, carry):
        lam_r = lam_ref[0, base + f]
        lam_i = lam_ref[1, base + f]
        dr = diag_base + lam_r
        inv_mag = 1.0 / (dr * dr + lam_i * lam_i)
        r_re = frame(0, f)
        r_im = frame(1, f)
        c_re = sweep_weights[0] * ((r_re * dr + r_im * lam_i) * inv_mag)
        c_im = sweep_weights[0] * ((r_im * dr - r_re * lam_i) * inv_mag)
        for order in (1, 2):
            n_re, b_re = around(c_re)
            n_im, b_im = around(c_im)
            if order == 2:
                n_re, b_re, n_im, b_im = n_re[0:8], b_re[0:8], n_im[0:8], b_im[0:8]
                c_re, c_im, r_re, r_im = c_re[0:8], c_im[0:8], r_re[0:8], r_im[0:8]
                dr, inv_mag, d = dr[0:8], inv_mag[0:8], diff[0:8]
            else:
                d = diff
            a_re = dr * c_re - lam_i * c_im - d * b_re - flow_speed * n_re
            a_im = dr * c_im + lam_i * c_re - d * b_im - flow_speed * n_im
            s_re = r_re - a_re
            s_im = r_im - a_im
            c_re = c_re + sweep_weights[order] * ((s_re * dr + s_im * lam_i) * inv_mag)
            c_im = c_im + sweep_weights[order] * ((s_im * dr - s_re * lam_i) * inv_mag)
            if order == 1:
                c_re = c_re * keep
                c_im = c_im * keep
        width = field.shape[2]
        for blk in range(field.shape[0]):
            lanes = slice(blk * width, (blk + 1) * width)
            field[blk, pl.ds(pl.multiple_of((base + f) * 8, 8), 8), :] = c_re[0:8, lanes]
            field[blk, pl.ds(pl.multiple_of((count + base + f) * 8, 8), 8), :] = c_im[0:8, lanes]
        return carry

    lax.fori_loop(0, block, body, 0, unroll=SWEEP_UNROLL)

    @pl.when(pl.program_id(0) == pl.num_programs(0) - 1)
    def _():
        table = table_ref[...]
        for blk in range(o_ref.shape[0]):
            for r in range(8):
                plane = field[blk, pl.ds(r, 2 * count, stride=8), :]
                o_ref[blk, pl.ds(r, 2 * count, stride=8), :] = jnp.dot(
                    table, plane, precision=lax.Precision.HIGH, preferred_element_type=jnp.float32
                )


def sweep_call(lam, spectrum, top, bottom, diff_frame, mask_frame, table, blocks):
    _, count, rows, cols = spectrum.shape
    block = F_BLOCK
    width = cols // blocks
    big = pl.BlockSpec((2, block, rows, cols), lambda g: (0, g, 0, 0))
    edge = pl.BlockSpec((2, block, HALO, cols), lambda g: (0, g, 0, 0))
    whole = pl.BlockSpec((16, cols), lambda g: (0, 0))
    square = pl.BlockSpec((2 * count, 2 * count), lambda g: (0, 0))
    out_rows = 2 * count * rows
    return pl.pallas_call(
        sweep_kernel,
        out_shape=jax.ShapeDtypeStruct((blocks, out_rows, width), jnp.float32),
        grid=(count // block,),
        in_specs=[pl.BlockSpec(memory_space=pltpu.SMEM), big, edge, edge, whole, whole, square],
        out_specs=pl.BlockSpec((blocks, out_rows, width), lambda g: (0, 0, 0)),
        scratch_shapes=[pltpu.VMEM((blocks, out_rows, width), jnp.float32)],
        compiler_params=pltpu.CompilerParams(dimension_semantics=("arbitrary",)),
        cost_estimate=pl.CostEstimate(
            flops=200 * spectrum.size, transcendentals=0, bytes_accessed=8 * spectrum.size
        ),
    )(lam, spectrum, top, bottom, diff_frame, mask_frame, table)


def combine_kernel(weights, fac_ref, a_ref, o_ref):
    block = a_ref.shape[2] // 8
    base = pl.program_id(0) * block
    half = float(np.float32(1.0 / math.sqrt(2.0)))

    def turn(p, eighths):
        re, im = p
        if eighths == 0:
            return p
        if eighths == 2:
            return -im, re
        if eighths == 1:
            return half * (re - im), half * (re + im)
        return -half * (re + im), half * (re - im)

    def body(qi, carry):
        rows = pl.ds(pl.multiple_of(qi * 8, 8), 8)
        x = [(a_ref[s, 0, rows, :], a_ref[s, 1, rows, :]) for s in range(a_ref.shape[0])]
        span = 1
        while span < len(x):
            y = list(x)
            for start in range(0, len(x), 2 * span):
                for j in range(span):
                    u = x[start + j]
                    v = turn(x[start + j + span], j * len(x) // (2 * span))
                    y[start + j] = (u[0] + v[0], u[1] + v[1])
                    y[start + j + span] = (u[0] - v[0], u[1] - v[1])
            x = y
            span *= 2
        for m, (re, im) in enumerate(x):
            scale = fac_ref[m, base + qi]
            o_ref[m, 0, rows, :] = re * scale
            o_ref[m, 1, rows, :] = im * scale
        return carry

    lax.fori_loop(0, block, body, 0, unroll=SWEEP_UNROLL)


def combine_call(weights, factor, arrived, q_block):
    blocks, _, rows, width = arrived.shape
    spec = pl.BlockSpec((blocks, 2, q_block * 8, width), lambda g: (0, 0, g, 0))
    return pl.pallas_call(
        functools.partial(combine_kernel, weights),
        out_shape=jax.ShapeDtypeStruct(arrived.shape, jnp.float32),
        grid=(rows // (q_block * 8),),
        in_specs=[pl.BlockSpec(memory_space=pltpu.SMEM), spec],
        out_specs=spec,
        compiler_params=pltpu.CompilerParams(dimension_semantics=("arbitrary",)),
        cost_estimate=pl.CostEstimate(
            flops=40 * arrived.size, transcendentals=0, bytes_accessed=8 * arrived.size
        ),
    )(factor, arrived)


def class_weights(tm_count, bit_count):
    rows = []
    for m in range(tm_count):
        row = []
        for source in range(tm_count):
            angle = 2.0 * math.pi * ((m * reverse_bits(source, bit_count)) % tm_count) / tm_count
            c, s = math.cos(angle), math.sin(angle)
            c = float(np.float32(0.0 if abs(c) < 1e-9 else c))
            s = float(np.float32(0.0 if abs(s) < 1e-9 else s))
            row.append((c, s))
        rows.append(tuple(row))
    return tuple(rows)


def frames(diffusivity, d_top, d_bot, space_place, space_count):
    rows, cols = diffusivity.shape
    gap = jnp.zeros((16 - rows - 2 * HALO, cols), jnp.float32)
    diff_frame = jnp.concatenate([diffusivity, d_bot, gap, d_top], axis=0)
    row = jnp.arange(16, dtype=jnp.int32)
    keep = (row < rows) | ((row == rows) & (space_place < space_count - 1)) | (
        (row == 15) & (space_place > 0)
    )
    mask_frame = jnp.broadcast_to(keep.astype(jnp.float32)[:, None], (16, cols))
    return diff_frame, mask_frame


def on_device(spectrum, diffusivity):
    local_count = spectrum.shape[1]
    row_count = spectrum.shape[2]
    col_count = spectrum.shape[3]
    tm_count = lax.axis_size("tm")
    space_count = lax.axis_size("space")
    bit_count = tm_count.bit_length() - 1
    total_steps = local_count * tm_count
    tm_place = lax.axis_index("tm")
    space_place = lax.axis_index("space")
    residue = reverse_bits(tm_place, bit_count)
    index_f = jnp.arange(local_count, dtype=jnp.int32)
    freq_ids = index_f * tm_count + residue
    lam = jnp.stack(shift_parts(freq_ids, total_steps))

    diff_slot = jnp.broadcast_to(diffusivity[None, None], (2, 1, row_count, col_count))
    top, bottom = halo_pair(jnp.concatenate([spectrum, diff_slot], axis=1), "space", 2, HALO)
    diff_frame, mask_frame = frames(diffusivity, top[0, local_count], bottom[0, local_count], space_place, space_count)
    grid_angle = (index_f[:, None] * freq_ids[None, :] % total_steps).astype(jnp.float32) * (
        2.0 * math.pi / total_steps
    )
    cosine = jnp.cos(grid_angle)
    sine = jnp.sin(grid_angle)
    table = jnp.concatenate(
        [jnp.concatenate([cosine, -sine], 1), jnp.concatenate([sine, cosine], 1)], 0
    )
    outgoing = sweep_call(lam, spectrum, top, bottom, diff_frame, mask_frame, table, tm_count)
    col_block = col_count // tm_count
    outgoing = outgoing.reshape(tm_count, 2, local_count * row_count, col_block)
    arrived = lax.all_to_all(outgoing, "tm", 0, 0, tiled=True)

    step_ids = (
        jnp.arange(tm_count, dtype=jnp.int32)[:, None] * local_count
        + jnp.arange(local_count, dtype=jnp.int32)[None, :]
    ).astype(jnp.float32)
    factor = jnp.exp(step_ids * (-math.log(alpha_wrap) / total_steps)) / math.sqrt(total_steps)
    combined = combine_call(class_weights(tm_count, bit_count), factor, arrived, Q_BLOCK)
    returned = lax.all_to_all(combined, "tm", 0, 0, tiled=True)
    returned = returned.reshape(tm_count, 2, local_count, row_count, col_block)
    return jnp.moveaxis(returned, 0, 3).reshape(2, local_count, row_count, col_count)


def solution(mesh):
    in_specs = (P(None, "tm", "space", None), P("space", None))
    out_specs = P(None, "tm", "space", None)
    return jax.shard_map(
        on_device, mesh=mesh, in_specs=in_specs, out_specs=out_specs, check_vma=False
    )
```

```python
import functools
import math

import jax
import jax.numpy as jnp
import numpy as np
from jax import lax
from jax.experimental import pallas as pl
from jax.experimental.pallas import tpu as pltpu
from jax.sharding import PartitionSpec as P

alpha_wrap = 0.25
step_rate = 0.5
flow_speed = 2.0
sweep_weights = [
    1.0 / (1.0 + 0.7 * math.cos(math.pi * (2 * order + 1) / 6.0)) for order in range(3)
]
Q_BLOCK = 16
F_BLOCK = 16
SWEEP_UNROLL = 2
HALO = 2


def reverse_bits(number, bit_count):
    result = number * 0
    for bit_place in range(bit_count):
        result = result + (number >> bit_place & 1) * (1 << bit_count - 1 - bit_place)
    return result


def shift_parts(freq_ids, total_steps):
    phase_angle = freq_ids.astype(jnp.float32) * (2.0 * math.pi / total_steps)
    root_scale = alpha_wrap ** (1.0 / total_steps)
    return (
        step_rate * (1.0 - root_scale * jnp.cos(phase_angle)),
        step_rate * root_scale * jnp.sin(phase_angle),
    )


def halo_pair(block, axis, dim, width):
    count = lax.axis_size(axis)
    forward = [(i, i + 1) for i in range(count - 1)]
    backward = [(i + 1, i) for i in range(count - 1)]
    size = block.shape[dim]
    top = lax.ppermute(lax.slice_in_dim(block, size - width, size, axis=dim), axis, forward)
    bottom = lax.ppermute(lax.slice_in_dim(block, 0, width, axis=dim), axis, backward)
    return top, bottom


def sweep_kernel(final, lam_ref, rhs_ref, top_ref, bot_ref, diff_ref, mask_ref, *rest):
    if final:
        low_ref, high_ref, prev_ref, o_ref, field = rest
    else:
        (o_ref,) = rest
        field = o_ref
    block = rhs_ref.shape[1]
    count = lam_ref.shape[1]
    cols = rhs_ref.shape[3]
    base = pl.program_id(0) * block
    diff = diff_ref[...]
    diag_base = 4.0 * diff + flow_speed
    keep = mask_ref[...]
    row8 = lax.broadcasted_iota(jnp.int32, (8, cols), 0)
    col = lax.broadcasted_iota(jnp.int32, (16, cols), 1)

    def frame(x, f):
        local = rhs_ref[x, f]
        bv = bot_ref[x, f]
        tv = top_ref[x, f]
        hi = jnp.where(row8 == 0, jnp.broadcast_to(bv[0:1], (8, cols)), 0.0)
        hi = jnp.where(row8 == 1, jnp.broadcast_to(bv[1:2], (8, cols)), hi)
        hi = jnp.where(row8 == 6, jnp.broadcast_to(tv[0:1], (8, cols)), hi)
        hi = jnp.where(row8 == 7, jnp.broadcast_to(tv[1:2], (8, cols)), hi)
        return jnp.concatenate([local, hi], axis=0)

    def around(v):
        north = pltpu.roll(v, 1, 0)
        south = pltpu.roll(v, 15, 0)
        west = jnp.where(col == 0, 0.0, pltpu.roll(v, 1, 1))
        east = jnp.where(col == cols - 1, 0.0, pltpu.roll(v, cols - 1, 1))
        return north, north + south + west + east

    def body(f, carry):
        lam_r = lam_ref[0, base + f]
        lam_i = lam_ref[1, base + f]
        dr = diag_base + lam_r
        inv_mag = 1.0 / (dr * dr + lam_i * lam_i)
        r_re = frame(0, f)
        r_im = frame(1, f)
        c_re = sweep_weights[0] * ((r_re * dr + r_im * lam_i) * inv_mag)
        c_im = sweep_weights[0] * ((r_im * dr - r_re * lam_i) * inv_mag)
        for order in (1, 2):
            n_re, b_re = around(c_re)
            n_im, b_im = around(c_im)
            if order == 2:
                n_re, b_re, n_im, b_im = n_re[0:8], b_re[0:8], n_im[0:8], b_im[0:8]
                c_re, c_im, r_re, r_im = c_re[0:8], c_im[0:8], r_re[0:8], r_im[0:8]
                dr, inv_mag, d = dr[0:8], inv_mag[0:8], diff[0:8]
            else:
                d = diff
            a_re = dr * c_re - lam_i * c_im - d * b_re - flow_speed * n_re
            a_im = dr * c_im + lam_i * c_re - d * b_im - flow_speed * n_im
            s_re = r_re - a_re
            s_im = r_im - a_im
            c_re = c_re + sweep_weights[order] * ((s_re * dr + s_im * lam_i) * inv_mag)
            c_im = c_im + sweep_weights[order] * ((s_im * dr - s_re * lam_i) * inv_mag)
            if order == 1:
                c_re = c_re * keep
                c_im = c_im * keep
        width = field.shape[2]
        for blk in range(field.shape[0]):
            lanes = slice(blk * width, (blk + 1) * width)
            field[blk, pl.ds(pl.multiple_of((base + f) * 8, 8), 8), :] = c_re[0:8, lanes]
            field[blk, pl.ds(pl.multiple_of((count + base + f) * 8, 8), 8), :] = c_im[0:8, lanes]
        return carry

    lax.fori_loop(0, block, body, 0, unroll=SWEEP_UNROLL)

    if not final:
        return

    @pl.when(pl.program_id(0) == pl.num_programs(0) - 1)
    def _():
        low = low_ref[...]
        high = high_ref[...]
        rows_out = o_ref.shape[1] // 8
        for blk in range(o_ref.shape[0]):
            for r in range(8):
                first = prev_ref[blk, pl.ds(r, 2 * count, stride=8), :]
                second = field[blk, pl.ds(r, 2 * count, stride=8), :]
                o_ref[blk, pl.ds(r, rows_out, stride=8), :] = jnp.dot(
                    low, first, precision=lax.Precision.HIGH, preferred_element_type=jnp.float32
                ) + jnp.dot(high, second, precision=lax.Precision.HIGH, preferred_element_type=jnp.float32)


def sweep_call(lam, spectrum, offset, top, bottom, diff_frame, mask_frame, blocks, final=None):
    _, total, rows, cols = spectrum.shape
    count = lam.shape[1]
    block = F_BLOCK
    width = cols // blocks
    skip = offset // block
    big = pl.BlockSpec((2, block, rows, cols), lambda g: (0, g + skip, 0, 0))
    edge = pl.BlockSpec((2, block, HALO, cols), lambda g: (0, g, 0, 0))
    whole = pl.BlockSpec((16, cols), lambda g: (0, 0))
    field_rows = 2 * count * rows
    in_specs = [pl.BlockSpec(memory_space=pltpu.SMEM), big, edge, edge, whole, whole]
    operands = [lam, spectrum, top, bottom, diff_frame, mask_frame]
    scratch = []
    out_rows = field_rows
    if final is not None:
        low, high, prev = final
        half = pl.BlockSpec(low.shape, lambda g: (0, 0))
        in_specs += [half, half, pl.BlockSpec(prev.shape, lambda g: (0, 0, 0))]
        operands += [low, high, prev]
        scratch = [pltpu.VMEM((blocks, field_rows, width), jnp.float32)]
        out_rows = 2 * total * rows
    return pl.pallas_call(
        functools.partial(sweep_kernel, final is not None),
        out_shape=jax.ShapeDtypeStruct((blocks, out_rows, width), jnp.float32),
        grid=(count // block,),
        in_specs=in_specs,
        out_specs=pl.BlockSpec((blocks, out_rows, width), lambda g: (0, 0, 0)),
        scratch_shapes=scratch,
        compiler_params=pltpu.CompilerParams(dimension_semantics=("arbitrary",)),
        cost_estimate=pl.CostEstimate(
            flops=100 * spectrum.size, transcendentals=0, bytes_accessed=4 * spectrum.size
        ),
    )(*operands)


def combine_kernel(weights, fac_ref, a_ref, o_ref):
    block = a_ref.shape[2] // 8
    base = pl.program_id(0) * block
    half = float(np.float32(1.0 / math.sqrt(2.0)))

    def turn(p, eighths):
        re, im = p
        if eighths == 0:
            return p
        if eighths == 2:
            return -im, re
        if eighths == 1:
            return half * (re - im), half * (re + im)
        return -half * (re + im), half * (re - im)

    def body(qi, carry):
        rows = pl.ds(pl.multiple_of(qi * 8, 8), 8)
        x = [(a_ref[s, 0, rows, :], a_ref[s, 1, rows, :]) for s in range(a_ref.shape[0])]
        span = 1
        while span < len(x):
            y = list(x)
            for start in range(0, len(x), 2 * span):
                for j in range(span):
                    u = x[start + j]
                    v = turn(x[start + j + span], j * len(x) // (2 * span))
                    y[start + j] = (u[0] + v[0], u[1] + v[1])
                    y[start + j + span] = (u[0] - v[0], u[1] - v[1])
            x = y
            span *= 2
        for m, (re, im) in enumerate(x):
            scale = fac_ref[m, base + qi]
            o_ref[m, 0, rows, :] = re * scale
            o_ref[m, 1, rows, :] = im * scale
        return carry

    lax.fori_loop(0, block, body, 0, unroll=SWEEP_UNROLL)


def combine_call(weights, factor, arrived, q_block):
    blocks, _, rows, width = arrived.shape
    spec = pl.BlockSpec((blocks, 2, q_block * 8, width), lambda g: (0, 0, g, 0))
    return pl.pallas_call(
        functools.partial(combine_kernel, weights),
        out_shape=jax.ShapeDtypeStruct(arrived.shape, jnp.float32),
        grid=(rows // (q_block * 8),),
        in_specs=[pl.BlockSpec(memory_space=pltpu.SMEM), spec],
        out_specs=spec,
        compiler_params=pltpu.CompilerParams(dimension_semantics=("arbitrary",)),
        cost_estimate=pl.CostEstimate(
            flops=40 * arrived.size, transcendentals=0, bytes_accessed=8 * arrived.size
        ),
    )(factor, arrived)


def class_weights(tm_count, bit_count):
    rows = []
    for m in range(tm_count):
        row = []
        for source in range(tm_count):
            angle = 2.0 * math.pi * ((m * reverse_bits(source, bit_count)) % tm_count) / tm_count
            c, s = math.cos(angle), math.sin(angle)
            c = float(np.float32(0.0 if abs(c) < 1e-9 else c))
            s = float(np.float32(0.0 if abs(s) < 1e-9 else s))
            row.append((c, s))
        rows.append(tuple(row))
    return tuple(rows)


def frames(diffusivity, d_top, d_bot, space_place, space_count):
    rows, cols = diffusivity.shape
    gap = jnp.zeros((16 - rows - 2 * HALO, cols), jnp.float32)
    diff_frame = jnp.concatenate([diffusivity, d_bot, gap, d_top], axis=0)
    row = jnp.arange(16, dtype=jnp.int32)
    keep = (row < rows) | ((row == rows) & (space_place < space_count - 1)) | (
        (row == 15) & (space_place > 0)
    )
    mask_frame = jnp.broadcast_to(keep.astype(jnp.float32)[:, None], (16, cols))
    return diff_frame, mask_frame


def on_device(spectrum, diffusivity):
    local_count = spectrum.shape[1]
    row_count = spectrum.shape[2]
    col_count = spectrum.shape[3]
    tm_count = lax.axis_size("tm")
    space_count = lax.axis_size("space")
    bit_count = tm_count.bit_length() - 1
    total_steps = local_count * tm_count
    tm_place = lax.axis_index("tm")
    space_place = lax.axis_index("space")
    residue = reverse_bits(tm_place, bit_count)
    index_f = jnp.arange(local_count, dtype=jnp.int32)
    freq_ids = index_f * tm_count + residue
    lam = jnp.stack(shift_parts(freq_ids, total_steps))

    half = local_count // 2
    diff_slot = jnp.broadcast_to(diffusivity[None, None], (2, 1, row_count, col_count))
    top_a, bottom_a = halo_pair(jnp.concatenate([spectrum[:, :half], diff_slot], axis=1), "space", 2, HALO)
    top_b, bottom_b = halo_pair(spectrum[:, half:], "space", 2, HALO)
    diff_frame, mask_frame = frames(diffusivity, top_a[0, half], bottom_a[0, half], space_place, space_count)
    grid_angle = (index_f[:, None] * freq_ids[None, :] % total_steps).astype(jnp.float32) * (
        2.0 * math.pi / total_steps
    )
    cosine = jnp.cos(grid_angle)
    sine = jnp.sin(grid_angle)
    table = jnp.concatenate(
        [jnp.concatenate([cosine, -sine], 1), jnp.concatenate([sine, cosine], 1)], 0
    )
    low = jnp.concatenate([table[:, :half], table[:, local_count:local_count + half]], 1)
    high = jnp.concatenate([table[:, half:local_count], table[:, local_count + half:]], 1)
    first = sweep_call(lam[:, :half], spectrum, 0, top_a, bottom_a, diff_frame, mask_frame, tm_count)
    outgoing = sweep_call(
        lam[:, half:], spectrum, half, top_b, bottom_b, diff_frame, mask_frame, tm_count,
        final=(low, high, first),
    )
    col_block = col_count // tm_count
    outgoing = outgoing.reshape(tm_count, 2, local_count * row_count, col_block)
    arrived = lax.all_to_all(outgoing, "tm", 0, 0, tiled=True)

    step_ids = (
        jnp.arange(tm_count, dtype=jnp.int32)[:, None] * local_count
        + jnp.arange(local_count, dtype=jnp.int32)[None, :]
    ).astype(jnp.float32)
    factor = jnp.exp(step_ids * (-math.log(alpha_wrap) / total_steps)) / math.sqrt(total_steps)
    combined = combine_call(class_weights(tm_count, bit_count), factor, arrived, Q_BLOCK)
    returned = lax.all_to_all(combined, "tm", 0, 0, tiled=True)
    returned = returned.reshape(tm_count, 2, local_count, row_count, col_block)
    return jnp.moveaxis(returned, 0, 3).reshape(2, local_count, row_count, col_count)


def solution(mesh):
    in_specs = (P(None, "tm", "space", None), P("space", None))
    out_specs = P(None, "tm", "space", None)
    return jax.shard_map(
        on_device, mesh=mesh, in_specs=in_specs, out_specs=out_specs, check_vma=False
    )
```

```python
import functools
import math

import jax
import jax.numpy as jnp
import numpy as np
from jax import lax
from jax.experimental import pallas as pl
from jax.experimental.pallas import tpu as pltpu
from jax.sharding import PartitionSpec as P

alpha_wrap = 0.25
step_rate = 0.5
flow_speed = 2.0
sweep_weights = [
    1.0 / (1.0 + 0.7 * math.cos(math.pi * (2 * order + 1) / 6.0)) for order in range(3)
]
Q_BLOCK = 16
F_BLOCK = 16
SWEEP_UNROLL = 2
FIRST_SWEEP = 16
HALO = 2


def reverse_bits(number, bit_count):
    result = number * 0
    for bit_place in range(bit_count):
        result = result + (number >> bit_place & 1) * (1 << bit_count - 1 - bit_place)
    return result


def shift_parts(freq_ids, total_steps):
    phase_angle = freq_ids.astype(jnp.float32) * (2.0 * math.pi / total_steps)
    root_scale = alpha_wrap ** (1.0 / total_steps)
    return (
        step_rate * (1.0 - root_scale * jnp.cos(phase_angle)),
        step_rate * root_scale * jnp.sin(phase_angle),
    )


def halo_pair(block, axis, dim, width):
    count = lax.axis_size(axis)
    forward = [(i, i + 1) for i in range(count - 1)]
    backward = [(i + 1, i) for i in range(count - 1)]
    size = block.shape[dim]
    top = lax.ppermute(lax.slice_in_dim(block, size - width, size, axis=dim), axis, forward)
    bottom = lax.ppermute(lax.slice_in_dim(block, 0, width, axis=dim), axis, backward)
    return top, bottom


def sweep_kernel(final, lam_ref, rhs_ref, top_ref, bot_ref, diff_ref, mask_ref, *rest):
    if final:
        low_ref, high_ref, prev_ref, o_ref, field = rest
    else:
        (o_ref,) = rest
        field = o_ref
    block = rhs_ref.shape[1]
    count = lam_ref.shape[1]
    cols = rhs_ref.shape[3]
    base = pl.program_id(0) * block
    diff = diff_ref[...]
    diag_base = 4.0 * diff + flow_speed
    keep = mask_ref[...]
    row8 = lax.broadcasted_iota(jnp.int32, (8, cols), 0)
    col = lax.broadcasted_iota(jnp.int32, (16, cols), 1)

    def frame(x, f):
        local = rhs_ref[x, f]
        bv = bot_ref[x, f]
        tv = top_ref[x, f]
        hi = jnp.where(row8 == 0, jnp.broadcast_to(bv[0:1], (8, cols)), 0.0)
        hi = jnp.where(row8 == 1, jnp.broadcast_to(bv[1:2], (8, cols)), hi)
        hi = jnp.where(row8 == 6, jnp.broadcast_to(tv[0:1], (8, cols)), hi)
        hi = jnp.where(row8 == 7, jnp.broadcast_to(tv[1:2], (8, cols)), hi)
        return jnp.concatenate([local, hi], axis=0)

    def around(v):
        north = pltpu.roll(v, 1, 0)
        south = pltpu.roll(v, 15, 0)
        west = jnp.where(col == 0, 0.0, pltpu.roll(v, 1, 1))
        east = jnp.where(col == cols - 1, 0.0, pltpu.roll(v, cols - 1, 1))
        return north, north + south + west + east

    def body(f, carry):
        lam_r = lam_ref[0, base + f]
        lam_i = lam_ref[1, base + f]
        dr = diag_base + lam_r
        inv_mag = 1.0 / (dr * dr + lam_i * lam_i)
        r_re = frame(0, f)
        r_im = frame(1, f)
        c_re = sweep_weights[0] * ((r_re * dr + r_im * lam_i) * inv_mag)
        c_im = sweep_weights[0] * ((r_im * dr - r_re * lam_i) * inv_mag)
        for order in (1, 2):
            n_re, b_re = around(c_re)
            n_im, b_im = around(c_im)
            if order == 2:
                n_re, b_re, n_im, b_im = n_re[0:8], b_re[0:8], n_im[0:8], b_im[0:8]
                c_re, c_im, r_re, r_im = c_re[0:8], c_im[0:8], r_re[0:8], r_im[0:8]
                dr, inv_mag, d = dr[0:8], inv_mag[0:8], diff[0:8]
            else:
                d = diff
            a_re = dr * c_re - lam_i * c_im - d * b_re - flow_speed * n_re
            a_im = dr * c_im + lam_i * c_re - d * b_im - flow_speed * n_im
            s_re = r_re - a_re
            s_im = r_im - a_im
            c_re = c_re + sweep_weights[order] * ((s_re * dr + s_im * lam_i) * inv_mag)
            c_im = c_im + sweep_weights[order] * ((s_im * dr - s_re * lam_i) * inv_mag)
            if order == 1:
                c_re = c_re * keep
                c_im = c_im * keep
        width = field.shape[2]
        for blk in range(field.shape[0]):
            lanes = slice(blk * width, (blk + 1) * width)
            field[blk, pl.ds(pl.multiple_of((base + f) * 8, 8), 8), :] = c_re[0:8, lanes]
            field[blk, pl.ds(pl.multiple_of((count + base + f) * 8, 8), 8), :] = c_im[0:8, lanes]
        return carry

    lax.fori_loop(0, block, body, 0, unroll=SWEEP_UNROLL)

    if not final:
        return

    @pl.when(pl.program_id(0) == pl.num_programs(0) - 1)
    def _():
        low = low_ref[...]
        high = high_ref[...]
        rows_out = o_ref.shape[1] // 8
        for blk in range(o_ref.shape[0]):
            for r in range(8):
                first = prev_ref[blk, pl.ds(r, prev_ref.shape[1] // 8, stride=8), :]
                second = field[blk, pl.ds(r, 2 * count, stride=8), :]
                o_ref[blk, pl.ds(r, rows_out, stride=8), :] = jnp.dot(
                    low, first, precision=lax.Precision.HIGH, preferred_element_type=jnp.float32
                ) + jnp.dot(high, second, precision=lax.Precision.HIGH, preferred_element_type=jnp.float32)


def sweep_call(lam, spectrum, offset, top, bottom, diff_frame, mask_frame, blocks, final=None):
    _, total, rows, cols = spectrum.shape
    count = lam.shape[1]
    block = F_BLOCK
    width = cols // blocks
    skip = offset // block
    big = pl.BlockSpec((2, block, rows, cols), lambda g: (0, g + skip, 0, 0))
    edge = pl.BlockSpec((2, block, HALO, cols), lambda g: (0, g, 0, 0))
    whole = pl.BlockSpec((16, cols), lambda g: (0, 0))
    field_rows = 2 * count * rows
    in_specs = [pl.BlockSpec(memory_space=pltpu.SMEM), big, edge, edge, whole, whole]
    operands = [lam, spectrum, top, bottom, diff_frame, mask_frame]
    scratch = []
    out_rows = field_rows
    if final is not None:
        low, high, prev = final
        in_specs += [
            pl.BlockSpec(low.shape, lambda g: (0, 0)),
            pl.BlockSpec(high.shape, lambda g: (0, 0)),
            pl.BlockSpec(prev.shape, lambda g: (0, 0, 0)),
        ]
        operands += [low, high, prev]
        scratch = [pltpu.VMEM((blocks, field_rows, width), jnp.float32)]
        out_rows = 2 * total * rows
    return pl.pallas_call(
        functools.partial(sweep_kernel, final is not None),
        out_shape=jax.ShapeDtypeStruct((blocks, out_rows, width), jnp.float32),
        grid=(count // block,),
        in_specs=in_specs,
        out_specs=pl.BlockSpec((blocks, out_rows, width), lambda g: (0, 0, 0)),
        scratch_shapes=scratch,
        compiler_params=pltpu.CompilerParams(dimension_semantics=("arbitrary",)),
        cost_estimate=pl.CostEstimate(
            flops=100 * spectrum.size, transcendentals=0, bytes_accessed=4 * spectrum.size
        ),
    )(*operands)


def combine_kernel(weights, fac_ref, a_ref, o_ref):
    block = a_ref.shape[2] // 8
    base = pl.program_id(0) * block
    half = float(np.float32(1.0 / math.sqrt(2.0)))

    def turn(p, eighths):
        re, im = p
        if eighths == 0:
            return p
        if eighths == 2:
            return -im, re
        if eighths == 1:
            return half * (re - im), half * (re + im)
        return -half * (re + im), half * (re - im)

    def body(qi, carry):
        rows = pl.ds(pl.multiple_of(qi * 8, 8), 8)
        x = [(a_ref[s, 0, rows, :], a_ref[s, 1, rows, :]) for s in range(a_ref.shape[0])]
        span = 1
        while span < len(x):
            y = list(x)
            for start in range(0, len(x), 2 * span):
                for j in range(span):
                    u = x[start + j]
                    v = turn(x[start + j + span], j * len(x) // (2 * span))
                    y[start + j] = (u[0] + v[0], u[1] + v[1])
                    y[start + j + span] = (u[0] - v[0], u[1] - v[1])
            x = y
            span *= 2
        for m, (re, im) in enumerate(x):
            scale = fac_ref[m, base + qi]
            o_ref[m, 0, rows, :] = re * scale
            o_ref[m, 1, rows, :] = im * scale
        return carry

    lax.fori_loop(0, block, body, 0, unroll=SWEEP_UNROLL)


def combine_call(weights, factor, arrived, q_block):
    blocks, _, rows, width = arrived.shape
    spec = pl.BlockSpec((blocks, 2, q_block * 8, width), lambda g: (0, 0, g, 0))
    return pl.pallas_call(
        functools.partial(combine_kernel, weights),
        out_shape=jax.ShapeDtypeStruct(arrived.shape, jnp.float32),
        grid=(rows // (q_block * 8),),
        in_specs=[pl.BlockSpec(memory_space=pltpu.SMEM), spec],
        out_specs=spec,
        compiler_params=pltpu.CompilerParams(dimension_semantics=("arbitrary",)),
        cost_estimate=pl.CostEstimate(
            flops=40 * arrived.size, transcendentals=0, bytes_accessed=8 * arrived.size
        ),
    )(factor, arrived)


def class_weights(tm_count, bit_count):
    rows = []
    for m in range(tm_count):
        row = []
        for source in range(tm_count):
            angle = 2.0 * math.pi * ((m * reverse_bits(source, bit_count)) % tm_count) / tm_count
            c, s = math.cos(angle), math.sin(angle)
            c = float(np.float32(0.0 if abs(c) < 1e-9 else c))
            s = float(np.float32(0.0 if abs(s) < 1e-9 else s))
            row.append((c, s))
        rows.append(tuple(row))
    return tuple(rows)


def frames(diffusivity, d_top, d_bot, space_place, space_count):
    rows, cols = diffusivity.shape
    gap = jnp.zeros((16 - rows - 2 * HALO, cols), jnp.float32)
    diff_frame = jnp.concatenate([diffusivity, d_bot, gap, d_top], axis=0)
    row = jnp.arange(16, dtype=jnp.int32)
    keep = (row < rows) | ((row == rows) & (space_place < space_count - 1)) | (
        (row == 15) & (space_place > 0)
    )
    mask_frame = jnp.broadcast_to(keep.astype(jnp.float32)[:, None], (16, cols))
    return diff_frame, mask_frame


def on_device(spectrum, diffusivity):
    local_count = spectrum.shape[1]
    row_count = spectrum.shape[2]
    col_count = spectrum.shape[3]
    tm_count = lax.axis_size("tm")
    space_count = lax.axis_size("space")
    bit_count = tm_count.bit_length() - 1
    total_steps = local_count * tm_count
    tm_place = lax.axis_index("tm")
    space_place = lax.axis_index("space")
    residue = reverse_bits(tm_place, bit_count)
    index_f = jnp.arange(local_count, dtype=jnp.int32)
    freq_ids = index_f * tm_count + residue
    lam = jnp.stack(shift_parts(freq_ids, total_steps))

    half = FIRST_SWEEP
    diff_slot = jnp.broadcast_to(diffusivity[None, None], (2, 1, row_count, col_count))
    top_a, bottom_a = halo_pair(jnp.concatenate([spectrum[:, :half], diff_slot], axis=1), "space", 2, HALO)
    top_b, bottom_b = halo_pair(spectrum[:, half:], "space", 2, HALO)
    diff_frame, mask_frame = frames(diffusivity, top_a[0, half], bottom_a[0, half], space_place, space_count)
    grid_angle = (index_f[:, None] * freq_ids[None, :] % total_steps).astype(jnp.float32) * (
        2.0 * math.pi / total_steps
    )
    cosine = jnp.cos(grid_angle)
    sine = jnp.sin(grid_angle)
    table = jnp.concatenate(
        [jnp.concatenate([cosine, -sine], 1), jnp.concatenate([sine, cosine], 1)], 0
    )
    low = jnp.concatenate([table[:, :half], table[:, local_count:local_count + half]], 1)
    high = jnp.concatenate([table[:, half:local_count], table[:, local_count + half:]], 1)
    first = sweep_call(lam[:, :half], spectrum, 0, top_a, bottom_a, diff_frame, mask_frame, tm_count)
    outgoing = sweep_call(
        lam[:, half:], spectrum, half, top_b, bottom_b, diff_frame, mask_frame, tm_count,
        final=(low, high, first),
    )
    col_block = col_count // tm_count
    outgoing = outgoing.reshape(tm_count, 2, local_count * row_count, col_block)
    arrived = lax.all_to_all(outgoing, "tm", 0, 0, tiled=True)

    step_ids = (
        jnp.arange(tm_count, dtype=jnp.int32)[:, None] * local_count
        + jnp.arange(local_count, dtype=jnp.int32)[None, :]
    ).astype(jnp.float32)
    factor = jnp.exp(step_ids * (-math.log(alpha_wrap) / total_steps)) / math.sqrt(total_steps)
    combined = combine_call(class_weights(tm_count, bit_count), factor, arrived, Q_BLOCK)
    returned = lax.all_to_all(combined, "tm", 0, 0, tiled=True)
    returned = returned.reshape(tm_count, 2, local_count, row_count, col_block)
    return jnp.moveaxis(returned, 0, 3).reshape(2, local_count, row_count, col_count)


def solution(mesh):
    in_specs = (P(None, "tm", "space", None), P("space", None))
    out_specs = P(None, "tm", "space", None)
    return jax.shard_map(
        on_device, mesh=mesh, in_specs=in_specs, out_specs=out_specs, check_vma=False
    )
```

```python
import functools
import math

import jax
import jax.numpy as jnp
import numpy as np
from jax import lax
from jax.experimental import pallas as pl
from jax.experimental.pallas import tpu as pltpu
from jax.sharding import PartitionSpec as P

alpha_wrap = 0.25
step_rate = 0.5
flow_speed = 2.0
sweep_weights = [
    1.0 / (1.0 + 0.7 * math.cos(math.pi * (2 * order + 1) / 6.0)) for order in range(3)
]
Q_BLOCK = 16
F_BLOCK = 16
SWEEP_UNROLL = 4
HALO = 2


def reverse_bits(number, bit_count):
    result = number * 0
    for bit_place in range(bit_count):
        result = result + (number >> bit_place & 1) * (1 << bit_count - 1 - bit_place)
    return result


def shift_parts(freq_ids, total_steps):
    phase_angle = freq_ids.astype(jnp.float32) * (2.0 * math.pi / total_steps)
    root_scale = alpha_wrap ** (1.0 / total_steps)
    return (
        step_rate * (1.0 - root_scale * jnp.cos(phase_angle)),
        step_rate * root_scale * jnp.sin(phase_angle),
    )


def halo_pair(block, axis, dim, width):
    count = lax.axis_size(axis)
    forward = [(i, i + 1) for i in range(count - 1)]
    backward = [(i + 1, i) for i in range(count - 1)]
    size = block.shape[dim]
    top = lax.ppermute(lax.slice_in_dim(block, size - width, size, axis=dim), axis, forward)
    bottom = lax.ppermute(lax.slice_in_dim(block, 0, width, axis=dim), axis, backward)
    return top, bottom


def sweep_kernel(final, lam_ref, rhs_ref, top_ref, bot_ref, diff_ref, mask_ref, *rest):
    if final:
        low_ref, high_ref, prev_ref, o_ref, field = rest
    else:
        (o_ref,) = rest
        field = o_ref
    block = rhs_ref.shape[1]
    count = lam_ref.shape[1]
    cols = rhs_ref.shape[3]
    base = pl.program_id(0) * block
    diff = diff_ref[...]
    diag_base = 4.0 * diff + flow_speed
    keep = mask_ref[...]
    row8 = lax.broadcasted_iota(jnp.int32, (8, cols), 0)
    col = lax.broadcasted_iota(jnp.int32, (16, cols), 1)

    def frame(x, f):
        local = rhs_ref[x, f]
        bv = bot_ref[x, f]
        tv = top_ref[x, f]
        hi = jnp.where(row8 == 0, jnp.broadcast_to(bv[0:1], (8, cols)), 0.0)
        hi = jnp.where(row8 == 1, jnp.broadcast_to(bv[1:2], (8, cols)), hi)
        hi = jnp.where(row8 == 6, jnp.broadcast_to(tv[0:1], (8, cols)), hi)
        hi = jnp.where(row8 == 7, jnp.broadcast_to(tv[1:2], (8, cols)), hi)
        return jnp.concatenate([local, hi], axis=0)

    def around(v):
        north = pltpu.roll(v, 1, 0)
        south = pltpu.roll(v, 15, 0)
        west = jnp.where(col == 0, 0.0, pltpu.roll(v, 1, 1))
        east = jnp.where(col == cols - 1, 0.0, pltpu.roll(v, cols - 1, 1))
        return north, north + south + west + east

    def body(f, carry):
        lam_r = lam_ref[0, base + f]
        lam_i = lam_ref[1, base + f]
        dr = diag_base + lam_r
        inv_mag = 1.0 / (dr * dr + lam_i * lam_i)
        r_re = frame(0, f)
        r_im = frame(1, f)
        c_re = sweep_weights[0] * ((r_re * dr + r_im * lam_i) * inv_mag)
        c_im = sweep_weights[0] * ((r_im * dr - r_re * lam_i) * inv_mag)
        for order in (1, 2):
            n_re, b_re = around(c_re)
            n_im, b_im = around(c_im)
            if order == 2:
                n_re, b_re, n_im, b_im = n_re[0:8], b_re[0:8], n_im[0:8], b_im[0:8]
                c_re, c_im, r_re, r_im = c_re[0:8], c_im[0:8], r_re[0:8], r_im[0:8]
                dr, inv_mag, d = dr[0:8], inv_mag[0:8], diff[0:8]
            else:
                d = diff
            a_re = dr * c_re - lam_i * c_im - d * b_re - flow_speed * n_re
            a_im = dr * c_im + lam_i * c_re - d * b_im - flow_speed * n_im
            s_re = r_re - a_re
            s_im = r_im - a_im
            c_re = c_re + sweep_weights[order] * ((s_re * dr + s_im * lam_i) * inv_mag)
            c_im = c_im + sweep_weights[order] * ((s_im * dr - s_re * lam_i) * inv_mag)
            if order == 1:
                c_re = c_re * keep
                c_im = c_im * keep
        width = field.shape[2]
        for blk in range(field.shape[0]):
            lanes = slice(blk * width, (blk + 1) * width)
            field[blk, pl.ds(pl.multiple_of((base + f) * 8, 8), 8), :] = c_re[0:8, lanes]
            field[blk, pl.ds(pl.multiple_of((count + base + f) * 8, 8), 8), :] = c_im[0:8, lanes]
        return carry

    lax.fori_loop(0, block, body, 0, unroll=SWEEP_UNROLL)

    if not final:
        return

    @pl.when(pl.program_id(0) == pl.num_programs(0) - 1)
    def _():
        low = low_ref[...]
        high = high_ref[...]
        rows_out = o_ref.shape[1] // 8
        for blk in range(o_ref.shape[0]):
            for r in range(8):
                first = prev_ref[blk, pl.ds(r, 2 * count, stride=8), :]
                second = field[blk, pl.ds(r, 2 * count, stride=8), :]
                o_ref[blk, pl.ds(r, rows_out, stride=8), :] = jnp.dot(
                    low, first, precision=lax.Precision.HIGH, preferred_element_type=jnp.float32
                ) + jnp.dot(high, second, precision=lax.Precision.HIGH, preferred_element_type=jnp.float32)


def sweep_call(lam, spectrum, offset, top, bottom, diff_frame, mask_frame, blocks, final=None):
    _, total, rows, cols = spectrum.shape
    count = lam.shape[1]
    block = F_BLOCK
    width = cols // blocks
    skip = offset // block
    big = pl.BlockSpec((2, block, rows, cols), lambda g: (0, g + skip, 0, 0))
    edge = pl.BlockSpec((2, block, HALO, cols), lambda g: (0, g, 0, 0))
    whole = pl.BlockSpec((16, cols), lambda g: (0, 0))
    field_rows = 2 * count * rows
    in_specs = [pl.BlockSpec(memory_space=pltpu.SMEM), big, edge, edge, whole, whole]
    operands = [lam, spectrum, top, bottom, diff_frame, mask_frame]
    scratch = []
    out_rows = field_rows
    if final is not None:
        low, high, prev = final
        half = pl.BlockSpec(low.shape, lambda g: (0, 0))
        in_specs += [half, half, pl.BlockSpec(prev.shape, lambda g: (0, 0, 0))]
        operands += [low, high, prev]
        scratch = [pltpu.VMEM((blocks, field_rows, width), jnp.float32)]
        out_rows = 2 * total * rows
    return pl.pallas_call(
        functools.partial(sweep_kernel, final is not None),
        out_shape=jax.ShapeDtypeStruct((blocks, out_rows, width), jnp.float32),
        grid=(count // block,),
        in_specs=in_specs,
        out_specs=pl.BlockSpec((blocks, out_rows, width), lambda g: (0, 0, 0)),
        scratch_shapes=scratch,
        compiler_params=pltpu.CompilerParams(dimension_semantics=("arbitrary",)),
        cost_estimate=pl.CostEstimate(
            flops=100 * spectrum.size, transcendentals=0, bytes_accessed=4 * spectrum.size
        ),
    )(*operands)


def combine_kernel(weights, fac_ref, a_ref, o_ref):
    block = a_ref.shape[2] // 8
    base = pl.program_id(0) * block
    half = float(np.float32(1.0 / math.sqrt(2.0)))

    def turn(p, eighths):
        re, im = p
        if eighths == 0:
            return p
        if eighths == 2:
            return -im, re
        if eighths == 1:
            return half * (re - im), half * (re + im)
        return -half * (re + im), half * (re - im)

    def body(qi, carry):
        rows = pl.ds(pl.multiple_of(qi * 8, 8), 8)
        x = [(a_ref[s, 0, rows, :], a_ref[s, 1, rows, :]) for s in range(a_ref.shape[0])]
        span = 1
        while span < len(x):
            y = list(x)
            for start in range(0, len(x), 2 * span):
                for j in range(span):
                    u = x[start + j]
                    v = turn(x[start + j + span], j * len(x) // (2 * span))
                    y[start + j] = (u[0] + v[0], u[1] + v[1])
                    y[start + j + span] = (u[0] - v[0], u[1] - v[1])
            x = y
            span *= 2
        for m, (re, im) in enumerate(x):
            scale = fac_ref[m, base + qi]
            o_ref[m, 0, rows, :] = re * scale
            o_ref[m, 1, rows, :] = im * scale
        return carry

    lax.fori_loop(0, block, body, 0, unroll=SWEEP_UNROLL)


def combine_call(weights, factor, arrived, q_block):
    blocks, _, rows, width = arrived.shape
    spec = pl.BlockSpec((blocks, 2, q_block * 8, width), lambda g: (0, 0, g, 0))
    return pl.pallas_call(
        functools.partial(combine_kernel, weights),
        out_shape=jax.ShapeDtypeStruct(arrived.shape, jnp.float32),
        grid=(rows // (q_block * 8),),
        in_specs=[pl.BlockSpec(memory_space=pltpu.SMEM), spec],
        out_specs=spec,
        compiler_params=pltpu.CompilerParams(dimension_semantics=("arbitrary",)),
        cost_estimate=pl.CostEstimate(
            flops=40 * arrived.size, transcendentals=0, bytes_accessed=8 * arrived.size
        ),
    )(factor, arrived)


def class_weights(tm_count, bit_count):
    rows = []
    for m in range(tm_count):
        row = []
        for source in range(tm_count):
            angle = 2.0 * math.pi * ((m * reverse_bits(source, bit_count)) % tm_count) / tm_count
            c, s = math.cos(angle), math.sin(angle)
            c = float(np.float32(0.0 if abs(c) < 1e-9 else c))
            s = float(np.float32(0.0 if abs(s) < 1e-9 else s))
            row.append((c, s))
        rows.append(tuple(row))
    return tuple(rows)


def frames(diffusivity, d_top, d_bot, space_place, space_count):
    rows, cols = diffusivity.shape
    gap = jnp.zeros((16 - rows - 2 * HALO, cols), jnp.float32)
    diff_frame = jnp.concatenate([diffusivity, d_bot, gap, d_top], axis=0)
    row = jnp.arange(16, dtype=jnp.int32)
    keep = (row < rows) | ((row == rows) & (space_place < space_count - 1)) | (
        (row == 15) & (space_place > 0)
    )
    mask_frame = jnp.broadcast_to(keep.astype(jnp.float32)[:, None], (16, cols))
    return diff_frame, mask_frame


def on_device(spectrum, diffusivity):
    local_count = spectrum.shape[1]
    row_count = spectrum.shape[2]
    col_count = spectrum.shape[3]
    tm_count = lax.axis_size("tm")
    space_count = lax.axis_size("space")
    bit_count = tm_count.bit_length() - 1
    total_steps = local_count * tm_count
    tm_place = lax.axis_index("tm")
    space_place = lax.axis_index("space")
    residue = reverse_bits(tm_place, bit_count)
    index_f = jnp.arange(local_count, dtype=jnp.int32)
    freq_ids = index_f * tm_count + residue
    lam = jnp.stack(shift_parts(freq_ids, total_steps))

    half = local_count // 2
    diff_slot = jnp.broadcast_to(diffusivity[None, None], (2, 1, row_count, col_count))
    top_a, bottom_a = halo_pair(jnp.concatenate([spectrum[:, :half], diff_slot], axis=1), "space", 2, HALO)
    top_b, bottom_b = halo_pair(spectrum[:, half:], "space", 2, HALO)
    diff_frame, mask_frame = frames(diffusivity, top_a[0, half], bottom_a[0, half], space_place, space_count)
    grid_angle = (index_f[:, None] * freq_ids[None, :] % total_steps).astype(jnp.float32) * (
        2.0 * math.pi / total_steps
    )
    cosine = jnp.cos(grid_angle)
    sine = jnp.sin(grid_angle)
    table = jnp.concatenate(
        [jnp.concatenate([cosine, -sine], 1), jnp.concatenate([sine, cosine], 1)], 0
    )
    low = jnp.concatenate([table[:, :half], table[:, local_count:local_count + half]], 1)
    high = jnp.concatenate([table[:, half:local_count], table[:, local_count + half:]], 1)
    first = sweep_call(lam[:, :half], spectrum, 0, top_a, bottom_a, diff_frame, mask_frame, tm_count)
    outgoing = sweep_call(
        lam[:, half:], spectrum, half, top_b, bottom_b, diff_frame, mask_frame, tm_count,
        final=(low, high, first),
    )
    col_block = col_count // tm_count
    outgoing = outgoing.reshape(tm_count, 2, local_count * row_count, col_block)
    arrived = lax.all_to_all(outgoing, "tm", 0, 0, tiled=True)

    step_ids = (
        jnp.arange(tm_count, dtype=jnp.int32)[:, None] * local_count
        + jnp.arange(local_count, dtype=jnp.int32)[None, :]
    ).astype(jnp.float32)
    factor = jnp.exp(step_ids * (-math.log(alpha_wrap) / total_steps)) / math.sqrt(total_steps)
    combined = combine_call(class_weights(tm_count, bit_count), factor, arrived, Q_BLOCK)
    returned = lax.all_to_all(combined, "tm", 0, 0, tiled=True)
    returned = returned.reshape(tm_count, 2, local_count, row_count, col_block)
    return jnp.moveaxis(returned, 0, 3).reshape(2, local_count, row_count, col_count)


def solution(mesh):
    in_specs = (P(None, "tm", "space", None), P("space", None))
    out_specs = P(None, "tm", "space", None)
    return jax.shard_map(
        on_device, mesh=mesh, in_specs=in_specs, out_specs=out_specs, check_vma=False
    )
```

```python
import functools
import math

import jax
import jax.numpy as jnp
import numpy as np
from jax import lax
from jax.experimental import pallas as pl
from jax.experimental.pallas import tpu as pltpu
from jax.sharding import PartitionSpec as P

alpha_wrap = 0.25
step_rate = 0.5
flow_speed = 2.0
sweep_weights = [
    1.0 / (1.0 + 0.7 * math.cos(math.pi * (2 * order + 1) / 6.0)) for order in range(3)
]
Q_BLOCK = 16
F_BLOCK = 16
SWEEP_UNROLL = 4
HALO = 2


def reverse_bits(number, bit_count):
    result = number * 0
    for bit_place in range(bit_count):
        result = result + (number >> bit_place & 1) * (1 << bit_count - 1 - bit_place)
    return result


def shift_parts(freq_ids, total_steps):
    phase_angle = freq_ids.astype(jnp.float32) * (2.0 * math.pi / total_steps)
    root_scale = alpha_wrap ** (1.0 / total_steps)
    return (
        step_rate * (1.0 - root_scale * jnp.cos(phase_angle)),
        step_rate * root_scale * jnp.sin(phase_angle),
    )


def halo_pair(block, axis, dim, width):
    count = lax.axis_size(axis)
    forward = [(i, i + 1) for i in range(count - 1)]
    backward = [(i + 1, i) for i in range(count - 1)]
    size = block.shape[dim]
    top = lax.ppermute(lax.slice_in_dim(block, size - width, size, axis=dim), axis, forward)
    bottom = lax.ppermute(lax.slice_in_dim(block, 0, width, axis=dim), axis, backward)
    return top, bottom


def sweep_kernel(final, lam_ref, rhs_ref, top_ref, bot_ref, diff_ref, mask_ref, *rest):
    if final:
        low_ref, high_ref, prev_ref, o_ref, field = rest
    else:
        (o_ref,) = rest
        field = o_ref
    block = rhs_ref.shape[1]
    count = lam_ref.shape[1]
    cols = rhs_ref.shape[3]
    base = pl.program_id(0) * block
    diff = diff_ref[...]
    diag_base = 4.0 * diff + flow_speed
    keep = mask_ref[...]
    row8 = lax.broadcasted_iota(jnp.int32, (8, cols), 0)
    col = lax.broadcasted_iota(jnp.int32, (16, cols), 1)

    def frame(x, f):
        local = rhs_ref[x, f]
        bv = bot_ref[x, f]
        tv = top_ref[x, f]
        hi = jnp.where(row8 == 0, jnp.broadcast_to(bv[0:1], (8, cols)), 0.0)
        hi = jnp.where(row8 == 1, jnp.broadcast_to(bv[1:2], (8, cols)), hi)
        hi = jnp.where(row8 == 6, jnp.broadcast_to(tv[0:1], (8, cols)), hi)
        hi = jnp.where(row8 == 7, jnp.broadcast_to(tv[1:2], (8, cols)), hi)
        return jnp.concatenate([local, hi], axis=0)

    def around(v):
        north = pltpu.roll(v, 1, 0)
        south = pltpu.roll(v, 15, 0)
        west = jnp.where(col == 0, 0.0, pltpu.roll(v, 1, 1))
        east = jnp.where(col == cols - 1, 0.0, pltpu.roll(v, cols - 1, 1))
        return north, north + south + west + east

    def body(f, carry):
        lam_r = lam_ref[0, base + f]
        lam_i = lam_ref[1, base + f]
        dr = diag_base + lam_r
        inv_mag = 1.0 / (dr * dr + lam_i * lam_i)
        r_re = frame(0, f)
        r_im = frame(1, f)
        c_re = sweep_weights[0] * ((r_re * dr + r_im * lam_i) * inv_mag)
        c_im = sweep_weights[0] * ((r_im * dr - r_re * lam_i) * inv_mag)
        for order in (1, 2):
            n_re, b_re = around(c_re)
            n_im, b_im = around(c_im)
            if order == 2:
                n_re, b_re, n_im, b_im = n_re[0:8], b_re[0:8], n_im[0:8], b_im[0:8]
                c_re, c_im, r_re, r_im = c_re[0:8], c_im[0:8], r_re[0:8], r_im[0:8]
                dr, inv_mag, d = dr[0:8], inv_mag[0:8], diff[0:8]
            else:
                d = diff
            a_re = dr * c_re - lam_i * c_im - d * b_re - flow_speed * n_re
            a_im = dr * c_im + lam_i * c_re - d * b_im - flow_speed * n_im
            s_re = r_re - a_re
            s_im = r_im - a_im
            c_re = c_re + sweep_weights[order] * ((s_re * dr + s_im * lam_i) * inv_mag)
            c_im = c_im + sweep_weights[order] * ((s_im * dr - s_re * lam_i) * inv_mag)
            if order == 1:
                c_re = c_re * keep
                c_im = c_im * keep
        width = field.shape[2]
        for blk in range(field.shape[0]):
            lanes = slice(blk * width, (blk + 1) * width)
            field[blk, pl.ds(pl.multiple_of((base + f) * 8, 8), 8), :] = c_re[0:8, lanes]
            field[blk, pl.ds(pl.multiple_of((count + base + f) * 8, 8), 8), :] = c_im[0:8, lanes]
        return carry

    lax.fori_loop(0, block, body, 0, unroll=SWEEP_UNROLL)

    if not final:
        return

    @pl.when(pl.program_id(0) == pl.num_programs(0) - 1)
    def _():
        low = low_ref[...]
        high = high_ref[...]
        rows_out = o_ref.shape[1] // 8
        for blk in range(o_ref.shape[0]):
            for r in range(8):
                first = prev_ref[blk, pl.ds(r, 2 * count, stride=8), :]
                second = field[blk, pl.ds(r, 2 * count, stride=8), :]
                o_ref[blk, pl.ds(r, rows_out, stride=8), :] = jnp.dot(
                    low, first, precision=lax.Precision.HIGH, preferred_element_type=jnp.float32
                ) + jnp.dot(high, second, precision=lax.Precision.HIGH, preferred_element_type=jnp.float32)


def sweep_call(lam, spectrum, offset, top, bottom, diff_frame, mask_frame, blocks, final=None):
    _, total, rows, cols = spectrum.shape
    count = lam.shape[1]
    block = F_BLOCK
    width = cols // blocks
    skip = offset // block
    big = pl.BlockSpec((2, block, rows, cols), lambda g: (0, g + skip, 0, 0))
    edge = pl.BlockSpec((2, block, HALO, cols), lambda g: (0, g, 0, 0))
    whole = pl.BlockSpec((16, cols), lambda g: (0, 0))
    field_rows = 2 * count * rows
    in_specs = [pl.BlockSpec(memory_space=pltpu.SMEM), big, edge, edge, whole, whole]
    operands = [lam, spectrum, top, bottom, diff_frame, mask_frame]
    scratch = []
    out_rows = field_rows
    if final is not None:
        low, high, prev = final
        half = pl.BlockSpec(low.shape, lambda g: (0, 0))
        in_specs += [half, half, pl.BlockSpec(prev.shape, lambda g: (0, 0, 0))]
        operands += [low, high, prev]
        scratch = [pltpu.VMEM((blocks, field_rows, width), jnp.float32)]
        out_rows = 2 * total * rows
    return pl.pallas_call(
        functools.partial(sweep_kernel, final is not None),
        out_shape=jax.ShapeDtypeStruct((blocks, out_rows, width), jnp.float32),
        grid=(count // block,),
        in_specs=in_specs,
        out_specs=pl.BlockSpec((blocks, out_rows, width), lambda g: (0, 0, 0)),
        scratch_shapes=scratch,
        compiler_params=pltpu.CompilerParams(dimension_semantics=("arbitrary",)),
        cost_estimate=pl.CostEstimate(
            flops=100 * spectrum.size, transcendentals=0, bytes_accessed=4 * spectrum.size
        ),
    )(*operands)


def combine_kernel(weights, dev_ref, fac_ref, a_ref, o_ref):
    block = a_ref.shape[2] // 8
    base = pl.program_id(0) * block
    half = float(np.float32(1.0 / math.sqrt(2.0)))

    def turn(p, eighths):
        re, im = p
        if eighths == 0:
            return p
        if eighths == 2:
            return -im, re
        if eighths == 1:
            return half * (re - im), half * (re + im)
        return -half * (re + im), half * (re - im)

    def body(qi, carry):
        rows = pl.ds(pl.multiple_of(qi * 8, 8), 8)
        x = [(a_ref[s, 0, rows, :], a_ref[s, 1, rows, :]) for s in range(a_ref.shape[0])]
        span = 1
        while span < len(x):
            y = list(x)
            for start in range(0, len(x), 2 * span):
                for j in range(span):
                    u = x[start + j]
                    v = turn(x[start + j + span], j * len(x) // (2 * span))
                    y[start + j] = (u[0] + v[0], u[1] + v[1])
                    y[start + j + span] = (u[0] - v[0], u[1] - v[1])
            x = y
            span *= 2
        device = dev_ref[0]
        for m, (re, im) in enumerate(x):
            scale = fac_ref[m, base + qi]
            o_ref[m ^ device, 0, rows, :] = re * scale
            o_ref[m ^ device, 1, rows, :] = im * scale
        return carry

    lax.fori_loop(0, block, body, 0, unroll=SWEEP_UNROLL)


def combine_call(weights, device, factor, arrived, q_block):
    blocks, _, rows, width = arrived.shape
    spec = pl.BlockSpec((blocks, 2, q_block * 8, width), lambda g: (0, 0, g, 0))
    return pl.pallas_call(
        functools.partial(combine_kernel, weights),
        out_shape=jax.ShapeDtypeStruct(arrived.shape, jnp.float32),
        grid=(rows // (q_block * 8),),
        in_specs=[pl.BlockSpec(memory_space=pltpu.SMEM)] * 2 + [spec],
        out_specs=spec,
        compiler_params=pltpu.CompilerParams(dimension_semantics=("arbitrary",)),
        cost_estimate=pl.CostEstimate(
            flops=40 * arrived.size, transcendentals=0, bytes_accessed=8 * arrived.size
        ),
    )(device, factor, arrived)


def place_kernel(dev_ref, *refs):
    count = len(refs) - 1
    in_refs, o_ref = refs[:count], refs[count]
    width = in_refs[0].shape[2]
    device = dev_ref[0]
    for slot, ref in enumerate(in_refs):
        start = pl.multiple_of((device ^ slot) * width, width)
        o_ref[:, :, pl.ds(start, width)] = ref[...]


def place_call(device, slots, q_block):
    _, rows, width = slots[0].shape
    count = len(slots)
    spec = pl.BlockSpec((2, q_block * 8, width), lambda g: (0, g, 0))
    return pl.pallas_call(
        place_kernel,
        out_shape=jax.ShapeDtypeStruct((2, rows, width * count), jnp.float32),
        grid=(rows // (q_block * 8),),
        in_specs=[pl.BlockSpec(memory_space=pltpu.SMEM)] + [spec] * count,
        out_specs=pl.BlockSpec((2, q_block * 8, width * count), lambda g: (0, g, 0)),
        compiler_params=pltpu.CompilerParams(dimension_semantics=("arbitrary",)),
    )(device, *slots)


def xor_exchange(slots, axis):
    received = [slots[0]]
    for slot in range(1, len(slots)):
        pairs = [(i, i ^ slot) for i in range(len(slots))]
        received.append(lax.ppermute(slots[slot], axis, pairs))
    return received


def class_weights(tm_count, bit_count):
    rows = []
    for m in range(tm_count):
        row = []
        for source in range(tm_count):
            angle = 2.0 * math.pi * ((m * reverse_bits(source, bit_count)) % tm_count) / tm_count
            c, s = math.cos(angle), math.sin(angle)
            c = float(np.float32(0.0 if abs(c) < 1e-9 else c))
            s = float(np.float32(0.0 if abs(s) < 1e-9 else s))
            row.append((c, s))
        rows.append(tuple(row))
    return tuple(rows)


def frames(diffusivity, d_top, d_bot, space_place, space_count):
    rows, cols = diffusivity.shape
    gap = jnp.zeros((16 - rows - 2 * HALO, cols), jnp.float32)
    diff_frame = jnp.concatenate([diffusivity, d_bot, gap, d_top], axis=0)
    row = jnp.arange(16, dtype=jnp.int32)
    keep = (row < rows) | ((row == rows) & (space_place < space_count - 1)) | (
        (row == 15) & (space_place > 0)
    )
    mask_frame = jnp.broadcast_to(keep.astype(jnp.float32)[:, None], (16, cols))
    return diff_frame, mask_frame


def on_device(spectrum, diffusivity):
    local_count = spectrum.shape[1]
    row_count = spectrum.shape[2]
    col_count = spectrum.shape[3]
    tm_count = lax.axis_size("tm")
    space_count = lax.axis_size("space")
    bit_count = tm_count.bit_length() - 1
    total_steps = local_count * tm_count
    tm_place = lax.axis_index("tm")
    space_place = lax.axis_index("space")
    residue = reverse_bits(tm_place, bit_count)
    index_f = jnp.arange(local_count, dtype=jnp.int32)
    freq_ids = index_f * tm_count + residue
    lam = jnp.stack(shift_parts(freq_ids, total_steps))

    half = local_count // 2
    diff_slot = jnp.broadcast_to(diffusivity[None, None], (2, 1, row_count, col_count))
    top_a, bottom_a = halo_pair(jnp.concatenate([spectrum[:, :half], diff_slot], axis=1), "space", 2, HALO)
    top_b, bottom_b = halo_pair(spectrum[:, half:], "space", 2, HALO)
    diff_frame, mask_frame = frames(diffusivity, top_a[0, half], bottom_a[0, half], space_place, space_count)
    grid_angle = (index_f[:, None] * freq_ids[None, :] % total_steps).astype(jnp.float32) * (
        2.0 * math.pi / total_steps
    )
    cosine = jnp.cos(grid_angle)
    sine = jnp.sin(grid_angle)
    table = jnp.concatenate(
        [jnp.concatenate([cosine, -sine], 1), jnp.concatenate([sine, cosine], 1)], 0
    )
    low = jnp.concatenate([table[:, :half], table[:, local_count:local_count + half]], 1)
    high = jnp.concatenate([table[:, half:local_count], table[:, local_count + half:]], 1)
    first = sweep_call(lam[:, :half], spectrum, 0, top_a, bottom_a, diff_frame, mask_frame, tm_count)
    outgoing = sweep_call(
        lam[:, half:], spectrum, half, top_b, bottom_b, diff_frame, mask_frame, tm_count,
        final=(low, high, first),
    )
    col_block = col_count // tm_count
    outgoing = outgoing.reshape(tm_count, 2, local_count * row_count, col_block)
    arrived = lax.all_to_all(outgoing, "tm", 0, 0, tiled=True)

    step_ids = (
        jnp.arange(tm_count, dtype=jnp.int32)[:, None] * local_count
        + jnp.arange(local_count, dtype=jnp.int32)[None, :]
    ).astype(jnp.float32)
    factor = jnp.exp(step_ids * (-math.log(alpha_wrap) / total_steps)) / math.sqrt(total_steps)
    device = jnp.reshape(tm_place, (1,)).astype(jnp.int32)
    combined = combine_call(class_weights(tm_count, bit_count), device, factor, arrived, Q_BLOCK)
    returned = xor_exchange([combined[s] for s in range(tm_count)], "tm")
    placed = place_call(device, returned, Q_BLOCK)
    return placed.reshape(2, local_count, row_count, col_count)


def solution(mesh):
    in_specs = (P(None, "tm", "space", None), P("space", None))
    out_specs = P(None, "tm", "space", None)
    return jax.shard_map(
        on_device, mesh=mesh, in_specs=in_specs, out_specs=out_specs, check_vma=False
    )
```

```python
import functools
import math

import jax
import jax.numpy as jnp
import numpy as np
from jax import lax
from jax.experimental import pallas as pl
from jax.experimental.pallas import tpu as pltpu
from jax.sharding import PartitionSpec as P

alpha_wrap = 0.25
step_rate = 0.5
flow_speed = 2.0
sweep_weights = [
    1.0 / (1.0 + 0.7 * math.cos(math.pi * (2 * order + 1) / 6.0)) for order in range(3)
]
Q_BLOCK = 16
F_BLOCK = 16
SWEEP_UNROLL = 4
HALO = 2


def reverse_bits(number, bit_count):
    result = number * 0
    for bit_place in range(bit_count):
        result = result + (number >> bit_place & 1) * (1 << bit_count - 1 - bit_place)
    return result


def shift_parts(freq_ids, total_steps):
    phase_angle = freq_ids.astype(jnp.float32) * (2.0 * math.pi / total_steps)
    root_scale = alpha_wrap ** (1.0 / total_steps)
    return (
        step_rate * (1.0 - root_scale * jnp.cos(phase_angle)),
        step_rate * root_scale * jnp.sin(phase_angle),
    )


def halo_pair(block, axis, dim, width):
    count = lax.axis_size(axis)
    forward = [(i, i + 1) for i in range(count - 1)]
    backward = [(i + 1, i) for i in range(count - 1)]
    size = block.shape[dim]
    top = lax.ppermute(lax.slice_in_dim(block, size - width, size, axis=dim), axis, forward)
    bottom = lax.ppermute(lax.slice_in_dim(block, 0, width, axis=dim), axis, backward)
    return top, bottom


def sweep_kernel(final, lam_ref, rhs_ref, top_ref, bot_ref, diff_ref, mask_ref, *rest):
    if final:
        low_ref, high_ref, prev_ref, o_ref, field = rest
    else:
        (o_ref,) = rest
        field = o_ref
    block = rhs_ref.shape[1]
    count = lam_ref.shape[1]
    cols = rhs_ref.shape[3]
    base = pl.program_id(0) * block
    diff = diff_ref[...]
    diag_base = 4.0 * diff + flow_speed
    keep = mask_ref[...]
    row8 = lax.broadcasted_iota(jnp.int32, (8, cols), 0)
    col = lax.broadcasted_iota(jnp.int32, (16, cols), 1)

    def frame(x, f):
        local = rhs_ref[x, f]
        bv = bot_ref[x, f]
        tv = top_ref[x, f]
        hi = jnp.where(row8 == 0, jnp.broadcast_to(bv[0:1], (8, cols)), 0.0)
        hi = jnp.where(row8 == 1, jnp.broadcast_to(bv[1:2], (8, cols)), hi)
        hi = jnp.where(row8 == 6, jnp.broadcast_to(tv[0:1], (8, cols)), hi)
        hi = jnp.where(row8 == 7, jnp.broadcast_to(tv[1:2], (8, cols)), hi)
        return jnp.concatenate([local, hi], axis=0)

    def around(v):
        north = pltpu.roll(v, 1, 0)
        south = pltpu.roll(v, 15, 0)
        west = jnp.where(col == 0, 0.0, pltpu.roll(v, 1, 1))
        east = jnp.where(col == cols - 1, 0.0, pltpu.roll(v, cols - 1, 1))
        return north, north + south + west + east

    def body(f, carry):
        lam_r = lam_ref[0, base + f]
        lam_i = lam_ref[1, base + f]
        dr = diag_base + lam_r
        inv_mag = 1.0 / (dr * dr + lam_i * lam_i)
        r_re = frame(0, f)
        r_im = frame(1, f)
        g_re = (r_re * dr + r_im * lam_i) * inv_mag
        g_im = (r_im * dr - r_re * lam_i) * inv_mag
        c_re = sweep_weights[0] * g_re
        c_im = sweep_weights[0] * g_im
        for order in (1, 2):
            n_re, b_re = around(c_re)
            n_im, b_im = around(c_im)
            if order == 2:
                n_re, b_re, n_im, b_im = n_re[0:8], b_re[0:8], n_im[0:8], b_im[0:8]
                c_re, c_im, g_re, g_im = c_re[0:8], c_im[0:8], g_re[0:8], g_im[0:8]
                dr, inv_mag, d = dr[0:8], inv_mag[0:8], diff[0:8]
            else:
                d = diff
            weight = sweep_weights[order]
            t_re = d * b_re + flow_speed * n_re
            t_im = d * b_im + flow_speed * n_im
            scaled = weight * inv_mag
            c_re = c_re + weight * (g_re - c_re) + (t_re * dr + t_im * lam_i) * scaled
            c_im = c_im + weight * (g_im - c_im) + (t_im * dr - t_re * lam_i) * scaled
            if order == 1:
                c_re = c_re * keep
                c_im = c_im * keep
        width = field.shape[2]
        for blk in range(field.shape[0]):
            lanes = slice(blk * width, (blk + 1) * width)
            field[blk, pl.ds(pl.multiple_of((base + f) * 8, 8), 8), :] = c_re[0:8, lanes]
            field[blk, pl.ds(pl.multiple_of((count + base + f) * 8, 8), 8), :] = c_im[0:8, lanes]
        return carry

    lax.fori_loop(0, block, body, 0, unroll=SWEEP_UNROLL)

    if not final:
        return

    @pl.when(pl.program_id(0) == pl.num_programs(0) - 1)
    def _():
        low = low_ref[...]
        high = high_ref[...]
        rows_out = o_ref.shape[1] // 8
        for blk in range(o_ref.shape[0]):
            for r in range(8):
                first = prev_ref[blk, pl.ds(r, 2 * count, stride=8), :]
                second = field[blk, pl.ds(r, 2 * count, stride=8), :]
                o_ref[blk, pl.ds(r, rows_out, stride=8), :] = jnp.dot(
                    low, first, precision=lax.Precision.HIGH, preferred_element_type=jnp.float32
                ) + jnp.dot(high, second, precision=lax.Precision.HIGH, preferred_element_type=jnp.float32)


def sweep_call(lam, spectrum, offset, top, bottom, diff_frame, mask_frame, blocks, final=None):
    _, total, rows, cols = spectrum.shape
    count = lam.shape[1]
    block = F_BLOCK
    width = cols // blocks
    skip = offset // block
    big = pl.BlockSpec((2, block, rows, cols), lambda g: (0, g + skip, 0, 0))
    edge = pl.BlockSpec((2, block, HALO, cols), lambda g: (0, g, 0, 0))
    whole = pl.BlockSpec((16, cols), lambda g: (0, 0))
    field_rows = 2 * count * rows
    in_specs = [pl.BlockSpec(memory_space=pltpu.SMEM), big, edge, edge, whole, whole]
    operands = [lam, spectrum, top, bottom, diff_frame, mask_frame]
    scratch = []
    out_rows = field_rows
    if final is not None:
        low, high, prev = final
        half = pl.BlockSpec(low.shape, lambda g: (0, 0))
        in_specs += [half, half, pl.BlockSpec(prev.shape, lambda g: (0, 0, 0))]
        operands += [low, high, prev]
        scratch = [pltpu.VMEM((blocks, field_rows, width), jnp.float32)]
        out_rows = 2 * total * rows
    return pl.pallas_call(
        functools.partial(sweep_kernel, final is not None),
        out_shape=jax.ShapeDtypeStruct((blocks, out_rows, width), jnp.float32),
        grid=(count // block,),
        in_specs=in_specs,
        out_specs=pl.BlockSpec((blocks, out_rows, width), lambda g: (0, 0, 0)),
        scratch_shapes=scratch,
        compiler_params=pltpu.CompilerParams(dimension_semantics=("arbitrary",)),
        cost_estimate=pl.CostEstimate(
            flops=100 * spectrum.size, transcendentals=0, bytes_accessed=4 * spectrum.size
        ),
    )(*operands)


def combine_kernel(weights, fac_ref, a_ref, o_ref):
    block = a_ref.shape[2] // 8
    base = pl.program_id(0) * block
    half = float(np.float32(1.0 / math.sqrt(2.0)))

    def turn(p, eighths):
        re, im = p
        if eighths == 0:
            return p
        if eighths == 2:
            return -im, re
        if eighths == 1:
            return half * (re - im), half * (re + im)
        return -half * (re + im), half * (re - im)

    def body(qi, carry):
        rows = pl.ds(pl.multiple_of(qi * 8, 8), 8)
        x = [(a_ref[s, 0, rows, :], a_ref[s, 1, rows, :]) for s in range(a_ref.shape[0])]
        span = 1
        while span < len(x):
            y = list(x)
            for start in range(0, len(x), 2 * span):
                for j in range(span):
                    u = x[start + j]
                    v = turn(x[start + j + span], j * len(x) // (2 * span))
                    y[start + j] = (u[0] + v[0], u[1] + v[1])
                    y[start + j + span] = (u[0] - v[0], u[1] - v[1])
            x = y
            span *= 2
        for m, (re, im) in enumerate(x):
            scale = fac_ref[m, base + qi]
            o_ref[m, 0, rows, :] = re * scale
            o_ref[m, 1, rows, :] = im * scale
        return carry

    lax.fori_loop(0, block, body, 0, unroll=SWEEP_UNROLL)


def combine_call(weights, factor, arrived, q_block):
    blocks, _, rows, width = arrived.shape
    spec = pl.BlockSpec((blocks, 2, q_block * 8, width), lambda g: (0, 0, g, 0))
    return pl.pallas_call(
        functools.partial(combine_kernel, weights),
        out_shape=jax.ShapeDtypeStruct(arrived.shape, jnp.float32),
        grid=(rows // (q_block * 8),),
        in_specs=[pl.BlockSpec(memory_space=pltpu.SMEM), spec],
        out_specs=spec,
        compiler_params=pltpu.CompilerParams(dimension_semantics=("arbitrary",)),
        cost_estimate=pl.CostEstimate(
            flops=40 * arrived.size, transcendentals=0, bytes_accessed=8 * arrived.size
        ),
    )(factor, arrived)


def class_weights(tm_count, bit_count):
    rows = []
    for m in range(tm_count):
        row = []
        for source in range(tm_count):
            angle = 2.0 * math.pi * ((m * reverse_bits(source, bit_count)) % tm_count) / tm_count
            c, s = math.cos(angle), math.sin(angle)
            c = float(np.float32(0.0 if abs(c) < 1e-9 else c))
            s = float(np.float32(0.0 if abs(s) < 1e-9 else s))
            row.append((c, s))
        rows.append(tuple(row))
    return tuple(rows)


def frames(diffusivity, d_top, d_bot, space_place, space_count):
    rows, cols = diffusivity.shape
    gap = jnp.zeros((16 - rows - 2 * HALO, cols), jnp.float32)
    diff_frame = jnp.concatenate([diffusivity, d_bot, gap, d_top], axis=0)
    row = jnp.arange(16, dtype=jnp.int32)
    keep = (row < rows) | ((row == rows) & (space_place < space_count - 1)) | (
        (row == 15) & (space_place > 0)
    )
    mask_frame = jnp.broadcast_to(keep.astype(jnp.float32)[:, None], (16, cols))
    return diff_frame, mask_frame


def on_device(spectrum, diffusivity):
    local_count = spectrum.shape[1]
    row_count = spectrum.shape[2]
    col_count = spectrum.shape[3]
    tm_count = lax.axis_size("tm")
    space_count = lax.axis_size("space")
    bit_count = tm_count.bit_length() - 1
    total_steps = local_count * tm_count
    tm_place = lax.axis_index("tm")
    space_place = lax.axis_index("space")
    residue = reverse_bits(tm_place, bit_count)
    index_f = jnp.arange(local_count, dtype=jnp.int32)
    freq_ids = index_f * tm_count + residue
    lam = jnp.stack(shift_parts(freq_ids, total_steps))

    half = local_count // 2
    diff_slot = jnp.broadcast_to(diffusivity[None, None], (2, 1, row_count, col_count))
    top_a, bottom_a = halo_pair(jnp.concatenate([spectrum[:, :half], diff_slot], axis=1), "space", 2, HALO)
    top_b, bottom_b = halo_pair(spectrum[:, half:], "space", 2, HALO)
    diff_frame, mask_frame = frames(diffusivity, top_a[0, half], bottom_a[0, half], space_place, space_count)
    grid_angle = (index_f[:, None] * freq_ids[None, :] % total_steps).astype(jnp.float32) * (
        2.0 * math.pi / total_steps
    )
    cosine = jnp.cos(grid_angle)
    sine = jnp.sin(grid_angle)
    table = jnp.concatenate(
        [jnp.concatenate([cosine, -sine], 1), jnp.concatenate([sine, cosine], 1)], 0
    )
    low = jnp.concatenate([table[:, :half], table[:, local_count:local_count + half]], 1)
    high = jnp.concatenate([table[:, half:local_count], table[:, local_count + half:]], 1)
    first = sweep_call(lam[:, :half], spectrum, 0, top_a, bottom_a, diff_frame, mask_frame, tm_count)
    outgoing = sweep_call(
        lam[:, half:], spectrum, half, top_b, bottom_b, diff_frame, mask_frame, tm_count,
        final=(low, high, first),
    )
    col_block = col_count // tm_count
    outgoing = outgoing.reshape(tm_count, 2, local_count * row_count, col_block)
    arrived = lax.all_to_all(outgoing, "tm", 0, 0, tiled=True)

    step_ids = (
        jnp.arange(tm_count, dtype=jnp.int32)[:, None] * local_count
        + jnp.arange(local_count, dtype=jnp.int32)[None, :]
    ).astype(jnp.float32)
    factor = jnp.exp(step_ids * (-math.log(alpha_wrap) / total_steps)) / math.sqrt(total_steps)
    combined = combine_call(class_weights(tm_count, bit_count), factor, arrived, Q_BLOCK)
    returned = lax.all_to_all(combined, "tm", 0, 0, tiled=True)
    returned = returned.reshape(tm_count, 2, local_count, row_count, col_block)
    return jnp.moveaxis(returned, 0, 3).reshape(2, local_count, row_count, col_count)


def solution(mesh):
    in_specs = (P(None, "tm", "space", None), P("space", None))
    out_specs = P(None, "tm", "space", None)
    return jax.shard_map(
        on_device, mesh=mesh, in_specs=in_specs, out_specs=out_specs, check_vma=False
    )
```

```python
import functools
import math

import jax
import jax.numpy as jnp
import numpy as np
from jax import lax
from jax.experimental import pallas as pl
from jax.experimental.pallas import tpu as pltpu
from jax.sharding import PartitionSpec as P

alpha_wrap = 0.25
step_rate = 0.5
flow_speed = 2.0
sweep_weights = [
    1.0 / (1.0 + 0.7 * math.cos(math.pi * (2 * order + 1) / 6.0)) for order in range(3)
]
Q_BLOCK = 32
F_BLOCK = 16
SWEEP_UNROLL = 4
HALO = 2


def reverse_bits(number, bit_count):
    result = number * 0
    for bit_place in range(bit_count):
        result = result + (number >> bit_place & 1) * (1 << bit_count - 1 - bit_place)
    return result


def shift_parts(freq_ids, total_steps):
    phase_angle = freq_ids.astype(jnp.float32) * (2.0 * math.pi / total_steps)
    root_scale = alpha_wrap ** (1.0 / total_steps)
    return (
        step_rate * (1.0 - root_scale * jnp.cos(phase_angle)),
        step_rate * root_scale * jnp.sin(phase_angle),
    )


def halo_pair(block, axis, dim, width):
    count = lax.axis_size(axis)
    forward = [(i, i + 1) for i in range(count - 1)]
    backward = [(i + 1, i) for i in range(count - 1)]
    size = block.shape[dim]
    top = lax.ppermute(lax.slice_in_dim(block, size - width, size, axis=dim), axis, forward)
    bottom = lax.ppermute(lax.slice_in_dim(block, 0, width, axis=dim), axis, backward)
    return top, bottom


def sweep_kernel(final, lam_ref, rhs_ref, top_ref, bot_ref, diff_ref, mask_ref, *rest):
    if final:
        low_ref, high_ref, prev_ref, o_ref, field = rest
    else:
        (o_ref,) = rest
        field = o_ref
    block = rhs_ref.shape[1]
    count = lam_ref.shape[1]
    cols = rhs_ref.shape[3]
    base = pl.program_id(0) * block
    diff = diff_ref[...]
    diag_base = 4.0 * diff + flow_speed
    keep = mask_ref[...]
    row8 = lax.broadcasted_iota(jnp.int32, (8, cols), 0)
    col = lax.broadcasted_iota(jnp.int32, (16, cols), 1)

    def frame(x, f):
        local = rhs_ref[x, f]
        bv = bot_ref[x, f]
        tv = top_ref[x, f]
        hi = jnp.where(row8 == 0, jnp.broadcast_to(bv[0:1], (8, cols)), 0.0)
        hi = jnp.where(row8 == 1, jnp.broadcast_to(bv[1:2], (8, cols)), hi)
        hi = jnp.where(row8 == 6, jnp.broadcast_to(tv[0:1], (8, cols)), hi)
        hi = jnp.where(row8 == 7, jnp.broadcast_to(tv[1:2], (8, cols)), hi)
        return jnp.concatenate([local, hi], axis=0)

    def around(v):
        north = pltpu.roll(v, 1, 0)
        south = pltpu.roll(v, 15, 0)
        west = jnp.where(col == 0, 0.0, pltpu.roll(v, 1, 1))
        east = jnp.where(col == cols - 1, 0.0, pltpu.roll(v, cols - 1, 1))
        return north, north + south + west + east

    def body(f, carry):
        lam_r = lam_ref[0, base + f]
        lam_i = lam_ref[1, base + f]
        dr = diag_base + lam_r
        inv_mag = 1.0 / (dr * dr + lam_i * lam_i)
        r_re = frame(0, f)
        r_im = frame(1, f)
        g_re = (r_re * dr + r_im * lam_i) * inv_mag
        g_im = (r_im * dr - r_re * lam_i) * inv_mag
        c_re = sweep_weights[0] * g_re
        c_im = sweep_weights[0] * g_im
        for order in (1, 2):
            n_re, b_re = around(c_re)
            n_im, b_im = around(c_im)
            if order == 2:
                n_re, b_re, n_im, b_im = n_re[0:8], b_re[0:8], n_im[0:8], b_im[0:8]
                c_re, c_im, g_re, g_im = c_re[0:8], c_im[0:8], g_re[0:8], g_im[0:8]
                dr, inv_mag, d = dr[0:8], inv_mag[0:8], diff[0:8]
            else:
                d = diff
            weight = sweep_weights[order]
            t_re = d * b_re + flow_speed * n_re
            t_im = d * b_im + flow_speed * n_im
            scaled = weight * inv_mag
            c_re = c_re + weight * (g_re - c_re) + (t_re * dr + t_im * lam_i) * scaled
            c_im = c_im + weight * (g_im - c_im) + (t_im * dr - t_re * lam_i) * scaled
            if order == 1:
                c_re = c_re * keep
                c_im = c_im * keep
        width = field.shape[2]
        for blk in range(field.shape[0]):
            lanes = slice(blk * width, (blk + 1) * width)
            field[blk, pl.ds(pl.multiple_of((base + f) * 8, 8), 8), :] = c_re[0:8, lanes]
            field[blk, pl.ds(pl.multiple_of((count + base + f) * 8, 8), 8), :] = c_im[0:8, lanes]
        return carry

    lax.fori_loop(0, block, body, 0, unroll=SWEEP_UNROLL)

    if not final:
        return

    @pl.when(pl.program_id(0) == pl.num_programs(0) - 1)
    def _():
        low = low_ref[...]
        high = high_ref[...]
        rows_out = o_ref.shape[1] // 8
        for blk in range(o_ref.shape[0]):
            for r in range(8):
                first = prev_ref[blk, pl.ds(r, 2 * count, stride=8), :]
                second = field[blk, pl.ds(r, 2 * count, stride=8), :]
                o_ref[blk, pl.ds(r, rows_out, stride=8), :] = jnp.dot(
                    low, first, precision=lax.Precision.HIGH, preferred_element_type=jnp.float32
                ) + jnp.dot(high, second, precision=lax.Precision.HIGH, preferred_element_type=jnp.float32)


def sweep_call(lam, spectrum, offset, top, bottom, diff_frame, mask_frame, blocks, final=None):
    _, total, rows, cols = spectrum.shape
    count = lam.shape[1]
    block = F_BLOCK
    width = cols // blocks
    skip = offset // block
    big = pl.BlockSpec((2, block, rows, cols), lambda g: (0, g + skip, 0, 0))
    edge = pl.BlockSpec((2, block, HALO, cols), lambda g: (0, g, 0, 0))
    whole = pl.BlockSpec((16, cols), lambda g: (0, 0))
    field_rows = 2 * count * rows
    in_specs = [pl.BlockSpec(memory_space=pltpu.SMEM), big, edge, edge, whole, whole]
    operands = [lam, spectrum, top, bottom, diff_frame, mask_frame]
    scratch = []
    out_rows = field_rows
    if final is not None:
        low, high, prev = final
        half = pl.BlockSpec(low.shape, lambda g: (0, 0))
        in_specs += [half, half, pl.BlockSpec(prev.shape, lambda g: (0, 0, 0))]
        operands += [low, high, prev]
        scratch = [pltpu.VMEM((blocks, field_rows, width), jnp.float32)]
        out_rows = 2 * total * rows
    return pl.pallas_call(
        functools.partial(sweep_kernel, final is not None),
        out_shape=jax.ShapeDtypeStruct((blocks, out_rows, width), jnp.float32),
        grid=(count // block,),
        in_specs=in_specs,
        out_specs=pl.BlockSpec((blocks, out_rows, width), lambda g: (0, 0, 0)),
        scratch_shapes=scratch,
        compiler_params=pltpu.CompilerParams(dimension_semantics=("arbitrary",)),
        cost_estimate=pl.CostEstimate(
            flops=100 * spectrum.size, transcendentals=0, bytes_accessed=4 * spectrum.size
        ),
    )(*operands)


def combine_kernel(weights, fac_ref, a_ref, o_ref):
    block = a_ref.shape[2] // 8
    base = pl.program_id(0) * block
    half = float(np.float32(1.0 / math.sqrt(2.0)))

    def turn(p, eighths):
        re, im = p
        if eighths == 0:
            return p
        if eighths == 2:
            return -im, re
        if eighths == 1:
            return half * (re - im), half * (re + im)
        return -half * (re + im), half * (re - im)

    def body(qi, carry):
        rows = pl.ds(pl.multiple_of(qi * 8, 8), 8)
        x = [(a_ref[s, 0, rows, :], a_ref[s, 1, rows, :]) for s in range(a_ref.shape[0])]
        span = 1
        while span < len(x):
            y = list(x)
            for start in range(0, len(x), 2 * span):
                for j in range(span):
                    u = x[start + j]
                    v = turn(x[start + j + span], j * len(x) // (2 * span))
                    y[start + j] = (u[0] + v[0], u[1] + v[1])
                    y[start + j + span] = (u[0] - v[0], u[1] - v[1])
            x = y
            span *= 2
        for m, (re, im) in enumerate(x):
            scale = fac_ref[m, base + qi]
            o_ref[m, 0, rows, :] = re * scale
            o_ref[m, 1, rows, :] = im * scale
        return carry

    lax.fori_loop(0, block, body, 0, unroll=SWEEP_UNROLL)


def combine_call(weights, factor, arrived, q_block):
    blocks, _, rows, width = arrived.shape
    spec = pl.BlockSpec((blocks, 2, q_block * 8, width), lambda g: (0, 0, g, 0))
    return pl.pallas_call(
        functools.partial(combine_kernel, weights),
        out_shape=jax.ShapeDtypeStruct(arrived.shape, jnp.float32),
        grid=(rows // (q_block * 8),),
        in_specs=[pl.BlockSpec(memory_space=pltpu.SMEM), spec],
        out_specs=spec,
        compiler_params=pltpu.CompilerParams(dimension_semantics=("arbitrary",)),
        cost_estimate=pl.CostEstimate(
            flops=40 * arrived.size, transcendentals=0, bytes_accessed=8 * arrived.size
        ),
    )(factor, arrived)


def class_weights(tm_count, bit_count):
    rows = []
    for m in range(tm_count):
        row = []
        for source in range(tm_count):
            angle = 2.0 * math.pi * ((m * reverse_bits(source, bit_count)) % tm_count) / tm_count
            c, s = math.cos(angle), math.sin(angle)
            c = float(np.float32(0.0 if abs(c) < 1e-9 else c))
            s = float(np.float32(0.0 if abs(s) < 1e-9 else s))
            row.append((c, s))
        rows.append(tuple(row))
    return tuple(rows)


def frames(diffusivity, d_top, d_bot, space_place, space_count):
    rows, cols = diffusivity.shape
    gap = jnp.zeros((16 - rows - 2 * HALO, cols), jnp.float32)
    diff_frame = jnp.concatenate([diffusivity, d_bot, gap, d_top], axis=0)
    row = jnp.arange(16, dtype=jnp.int32)
    keep = (row < rows) | ((row == rows) & (space_place < space_count - 1)) | (
        (row == 15) & (space_place > 0)
    )
    mask_frame = jnp.broadcast_to(keep.astype(jnp.float32)[:, None], (16, cols))
    return diff_frame, mask_frame


def on_device(spectrum, diffusivity):
    local_count = spectrum.shape[1]
    row_count = spectrum.shape[2]
    col_count = spectrum.shape[3]
    tm_count = lax.axis_size("tm")
    space_count = lax.axis_size("space")
    bit_count = tm_count.bit_length() - 1
    total_steps = local_count * tm_count
    tm_place = lax.axis_index("tm")
    space_place = lax.axis_index("space")
    residue = reverse_bits(tm_place, bit_count)
    index_f = jnp.arange(local_count, dtype=jnp.int32)
    freq_ids = index_f * tm_count + residue
    lam = jnp.stack(shift_parts(freq_ids, total_steps))

    half = local_count // 2
    diff_slot = jnp.broadcast_to(diffusivity[None, None], (2, 1, row_count, col_count))
    top_a, bottom_a = halo_pair(jnp.concatenate([spectrum[:, :half], diff_slot], axis=1), "space", 2, HALO)
    top_b, bottom_b = halo_pair(spectrum[:, half:], "space", 2, HALO)
    diff_frame, mask_frame = frames(diffusivity, top_a[0, half], bottom_a[0, half], space_place, space_count)
    grid_angle = (index_f[:, None] * freq_ids[None, :] % total_steps).astype(jnp.float32) * (
        2.0 * math.pi / total_steps
    )
    cosine = jnp.cos(grid_angle)
    sine = jnp.sin(grid_angle)
    table = jnp.concatenate(
        [jnp.concatenate([cosine, -sine], 1), jnp.concatenate([sine, cosine], 1)], 0
    )
    low = jnp.concatenate([table[:, :half], table[:, local_count:local_count + half]], 1)
    high = jnp.concatenate([table[:, half:local_count], table[:, local_count + half:]], 1)
    first = sweep_call(lam[:, :half], spectrum, 0, top_a, bottom_a, diff_frame, mask_frame, tm_count)
    outgoing = sweep_call(
        lam[:, half:], spectrum, half, top_b, bottom_b, diff_frame, mask_frame, tm_count,
        final=(low, high, first),
    )
    col_block = col_count // tm_count
    outgoing = outgoing.reshape(tm_count, 2, local_count * row_count, col_block)
    arrived = lax.all_to_all(outgoing, "tm", 0, 0, tiled=True)

    step_ids = (
        jnp.arange(tm_count, dtype=jnp.int32)[:, None] * local_count
        + jnp.arange(local_count, dtype=jnp.int32)[None, :]
    ).astype(jnp.float32)
    factor = jnp.exp(step_ids * (-math.log(alpha_wrap) / total_steps)) / math.sqrt(total_steps)
    combined = combine_call(class_weights(tm_count, bit_count), factor, arrived, Q_BLOCK)
    returned = lax.all_to_all(combined, "tm", 0, 0, tiled=True)
    returned = returned.reshape(tm_count, 2, local_count, row_count, col_block)
    return jnp.moveaxis(returned, 0, 3).reshape(2, local_count, row_count, col_count)


def solution(mesh):
    in_specs = (P(None, "tm", "space", None), P("space", None))
    out_specs = P(None, "tm", "space", None)
    return jax.shard_map(
        on_device, mesh=mesh, in_specs=in_specs, out_specs=out_specs, check_vma=False
    )
```

```python
import functools
import math

import jax
import jax.numpy as jnp
import numpy as np
from jax import lax
from jax.experimental import pallas as pl
from jax.experimental.pallas import tpu as pltpu
from jax.sharding import PartitionSpec as P

alpha_wrap = 0.25
step_rate = 0.5
flow_speed = 2.0
sweep_weights = [
    1.0 / (1.0 + 0.7 * math.cos(math.pi * (2 * order + 1) / 6.0)) for order in range(3)
]
Q_BLOCK = 32
F_BLOCK = 16
SWEEP_UNROLL = 4
HALO = 2


def reverse_bits(number, bit_count):
    result = number * 0
    for bit_place in range(bit_count):
        result = result + (number >> bit_place & 1) * (1 << bit_count - 1 - bit_place)
    return result


def shift_parts(freq_ids, total_steps):
    phase_angle = freq_ids.astype(jnp.float32) * (2.0 * math.pi / total_steps)
    root_scale = alpha_wrap ** (1.0 / total_steps)
    return (
        step_rate * (1.0 - root_scale * jnp.cos(phase_angle)),
        step_rate * root_scale * jnp.sin(phase_angle),
    )


def halo_pair(block, axis, dim, width):
    count = lax.axis_size(axis)
    forward = [(i, i + 1) for i in range(count - 1)]
    backward = [(i + 1, i) for i in range(count - 1)]
    size = block.shape[dim]
    top = lax.ppermute(lax.slice_in_dim(block, size - width, size, axis=dim), axis, forward)
    bottom = lax.ppermute(lax.slice_in_dim(block, 0, width, axis=dim), axis, backward)
    return top, bottom


def sweep_kernel(final, lam_ref, rhs_ref, top_ref, bot_ref, diff_ref, mask_ref, *rest):
    if final:
        low_ref, prev_ref, o_ref, field = rest
    else:
        (o_ref,) = rest
        field = o_ref
    block = rhs_ref.shape[1]
    count = lam_ref.shape[1]
    cols = rhs_ref.shape[3]
    base = pl.program_id(0) * block
    diff = diff_ref[...]
    diag_base = 4.0 * diff + flow_speed
    keep = mask_ref[...]
    row8 = lax.broadcasted_iota(jnp.int32, (8, cols), 0)
    col = lax.broadcasted_iota(jnp.int32, (16, cols), 1)

    def frame(x, f):
        local = rhs_ref[x, f]
        bv = bot_ref[x, f]
        tv = top_ref[x, f]
        hi = jnp.where(row8 == 0, jnp.broadcast_to(bv[0:1], (8, cols)), 0.0)
        hi = jnp.where(row8 == 1, jnp.broadcast_to(bv[1:2], (8, cols)), hi)
        hi = jnp.where(row8 == 6, jnp.broadcast_to(tv[0:1], (8, cols)), hi)
        hi = jnp.where(row8 == 7, jnp.broadcast_to(tv[1:2], (8, cols)), hi)
        return jnp.concatenate([local, hi], axis=0)

    def around(v):
        north = pltpu.roll(v, 1, 0)
        south = pltpu.roll(v, 15, 0)
        west = jnp.where(col == 0, 0.0, pltpu.roll(v, 1, 1))
        east = jnp.where(col == cols - 1, 0.0, pltpu.roll(v, cols - 1, 1))
        return north, north + south + west + east

    def body(f, carry):
        lam_r = lam_ref[0, base + f]
        lam_i = lam_ref[1, base + f]
        dr = diag_base + lam_r
        inv_mag = 1.0 / (dr * dr + lam_i * lam_i)
        r_re = frame(0, f)
        r_im = frame(1, f)
        g_re = (r_re * dr + r_im * lam_i) * inv_mag
        g_im = (r_im * dr - r_re * lam_i) * inv_mag
        c_re = sweep_weights[0] * g_re
        c_im = sweep_weights[0] * g_im
        for order in (1, 2):
            n_re, b_re = around(c_re)
            n_im, b_im = around(c_im)
            if order == 2:
                n_re, b_re, n_im, b_im = n_re[0:8], b_re[0:8], n_im[0:8], b_im[0:8]
                c_re, c_im, g_re, g_im = c_re[0:8], c_im[0:8], g_re[0:8], g_im[0:8]
                dr, inv_mag, d = dr[0:8], inv_mag[0:8], diff[0:8]
            else:
                d = diff
            weight = sweep_weights[order]
            t_re = d * b_re + flow_speed * n_re
            t_im = d * b_im + flow_speed * n_im
            scaled = weight * inv_mag
            c_re = c_re + weight * (g_re - c_re) + (t_re * dr + t_im * lam_i) * scaled
            c_im = c_im + weight * (g_im - c_im) + (t_im * dr - t_re * lam_i) * scaled
            if order == 1:
                c_re = c_re * keep
                c_im = c_im * keep
        width = field.shape[2]
        for blk in range(field.shape[0]):
            lanes = slice(blk * width, (blk + 1) * width)
            field[blk, pl.ds(pl.multiple_of((base + f) * 8, 8), 8), :] = c_re[0:8, lanes]
            field[blk, pl.ds(pl.multiple_of((count + base + f) * 8, 8), 8), :] = c_im[0:8, lanes]
        return carry

    lax.fori_loop(0, block, body, 0, unroll=SWEEP_UNROLL)

    if not final:
        return

    @pl.when(pl.program_id(0) == pl.num_programs(0) - 1)
    def _():
        table = low_ref[...]
        rows_out = o_ref.shape[1] // 8
        for blk in range(o_ref.shape[0]):
            for r in range(8):
                first = prev_ref[blk, pl.ds(r, 2 * count, stride=8), :]
                second = field[blk, pl.ds(r, 2 * count, stride=8), :]
                o_ref[blk, pl.ds(r, rows_out, stride=8), :] = jnp.dot(
                    table, jnp.concatenate([first, second], axis=0),
                    precision=lax.Precision.HIGH, preferred_element_type=jnp.float32,
                )


def sweep_call(lam, spectrum, offset, top, bottom, diff_frame, mask_frame, blocks, final=None):
    _, total, rows, cols = spectrum.shape
    count = lam.shape[1]
    block = F_BLOCK
    width = cols // blocks
    skip = offset // block
    big = pl.BlockSpec((2, block, rows, cols), lambda g: (0, g + skip, 0, 0))
    edge = pl.BlockSpec((2, block, HALO, cols), lambda g: (0, g, 0, 0))
    whole = pl.BlockSpec((16, cols), lambda g: (0, 0))
    field_rows = 2 * count * rows
    in_specs = [pl.BlockSpec(memory_space=pltpu.SMEM), big, edge, edge, whole, whole]
    operands = [lam, spectrum, top, bottom, diff_frame, mask_frame]
    scratch = []
    out_rows = field_rows
    if final is not None:
        table, prev = final
        in_specs += [pl.BlockSpec(table.shape, lambda g: (0, 0)), pl.BlockSpec(prev.shape, lambda g: (0, 0, 0))]
        operands += [table, prev]
        scratch = [pltpu.VMEM((blocks, field_rows, width), jnp.float32)]
        out_rows = 2 * total * rows
    return pl.pallas_call(
        functools.partial(sweep_kernel, final is not None),
        out_shape=jax.ShapeDtypeStruct((blocks, out_rows, width), jnp.float32),
        grid=(count // block,),
        in_specs=in_specs,
        out_specs=pl.BlockSpec((blocks, out_rows, width), lambda g: (0, 0, 0)),
        scratch_shapes=scratch,
        compiler_params=pltpu.CompilerParams(dimension_semantics=("arbitrary",)),
        cost_estimate=pl.CostEstimate(
            flops=100 * spectrum.size, transcendentals=0, bytes_accessed=4 * spectrum.size
        ),
    )(*operands)


def combine_kernel(weights, fac_ref, a_ref, o_ref):
    block = a_ref.shape[2] // 8
    base = pl.program_id(0) * block
    half = float(np.float32(1.0 / math.sqrt(2.0)))

    def turn(p, eighths):
        re, im = p
        if eighths == 0:
            return p
        if eighths == 2:
            return -im, re
        if eighths == 1:
            return half * (re - im), half * (re + im)
        return -half * (re + im), half * (re - im)

    def body(qi, carry):
        rows = pl.ds(pl.multiple_of(qi * 8, 8), 8)
        x = [(a_ref[s, 0, rows, :], a_ref[s, 1, rows, :]) for s in range(a_ref.shape[0])]
        span = 1
        while span < len(x):
            y = list(x)
            for start in range(0, len(x), 2 * span):
                for j in range(span):
                    u = x[start + j]
                    v = turn(x[start + j + span], j * len(x) // (2 * span))
                    y[start + j] = (u[0] + v[0], u[1] + v[1])
                    y[start + j + span] = (u[0] - v[0], u[1] - v[1])
            x = y
            span *= 2
        for m, (re, im) in enumerate(x):
            scale = fac_ref[m, base + qi]
            o_ref[m, 0, rows, :] = re * scale
            o_ref[m, 1, rows, :] = im * scale
        return carry

    lax.fori_loop(0, block, body, 0, unroll=SWEEP_UNROLL)


def combine_call(weights, factor, arrived, q_block):
    blocks, _, rows, width = arrived.shape
    spec = pl.BlockSpec((blocks, 2, q_block * 8, width), lambda g: (0, 0, g, 0))
    return pl.pallas_call(
        functools.partial(combine_kernel, weights),
        out_shape=jax.ShapeDtypeStruct(arrived.shape, jnp.float32),
        grid=(rows // (q_block * 8),),
        in_specs=[pl.BlockSpec(memory_space=pltpu.SMEM), spec],
        out_specs=spec,
        compiler_params=pltpu.CompilerParams(dimension_semantics=("arbitrary",)),
        cost_estimate=pl.CostEstimate(
            flops=40 * arrived.size, transcendentals=0, bytes_accessed=8 * arrived.size
        ),
    )(factor, arrived)


def class_weights(tm_count, bit_count):
    rows = []
    for m in range(tm_count):
        row = []
        for source in range(tm_count):
            angle = 2.0 * math.pi * ((m * reverse_bits(source, bit_count)) % tm_count) / tm_count
            c, s = math.cos(angle), math.sin(angle)
            c = float(np.float32(0.0 if abs(c) < 1e-9 else c))
            s = float(np.float32(0.0 if abs(s) < 1e-9 else s))
            row.append((c, s))
        rows.append(tuple(row))
    return tuple(rows)


def frames(diffusivity, d_top, d_bot, space_place, space_count):
    rows, cols = diffusivity.shape
    gap = jnp.zeros((16 - rows - 2 * HALO, cols), jnp.float32)
    diff_frame = jnp.concatenate([diffusivity, d_bot, gap, d_top], axis=0)
    row = jnp.arange(16, dtype=jnp.int32)
    keep = (row < rows) | ((row == rows) & (space_place < space_count - 1)) | (
        (row == 15) & (space_place > 0)
    )
    mask_frame = jnp.broadcast_to(keep.astype(jnp.float32)[:, None], (16, cols))
    return diff_frame, mask_frame


def on_device(spectrum, diffusivity):
    local_count = spectrum.shape[1]
    row_count = spectrum.shape[2]
    col_count = spectrum.shape[3]
    tm_count = lax.axis_size("tm")
    space_count = lax.axis_size("space")
    bit_count = tm_count.bit_length() - 1
    total_steps = local_count * tm_count
    tm_place = lax.axis_index("tm")
    space_place = lax.axis_index("space")
    residue = reverse_bits(tm_place, bit_count)
    index_f = jnp.arange(local_count, dtype=jnp.int32)
    freq_ids = index_f * tm_count + residue
    lam = jnp.stack(shift_parts(freq_ids, total_steps))

    half = local_count // 2
    diff_slot = jnp.broadcast_to(diffusivity[None, None], (2, 1, row_count, col_count))
    top_a, bottom_a = halo_pair(jnp.concatenate([spectrum[:, :half], diff_slot], axis=1), "space", 2, HALO)
    top_b, bottom_b = halo_pair(spectrum[:, half:], "space", 2, HALO)
    diff_frame, mask_frame = frames(diffusivity, top_a[0, half], bottom_a[0, half], space_place, space_count)
    grid_angle = (index_f[:, None] * freq_ids[None, :] % total_steps).astype(jnp.float32) * (
        2.0 * math.pi / total_steps
    )
    cosine = jnp.cos(grid_angle)
    sine = jnp.sin(grid_angle)
    table = jnp.concatenate(
        [jnp.concatenate([cosine, -sine], 1), jnp.concatenate([sine, cosine], 1)], 0
    )
    low = jnp.concatenate([table[:, :half], table[:, local_count:local_count + half]], 1)
    high = jnp.concatenate([table[:, half:local_count], table[:, local_count + half:]], 1)
    first = sweep_call(lam[:, :half], spectrum, 0, top_a, bottom_a, diff_frame, mask_frame, tm_count)
    outgoing = sweep_call(
        lam[:, half:], spectrum, half, top_b, bottom_b, diff_frame, mask_frame, tm_count,
        final=(jnp.concatenate([low, high], 1), first),
    )
    col_block = col_count // tm_count
    outgoing = outgoing.reshape(tm_count, 2, local_count * row_count, col_block)
    arrived = lax.all_to_all(outgoing, "tm", 0, 0, tiled=True)

    step_ids = (
        jnp.arange(tm_count, dtype=jnp.int32)[:, None] * local_count
        + jnp.arange(local_count, dtype=jnp.int32)[None, :]
    ).astype(jnp.float32)
    factor = jnp.exp(step_ids * (-math.log(alpha_wrap) / total_steps)) / math.sqrt(total_steps)
    combined = combine_call(class_weights(tm_count, bit_count), factor, arrived, Q_BLOCK)
    returned = lax.all_to_all(combined, "tm", 0, 0, tiled=True)
    returned = returned.reshape(tm_count, 2, local_count, row_count, col_block)
    return jnp.moveaxis(returned, 0, 3).reshape(2, local_count, row_count, col_count)


def solution(mesh):
    in_specs = (P(None, "tm", "space", None), P("space", None))
    out_specs = P(None, "tm", "space", None)
    return jax.shard_map(
        on_device, mesh=mesh, in_specs=in_specs, out_specs=out_specs, check_vma=False
    )
```

```python
import functools
import math

import jax
import jax.numpy as jnp
import numpy as np
from jax import lax
from jax.experimental import pallas as pl
from jax.experimental.pallas import tpu as pltpu
from jax.sharding import PartitionSpec as P

alpha_wrap = 0.25
step_rate = 0.5
flow_speed = 2.0
sweep_weights = [
    1.0 / (1.0 + 0.7 * math.cos(math.pi * (2 * order + 1) / 6.0)) for order in range(3)
]
Q_BLOCK = 64
F_BLOCK = 16
SWEEP_UNROLL = 4
HALO = 2


def reverse_bits(number, bit_count):
    result = number * 0
    for bit_place in range(bit_count):
        result = result + (number >> bit_place & 1) * (1 << bit_count - 1 - bit_place)
    return result


def shift_parts(freq_ids, total_steps):
    phase_angle = freq_ids.astype(jnp.float32) * (2.0 * math.pi / total_steps)
    root_scale = alpha_wrap ** (1.0 / total_steps)
    return (
        step_rate * (1.0 - root_scale * jnp.cos(phase_angle)),
        step_rate * root_scale * jnp.sin(phase_angle),
    )


def halo_pair(block, axis, dim, width):
    count = lax.axis_size(axis)
    forward = [(i, i + 1) for i in range(count - 1)]
    backward = [(i + 1, i) for i in range(count - 1)]
    size = block.shape[dim]
    top = lax.ppermute(lax.slice_in_dim(block, size - width, size, axis=dim), axis, forward)
    bottom = lax.ppermute(lax.slice_in_dim(block, 0, width, axis=dim), axis, backward)
    return top, bottom


def sweep_kernel(final, lam_ref, rhs_ref, top_ref, bot_ref, diff_ref, mask_ref, *rest):
    if final:
        low_ref, prev_ref, o_ref, field = rest
    else:
        (o_ref,) = rest
        field = o_ref
    block = rhs_ref.shape[1]
    count = lam_ref.shape[1]
    cols = rhs_ref.shape[3]
    base = pl.program_id(0) * block
    diff = diff_ref[...]
    diag_base = 4.0 * diff + flow_speed
    keep = mask_ref[...]
    row8 = lax.broadcasted_iota(jnp.int32, (8, cols), 0)
    col = lax.broadcasted_iota(jnp.int32, (16, cols), 1)

    def frame(x, f):
        local = rhs_ref[x, f]
        bv = bot_ref[x, f]
        tv = top_ref[x, f]
        hi = jnp.where(row8 == 0, jnp.broadcast_to(bv[0:1], (8, cols)), 0.0)
        hi = jnp.where(row8 == 1, jnp.broadcast_to(bv[1:2], (8, cols)), hi)
        hi = jnp.where(row8 == 6, jnp.broadcast_to(tv[0:1], (8, cols)), hi)
        hi = jnp.where(row8 == 7, jnp.broadcast_to(tv[1:2], (8, cols)), hi)
        return jnp.concatenate([local, hi], axis=0)

    def around(v):
        north = pltpu.roll(v, 1, 0)
        south = pltpu.roll(v, 15, 0)
        west = jnp.where(col == 0, 0.0, pltpu.roll(v, 1, 1))
        east = jnp.where(col == cols - 1, 0.0, pltpu.roll(v, cols - 1, 1))
        return north, north + south + west + east

    def body(f, carry):
        lam_r = lam_ref[0, base + f]
        lam_i = lam_ref[1, base + f]
        dr = diag_base + lam_r
        inv_mag = 1.0 / (dr * dr + lam_i * lam_i)
        r_re = frame(0, f)
        r_im = frame(1, f)
        g_re = (r_re * dr + r_im * lam_i) * inv_mag
        g_im = (r_im * dr - r_re * lam_i) * inv_mag
        c_re = sweep_weights[0] * g_re
        c_im = sweep_weights[0] * g_im
        for order in (1, 2):
            n_re, b_re = around(c_re)
            n_im, b_im = around(c_im)
            if order == 2:
                n_re, b_re, n_im, b_im = n_re[0:8], b_re[0:8], n_im[0:8], b_im[0:8]
                c_re, c_im, g_re, g_im = c_re[0:8], c_im[0:8], g_re[0:8], g_im[0:8]
                dr, inv_mag, d = dr[0:8], inv_mag[0:8], diff[0:8]
            else:
                d = diff
            weight = sweep_weights[order]
            t_re = d * b_re + flow_speed * n_re
            t_im = d * b_im + flow_speed * n_im
            scaled = weight * inv_mag
            c_re = c_re + weight * (g_re - c_re) + (t_re * dr + t_im * lam_i) * scaled
            c_im = c_im + weight * (g_im - c_im) + (t_im * dr - t_re * lam_i) * scaled
            if order == 1:
                c_re = c_re * keep
                c_im = c_im * keep
        width = field.shape[2]
        for blk in range(field.shape[0]):
            lanes = slice(blk * width, (blk + 1) * width)
            field[blk, pl.ds(pl.multiple_of((base + f) * 8, 8), 8), :] = c_re[0:8, lanes]
            field[blk, pl.ds(pl.multiple_of((count + base + f) * 8, 8), 8), :] = c_im[0:8, lanes]
        return carry

    lax.fori_loop(0, block, body, 0, unroll=SWEEP_UNROLL)

    if not final:
        return

    @pl.when(pl.program_id(0) == pl.num_programs(0) - 1)
    def _():
        table = low_ref[...]
        rows_out = o_ref.shape[1] // 8
        for blk in range(o_ref.shape[0]):
            for r in range(8):
                first = prev_ref[blk, pl.ds(r, 2 * count, stride=8), :]
                second = field[blk, pl.ds(r, 2 * count, stride=8), :]
                o_ref[blk, pl.ds(r, rows_out, stride=8), :] = jnp.dot(
                    table, jnp.concatenate([first, second], axis=0),
                    precision=lax.Precision.HIGH, preferred_element_type=jnp.float32,
                )


def sweep_call(lam, spectrum, offset, top, bottom, diff_frame, mask_frame, blocks, final=None):
    _, total, rows, cols = spectrum.shape
    count = lam.shape[1]
    block = F_BLOCK
    width = cols // blocks
    skip = offset // block
    big = pl.BlockSpec((2, block, rows, cols), lambda g: (0, g + skip, 0, 0))
    edge = pl.BlockSpec((2, block, HALO, cols), lambda g: (0, g, 0, 0))
    whole = pl.BlockSpec((16, cols), lambda g: (0, 0))
    field_rows = 2 * count * rows
    in_specs = [pl.BlockSpec(memory_space=pltpu.SMEM), big, edge, edge, whole, whole]
    operands = [lam, spectrum, top, bottom, diff_frame, mask_frame]
    scratch = []
    out_rows = field_rows
    if final is not None:
        table, prev = final
        in_specs += [pl.BlockSpec(table.shape, lambda g: (0, 0)), pl.BlockSpec(prev.shape, lambda g: (0, 0, 0))]
        operands += [table, prev]
        scratch = [pltpu.VMEM((blocks, field_rows, width), jnp.float32)]
        out_rows = 2 * total * rows
    return pl.pallas_call(
        functools.partial(sweep_kernel, final is not None),
        out_shape=jax.ShapeDtypeStruct((blocks, out_rows, width), jnp.float32),
        grid=(count // block,),
        in_specs=in_specs,
        out_specs=pl.BlockSpec((blocks, out_rows, width), lambda g: (0, 0, 0)),
        scratch_shapes=scratch,
        compiler_params=pltpu.CompilerParams(dimension_semantics=("arbitrary",)),
        cost_estimate=pl.CostEstimate(
            flops=100 * spectrum.size, transcendentals=0, bytes_accessed=4 * spectrum.size
        ),
    )(*operands)


def combine_kernel(weights, fac_ref, a_ref, o_ref):
    block = a_ref.shape[2] // 8
    base = pl.program_id(0) * block
    half = float(np.float32(1.0 / math.sqrt(2.0)))

    def turn(p, eighths):
        re, im = p
        if eighths == 0:
            return p
        if eighths == 2:
            return -im, re
        if eighths == 1:
            return half * (re - im), half * (re + im)
        return -half * (re + im), half * (re - im)

    def body(qi, carry):
        rows = pl.ds(pl.multiple_of(qi * 8, 8), 8)
        x = [(a_ref[s, 0, rows, :], a_ref[s, 1, rows, :]) for s in range(a_ref.shape[0])]
        span = 1
        while span < len(x):
            y = list(x)
            for start in range(0, len(x), 2 * span):
                for j in range(span):
                    u = x[start + j]
                    v = turn(x[start + j + span], j * len(x) // (2 * span))
                    y[start + j] = (u[0] + v[0], u[1] + v[1])
                    y[start + j + span] = (u[0] - v[0], u[1] - v[1])
            x = y
            span *= 2
        for m, (re, im) in enumerate(x):
            scale = fac_ref[m, base + qi]
            o_ref[m, 0, rows, :] = re * scale
            o_ref[m, 1, rows, :] = im * scale
        return carry

    lax.fori_loop(0, block, body, 0, unroll=SWEEP_UNROLL)


def combine_call(weights, factor, arrived, q_block):
    blocks, _, rows, width = arrived.shape
    spec = pl.BlockSpec((blocks, 2, q_block * 8, width), lambda g: (0, 0, g, 0))
    return pl.pallas_call(
        functools.partial(combine_kernel, weights),
        out_shape=jax.ShapeDtypeStruct(arrived.shape, jnp.float32),
        grid=(rows // (q_block * 8),),
        in_specs=[pl.BlockSpec(memory_space=pltpu.SMEM), spec],
        out_specs=spec,
        compiler_params=pltpu.CompilerParams(dimension_semantics=("arbitrary",)),
        cost_estimate=pl.CostEstimate(
            flops=40 * arrived.size, transcendentals=0, bytes_accessed=8 * arrived.size
        ),
    )(factor, arrived)


def class_weights(tm_count, bit_count):
    rows = []
    for m in range(tm_count):
        row = []
        for source in range(tm_count):
            angle = 2.0 * math.pi * ((m * reverse_bits(source, bit_count)) % tm_count) / tm_count
            c, s = math.cos(angle), math.sin(angle)
            c = float(np.float32(0.0 if abs(c) < 1e-9 else c))
            s = float(np.float32(0.0 if abs(s) < 1e-9 else s))
            row.append((c, s))
        rows.append(tuple(row))
    return tuple(rows)


def frames(diffusivity, d_top, d_bot, space_place, space_count):
    rows, cols = diffusivity.shape
    gap = jnp.zeros((16 - rows - 2 * HALO, cols), jnp.float32)
    diff_frame = jnp.concatenate([diffusivity, d_bot, gap, d_top], axis=0)
    row = jnp.arange(16, dtype=jnp.int32)
    keep = (row < rows) | ((row == rows) & (space_place < space_count - 1)) | (
        (row == 15) & (space_place > 0)
    )
    mask_frame = jnp.broadcast_to(keep.astype(jnp.float32)[:, None], (16, cols))
    return diff_frame, mask_frame


def on_device(spectrum, diffusivity):
    local_count = spectrum.shape[1]
    row_count = spectrum.shape[2]
    col_count = spectrum.shape[3]
    tm_count = lax.axis_size("tm")
    space_count = lax.axis_size("space")
    bit_count = tm_count.bit_length() - 1
    total_steps = local_count * tm_count
    tm_place = lax.axis_index("tm")
    space_place = lax.axis_index("space")
    residue = reverse_bits(tm_place, bit_count)
    index_f = jnp.arange(local_count, dtype=jnp.int32)
    freq_ids = index_f * tm_count + residue
    lam = jnp.stack(shift_parts(freq_ids, total_steps))

    half = local_count // 2
    diff_slot = jnp.broadcast_to(diffusivity[None, None], (2, 1, row_count, col_count))
    top_a, bottom_a = halo_pair(jnp.concatenate([spectrum[:, :half], diff_slot], axis=1), "space", 2, HALO)
    top_b, bottom_b = halo_pair(spectrum[:, half:], "space", 2, HALO)
    diff_frame, mask_frame = frames(diffusivity, top_a[0, half], bottom_a[0, half], space_place, space_count)
    grid_angle = (index_f[:, None] * freq_ids[None, :] % total_steps).astype(jnp.float32) * (
        2.0 * math.pi / total_steps
    )
    cosine = jnp.cos(grid_angle)
    sine = jnp.sin(grid_angle)
    table = jnp.concatenate(
        [jnp.concatenate([cosine, -sine], 1), jnp.concatenate([sine, cosine], 1)], 0
    )
    low = jnp.concatenate([table[:, :half], table[:, local_count:local_count + half]], 1)
    high = jnp.concatenate([table[:, half:local_count], table[:, local_count + half:]], 1)
    first = sweep_call(lam[:, :half], spectrum, 0, top_a, bottom_a, diff_frame, mask_frame, tm_count)
    outgoing = sweep_call(
        lam[:, half:], spectrum, half, top_b, bottom_b, diff_frame, mask_frame, tm_count,
        final=(jnp.concatenate([low, high], 1), first),
    )
    col_block = col_count // tm_count
    outgoing = outgoing.reshape(tm_count, 2, local_count * row_count, col_block)
    arrived = lax.all_to_all(outgoing, "tm", 0, 0, tiled=True)

    step_ids = (
        jnp.arange(tm_count, dtype=jnp.int32)[:, None] * local_count
        + jnp.arange(local_count, dtype=jnp.int32)[None, :]
    ).astype(jnp.float32)
    factor = jnp.exp(step_ids * (-math.log(alpha_wrap) / total_steps)) / math.sqrt(total_steps)
    combined = combine_call(class_weights(tm_count, bit_count), factor, arrived, Q_BLOCK)
    returned = lax.all_to_all(combined, "tm", 0, 0, tiled=True)
    returned = returned.reshape(tm_count, 2, local_count, row_count, col_block)
    return jnp.moveaxis(returned, 0, 3).reshape(2, local_count, row_count, col_count)


def solution(mesh):
    in_specs = (P(None, "tm", "space", None), P("space", None))
    out_specs = P(None, "tm", "space", None)
    return jax.shard_map(
        on_device, mesh=mesh, in_specs=in_specs, out_specs=out_specs, check_vma=False
    )
```

```python
import functools
import math

import jax
import jax.numpy as jnp
import numpy as np
from jax import lax
from jax.experimental import pallas as pl
from jax.experimental.pallas import tpu as pltpu
from jax.sharding import PartitionSpec as P

alpha_wrap = 0.25
step_rate = 0.5
flow_speed = 2.0
sweep_weights = [
    1.0 / (1.0 + 0.7 * math.cos(math.pi * (2 * order + 1) / 6.0)) for order in range(3)
]
Q_BLOCK = 32
F_BLOCK = 32
SWEEP_UNROLL = 4
HALO = 2


def reverse_bits(number, bit_count):
    result = number * 0
    for bit_place in range(bit_count):
        result = result + (number >> bit_place & 1) * (1 << bit_count - 1 - bit_place)
    return result


def shift_parts(freq_ids, total_steps):
    phase_angle = freq_ids.astype(jnp.float32) * (2.0 * math.pi / total_steps)
    root_scale = alpha_wrap ** (1.0 / total_steps)
    return (
        step_rate * (1.0 - root_scale * jnp.cos(phase_angle)),
        step_rate * root_scale * jnp.sin(phase_angle),
    )


def halo_pair(block, axis, dim, width):
    count = lax.axis_size(axis)
    forward = [(i, i + 1) for i in range(count - 1)]
    backward = [(i + 1, i) for i in range(count - 1)]
    size = block.shape[dim]
    top = lax.ppermute(lax.slice_in_dim(block, size - width, size, axis=dim), axis, forward)
    bottom = lax.ppermute(lax.slice_in_dim(block, 0, width, axis=dim), axis, backward)
    return top, bottom


def sweep_kernel(final, lam_ref, rhs_ref, top_ref, bot_ref, diff_ref, mask_ref, *rest):
    if final:
        low_ref, prev_ref, o_ref, field = rest
    else:
        (o_ref,) = rest
        field = o_ref
    block = rhs_ref.shape[1]
    count = lam_ref.shape[1]
    cols = rhs_ref.shape[3]
    base = pl.program_id(0) * block
    diff = diff_ref[...]
    diag_base = 4.0 * diff + flow_speed
    keep = mask_ref[...]
    row8 = lax.broadcasted_iota(jnp.int32, (8, cols), 0)
    col = lax.broadcasted_iota(jnp.int32, (16, cols), 1)

    def frame(x, f):
        local = rhs_ref[x, f]
        bv = bot_ref[x, f]
        tv = top_ref[x, f]
        hi = jnp.where(row8 == 0, jnp.broadcast_to(bv[0:1], (8, cols)), 0.0)
        hi = jnp.where(row8 == 1, jnp.broadcast_to(bv[1:2], (8, cols)), hi)
        hi = jnp.where(row8 == 6, jnp.broadcast_to(tv[0:1], (8, cols)), hi)
        hi = jnp.where(row8 == 7, jnp.broadcast_to(tv[1:2], (8, cols)), hi)
        return jnp.concatenate([local, hi], axis=0)

    def around(v):
        north = pltpu.roll(v, 1, 0)
        south = pltpu.roll(v, 15, 0)
        west = jnp.where(col == 0, 0.0, pltpu.roll(v, 1, 1))
        east = jnp.where(col == cols - 1, 0.0, pltpu.roll(v, cols - 1, 1))
        return north, north + south + west + east

    def body(f, carry):
        lam_r = lam_ref[0, base + f]
        lam_i = lam_ref[1, base + f]
        dr = diag_base + lam_r
        inv_mag = 1.0 / (dr * dr + lam_i * lam_i)
        r_re = frame(0, f)
        r_im = frame(1, f)
        g_re = (r_re * dr + r_im * lam_i) * inv_mag
        g_im = (r_im * dr - r_re * lam_i) * inv_mag
        c_re = sweep_weights[0] * g_re
        c_im = sweep_weights[0] * g_im
        for order in (1, 2):
            n_re, b_re = around(c_re)
            n_im, b_im = around(c_im)
            if order == 2:
                n_re, b_re, n_im, b_im = n_re[0:8], b_re[0:8], n_im[0:8], b_im[0:8]
                c_re, c_im, g_re, g_im = c_re[0:8], c_im[0:8], g_re[0:8], g_im[0:8]
                dr, inv_mag, d = dr[0:8], inv_mag[0:8], diff[0:8]
            else:
                d = diff
            weight = sweep_weights[order]
            t_re = d * b_re + flow_speed * n_re
            t_im = d * b_im + flow_speed * n_im
            scaled = weight * inv_mag
            c_re = c_re + weight * (g_re - c_re) + (t_re * dr + t_im * lam_i) * scaled
            c_im = c_im + weight * (g_im - c_im) + (t_im * dr - t_re * lam_i) * scaled
            if order == 1:
                c_re = c_re * keep
                c_im = c_im * keep
        width = field.shape[2]
        for blk in range(field.shape[0]):
            lanes = slice(blk * width, (blk + 1) * width)
            field[blk, pl.ds(pl.multiple_of((base + f) * 8, 8), 8), :] = c_re[0:8, lanes]
            field[blk, pl.ds(pl.multiple_of((count + base + f) * 8, 8), 8), :] = c_im[0:8, lanes]
        return carry

    lax.fori_loop(0, block, body, 0, unroll=SWEEP_UNROLL)

    if not final:
        return

    @pl.when(pl.program_id(0) == pl.num_programs(0) - 1)
    def _():
        table = low_ref[...]
        rows_out = o_ref.shape[1] // 8
        for blk in range(o_ref.shape[0]):
            for r in range(8):
                first = prev_ref[blk, pl.ds(r, 2 * count, stride=8), :]
                second = field[blk, pl.ds(r, 2 * count, stride=8), :]
                o_ref[blk, pl.ds(r, rows_out, stride=8), :] = jnp.dot(
                    table, jnp.concatenate([first, second], axis=0),
                    precision=lax.Precision.HIGH, preferred_element_type=jnp.float32,
                )


def sweep_call(lam, spectrum, offset, top, bottom, diff_frame, mask_frame, blocks, final=None):
    _, total, rows, cols = spectrum.shape
    count = lam.shape[1]
    block = F_BLOCK
    width = cols // blocks
    skip = offset // block
    big = pl.BlockSpec((2, block, rows, cols), lambda g: (0, g + skip, 0, 0))
    edge = pl.BlockSpec((2, block, HALO, cols), lambda g: (0, g, 0, 0))
    whole = pl.BlockSpec((16, cols), lambda g: (0, 0))
    field_rows = 2 * count * rows
    in_specs = [pl.BlockSpec(memory_space=pltpu.SMEM), big, edge, edge, whole, whole]
    operands = [lam, spectrum, top, bottom, diff_frame, mask_frame]
    scratch = []
    out_rows = field_rows
    if final is not None:
        table, prev = final
        in_specs += [pl.BlockSpec(table.shape, lambda g: (0, 0)), pl.BlockSpec(prev.shape, lambda g: (0, 0, 0))]
        operands += [table, prev]
        scratch = [pltpu.VMEM((blocks, field_rows, width), jnp.float32)]
        out_rows = 2 * total * rows
    return pl.pallas_call(
        functools.partial(sweep_kernel, final is not None),
        out_shape=jax.ShapeDtypeStruct((blocks, out_rows, width), jnp.float32),
        grid=(count // block,),
        in_specs=in_specs,
        out_specs=pl.BlockSpec((blocks, out_rows, width), lambda g: (0, 0, 0)),
        scratch_shapes=scratch,
        compiler_params=pltpu.CompilerParams(dimension_semantics=("arbitrary",)),
        cost_estimate=pl.CostEstimate(
            flops=100 * spectrum.size, transcendentals=0, bytes_accessed=4 * spectrum.size
        ),
    )(*operands)


def combine_kernel(weights, fac_ref, a_ref, o_ref):
    block = a_ref.shape[2] // 8
    base = pl.program_id(0) * block
    half = float(np.float32(1.0 / math.sqrt(2.0)))

    def turn(p, eighths):
        re, im = p
        if eighths == 0:
            return p
        if eighths == 2:
            return -im, re
        if eighths == 1:
            return half * (re - im), half * (re + im)
        return -half * (re + im), half * (re - im)

    def body(qi, carry):
        rows = pl.ds(pl.multiple_of(qi * 8, 8), 8)
        x = [(a_ref[s, 0, rows, :], a_ref[s, 1, rows, :]) for s in range(a_ref.shape[0])]
        span = 1
        while span < len(x):
            y = list(x)
            for start in range(0, len(x), 2 * span):
                for j in range(span):
                    u = x[start + j]
                    v = turn(x[start + j + span], j * len(x) // (2 * span))
                    y[start + j] = (u[0] + v[0], u[1] + v[1])
                    y[start + j + span] = (u[0] - v[0], u[1] - v[1])
            x = y
            span *= 2
        for m, (re, im) in enumerate(x):
            scale = fac_ref[m, base + qi]
            o_ref[m, 0, rows, :] = re * scale
            o_ref[m, 1, rows, :] = im * scale
        return carry

    lax.fori_loop(0, block, body, 0, unroll=SWEEP_UNROLL)


def combine_call(weights, factor, arrived, q_block):
    blocks, _, rows, width = arrived.shape
    spec = pl.BlockSpec((blocks, 2, q_block * 8, width), lambda g: (0, 0, g, 0))
    return pl.pallas_call(
        functools.partial(combine_kernel, weights),
        out_shape=jax.ShapeDtypeStruct(arrived.shape, jnp.float32),
        grid=(rows // (q_block * 8),),
        in_specs=[pl.BlockSpec(memory_space=pltpu.SMEM), spec],
        out_specs=spec,
        compiler_params=pltpu.CompilerParams(dimension_semantics=("arbitrary",)),
        cost_estimate=pl.CostEstimate(
            flops=40 * arrived.size, transcendentals=0, bytes_accessed=8 * arrived.size
        ),
    )(factor, arrived)


def class_weights(tm_count, bit_count):
    rows = []
    for m in range(tm_count):
        row = []
        for source in range(tm_count):
            angle = 2.0 * math.pi * ((m * reverse_bits(source, bit_count)) % tm_count) / tm_count
            c, s = math.cos(angle), math.sin(angle)
            c = float(np.float32(0.0 if abs(c) < 1e-9 else c))
            s = float(np.float32(0.0 if abs(s) < 1e-9 else s))
            row.append((c, s))
        rows.append(tuple(row))
    return tuple(rows)


def frames(diffusivity, d_top, d_bot, space_place, space_count):
    rows, cols = diffusivity.shape
    gap = jnp.zeros((16 - rows - 2 * HALO, cols), jnp.float32)
    diff_frame = jnp.concatenate([diffusivity, d_bot, gap, d_top], axis=0)
    row = jnp.arange(16, dtype=jnp.int32)
    keep = (row < rows) | ((row == rows) & (space_place < space_count - 1)) | (
        (row == 15) & (space_place > 0)
    )
    mask_frame = jnp.broadcast_to(keep.astype(jnp.float32)[:, None], (16, cols))
    return diff_frame, mask_frame


def on_device(spectrum, diffusivity):
    local_count = spectrum.shape[1]
    row_count = spectrum.shape[2]
    col_count = spectrum.shape[3]
    tm_count = lax.axis_size("tm")
    space_count = lax.axis_size("space")
    bit_count = tm_count.bit_length() - 1
    total_steps = local_count * tm_count
    tm_place = lax.axis_index("tm")
    space_place = lax.axis_index("space")
    residue = reverse_bits(tm_place, bit_count)
    index_f = jnp.arange(local_count, dtype=jnp.int32)
    freq_ids = index_f * tm_count + residue
    lam = jnp.stack(shift_parts(freq_ids, total_steps))

    half = local_count // 2
    diff_slot = jnp.broadcast_to(diffusivity[None, None], (2, 1, row_count, col_count))
    top_a, bottom_a = halo_pair(jnp.concatenate([spectrum[:, :half], diff_slot], axis=1), "space", 2, HALO)
    top_b, bottom_b = halo_pair(spectrum[:, half:], "space", 2, HALO)
    diff_frame, mask_frame = frames(diffusivity, top_a[0, half], bottom_a[0, half], space_place, space_count)
    grid_angle = (index_f[:, None] * freq_ids[None, :] % total_steps).astype(jnp.float32) * (
        2.0 * math.pi / total_steps
    )
    cosine = jnp.cos(grid_angle)
    sine = jnp.sin(grid_angle)
    table = jnp.concatenate(
        [jnp.concatenate([cosine, -sine], 1), jnp.concatenate([sine, cosine], 1)], 0
    )
    low = jnp.concatenate([table[:, :half], table[:, local_count:local_count + half]], 1)
    high = jnp.concatenate([table[:, half:local_count], table[:, local_count + half:]], 1)
    first = sweep_call(lam[:, :half], spectrum, 0, top_a, bottom_a, diff_frame, mask_frame, tm_count)
    outgoing = sweep_call(
        lam[:, half:], spectrum, half, top_b, bottom_b, diff_frame, mask_frame, tm_count,
        final=(jnp.concatenate([low, high], 1), first),
    )
    col_block = col_count // tm_count
    outgoing = outgoing.reshape(tm_count, 2, local_count * row_count, col_block)
    arrived = lax.all_to_all(outgoing, "tm", 0, 0, tiled=True)

    step_ids = (
        jnp.arange(tm_count, dtype=jnp.int32)[:, None] * local_count
        + jnp.arange(local_count, dtype=jnp.int32)[None, :]
    ).astype(jnp.float32)
    factor = jnp.exp(step_ids * (-math.log(alpha_wrap) / total_steps)) / math.sqrt(total_steps)
    combined = combine_call(class_weights(tm_count, bit_count), factor, arrived, Q_BLOCK)
    returned = lax.all_to_all(combined, "tm", 0, 0, tiled=True)
    returned = returned.reshape(tm_count, 2, local_count, row_count, col_block)
    return jnp.moveaxis(returned, 0, 3).reshape(2, local_count, row_count, col_count)


def solution(mesh):
    in_specs = (P(None, "tm", "space", None), P("space", None))
    out_specs = P(None, "tm", "space", None)
    return jax.shard_map(
        on_device, mesh=mesh, in_specs=in_specs, out_specs=out_specs, check_vma=False
    )
```

```python
import functools
import math

import jax
import jax.numpy as jnp
import numpy as np
from jax import lax
from jax.experimental import pallas as pl
from jax.experimental.pallas import tpu as pltpu
from jax.sharding import PartitionSpec as P

alpha_wrap = 0.25
step_rate = 0.5
flow_speed = 2.0
sweep_weights = [
    1.0 / (1.0 + 0.7 * math.cos(math.pi * (2 * order + 1) / 6.0)) for order in range(3)
]
Q_BLOCK = 32
F_BLOCK = 16
SWEEP_UNROLL = 8
HALO = 2


def reverse_bits(number, bit_count):
    result = number * 0
    for bit_place in range(bit_count):
        result = result + (number >> bit_place & 1) * (1 << bit_count - 1 - bit_place)
    return result


def shift_parts(freq_ids, total_steps):
    phase_angle = freq_ids.astype(jnp.float32) * (2.0 * math.pi / total_steps)
    root_scale = alpha_wrap ** (1.0 / total_steps)
    return (
        step_rate * (1.0 - root_scale * jnp.cos(phase_angle)),
        step_rate * root_scale * jnp.sin(phase_angle),
    )


def halo_pair(block, axis, dim, width):
    count = lax.axis_size(axis)
    forward = [(i, i + 1) for i in range(count - 1)]
    backward = [(i + 1, i) for i in range(count - 1)]
    size = block.shape[dim]
    top = lax.ppermute(lax.slice_in_dim(block, size - width, size, axis=dim), axis, forward)
    bottom = lax.ppermute(lax.slice_in_dim(block, 0, width, axis=dim), axis, backward)
    return top, bottom


def sweep_kernel(final, lam_ref, rhs_ref, top_ref, bot_ref, diff_ref, mask_ref, *rest):
    if final:
        low_ref, prev_ref, o_ref, field = rest
    else:
        (o_ref,) = rest
        field = o_ref
    block = rhs_ref.shape[1]
    count = lam_ref.shape[1]
    cols = rhs_ref.shape[3]
    base = pl.program_id(0) * block
    diff = diff_ref[...]
    diag_base = 4.0 * diff + flow_speed
    keep = mask_ref[...]
    row8 = lax.broadcasted_iota(jnp.int32, (8, cols), 0)
    col = lax.broadcasted_iota(jnp.int32, (16, cols), 1)

    def frame(x, f):
        local = rhs_ref[x, f]
        bv = bot_ref[x, f]
        tv = top_ref[x, f]
        hi = jnp.where(row8 == 0, jnp.broadcast_to(bv[0:1], (8, cols)), 0.0)
        hi = jnp.where(row8 == 1, jnp.broadcast_to(bv[1:2], (8, cols)), hi)
        hi = jnp.where(row8 == 6, jnp.broadcast_to(tv[0:1], (8, cols)), hi)
        hi = jnp.where(row8 == 7, jnp.broadcast_to(tv[1:2], (8, cols)), hi)
        return jnp.concatenate([local, hi], axis=0)

    def around(v):
        north = pltpu.roll(v, 1, 0)
        south = pltpu.roll(v, 15, 0)
        west = jnp.where(col == 0, 0.0, pltpu.roll(v, 1, 1))
        east = jnp.where(col == cols - 1, 0.0, pltpu.roll(v, cols - 1, 1))
        return north, north + south + west + east

    def body(f, carry):
        lam_r = lam_ref[0, base + f]
        lam_i = lam_ref[1, base + f]
        dr = diag_base + lam_r
        inv_mag = 1.0 / (dr * dr + lam_i * lam_i)
        r_re = frame(0, f)
        r_im = frame(1, f)
        g_re = (r_re * dr + r_im * lam_i) * inv_mag
        g_im = (r_im * dr - r_re * lam_i) * inv_mag
        c_re = sweep_weights[0] * g_re
        c_im = sweep_weights[0] * g_im
        for order in (1, 2):
            n_re, b_re = around(c_re)
            n_im, b_im = around(c_im)
            if order == 2:
                n_re, b_re, n_im, b_im = n_re[0:8], b_re[0:8], n_im[0:8], b_im[0:8]
                c_re, c_im, g_re, g_im = c_re[0:8], c_im[0:8], g_re[0:8], g_im[0:8]
                dr, inv_mag, d = dr[0:8], inv_mag[0:8], diff[0:8]
            else:
                d = diff
            weight = sweep_weights[order]
            t_re = d * b_re + flow_speed * n_re
            t_im = d * b_im + flow_speed * n_im
            scaled = weight * inv_mag
            c_re = c_re + weight * (g_re - c_re) + (t_re * dr + t_im * lam_i) * scaled
            c_im = c_im + weight * (g_im - c_im) + (t_im * dr - t_re * lam_i) * scaled
            if order == 1:
                c_re = c_re * keep
                c_im = c_im * keep
        width = field.shape[2]
        for blk in range(field.shape[0]):
            lanes = slice(blk * width, (blk + 1) * width)
            field[blk, pl.ds(pl.multiple_of((base + f) * 8, 8), 8), :] = c_re[0:8, lanes]
            field[blk, pl.ds(pl.multiple_of((count + base + f) * 8, 8), 8), :] = c_im[0:8, lanes]
        return carry

    lax.fori_loop(0, block, body, 0, unroll=SWEEP_UNROLL)

    if not final:
        return

    @pl.when(pl.program_id(0) == pl.num_programs(0) - 1)
    def _():
        table = low_ref[...]
        rows_out = o_ref.shape[1] // 8
        for blk in range(o_ref.shape[0]):
            for r in range(8):
                first = prev_ref[blk, pl.ds(r, 2 * count, stride=8), :]
                second = field[blk, pl.ds(r, 2 * count, stride=8), :]
                o_ref[blk, pl.ds(r, rows_out, stride=8), :] = jnp.dot(
                    table, jnp.concatenate([first, second], axis=0),
                    precision=lax.Precision.HIGH, preferred_element_type=jnp.float32,
                )


def sweep_call(lam, spectrum, offset, top, bottom, diff_frame, mask_frame, blocks, final=None):
    _, total, rows, cols = spectrum.shape
    count = lam.shape[1]
    block = F_BLOCK
    width = cols // blocks
    skip = offset // block
    big = pl.BlockSpec((2, block, rows, cols), lambda g: (0, g + skip, 0, 0))
    edge = pl.BlockSpec((2, block, HALO, cols), lambda g: (0, g, 0, 0))
    whole = pl.BlockSpec((16, cols), lambda g: (0, 0))
    field_rows = 2 * count * rows
    in_specs = [pl.BlockSpec(memory_space=pltpu.SMEM), big, edge, edge, whole, whole]
    operands = [lam, spectrum, top, bottom, diff_frame, mask_frame]
    scratch = []
    out_rows = field_rows
    if final is not None:
        table, prev = final
        in_specs += [pl.BlockSpec(table.shape, lambda g: (0, 0)), pl.BlockSpec(prev.shape, lambda g: (0, 0, 0))]
        operands += [table, prev]
        scratch = [pltpu.VMEM((blocks, field_rows, width), jnp.float32)]
        out_rows = 2 * total * rows
    return pl.pallas_call(
        functools.partial(sweep_kernel, final is not None),
        out_shape=jax.ShapeDtypeStruct((blocks, out_rows, width), jnp.float32),
        grid=(count // block,),
        in_specs=in_specs,
        out_specs=pl.BlockSpec((blocks, out_rows, width), lambda g: (0, 0, 0)),
        scratch_shapes=scratch,
        compiler_params=pltpu.CompilerParams(dimension_semantics=("arbitrary",)),
        cost_estimate=pl.CostEstimate(
            flops=100 * spectrum.size, transcendentals=0, bytes_accessed=4 * spectrum.size
        ),
    )(*operands)


def combine_kernel(weights, fac_ref, a_ref, o_ref):
    block = a_ref.shape[2] // 8
    base = pl.program_id(0) * block
    half = float(np.float32(1.0 / math.sqrt(2.0)))

    def turn(p, eighths):
        re, im = p
        if eighths == 0:
            return p
        if eighths == 2:
            return -im, re
        if eighths == 1:
            return half * (re - im), half * (re + im)
        return -half * (re + im), half * (re - im)

    def body(qi, carry):
        rows = pl.ds(pl.multiple_of(qi * 8, 8), 8)
        x = [(a_ref[s, 0, rows, :], a_ref[s, 1, rows, :]) for s in range(a_ref.shape[0])]
        span = 1
        while span < len(x):
            y = list(x)
            for start in range(0, len(x), 2 * span):
                for j in range(span):
                    u = x[start + j]
                    v = turn(x[start + j + span], j * len(x) // (2 * span))
                    y[start + j] = (u[0] + v[0], u[1] + v[1])
                    y[start + j + span] = (u[0] - v[0], u[1] - v[1])
            x = y
            span *= 2
        for m, (re, im) in enumerate(x):
            scale = fac_ref[m, base + qi]
            o_ref[m, 0, rows, :] = re * scale
            o_ref[m, 1, rows, :] = im * scale
        return carry

    lax.fori_loop(0, block, body, 0, unroll=SWEEP_UNROLL)


def combine_call(weights, factor, arrived, q_block):
    blocks, _, rows, width = arrived.shape
    spec = pl.BlockSpec((blocks, 2, q_block * 8, width), lambda g: (0, 0, g, 0))
    return pl.pallas_call(
        functools.partial(combine_kernel, weights),
        out_shape=jax.ShapeDtypeStruct(arrived.shape, jnp.float32),
        grid=(rows // (q_block * 8),),
        in_specs=[pl.BlockSpec(memory_space=pltpu.SMEM), spec],
        out_specs=spec,
        compiler_params=pltpu.CompilerParams(dimension_semantics=("arbitrary",)),
        cost_estimate=pl.CostEstimate(
            flops=40 * arrived.size, transcendentals=0, bytes_accessed=8 * arrived.size
        ),
    )(factor, arrived)


def class_weights(tm_count, bit_count):
    rows = []
    for m in range(tm_count):
        row = []
        for source in range(tm_count):
            angle = 2.0 * math.pi * ((m * reverse_bits(source, bit_count)) % tm_count) / tm_count
            c, s = math.cos(angle), math.sin(angle)
            c = float(np.float32(0.0 if abs(c) < 1e-9 else c))
            s = float(np.float32(0.0 if abs(s) < 1e-9 else s))
            row.append((c, s))
        rows.append(tuple(row))
    return tuple(rows)


def frames(diffusivity, d_top, d_bot, space_place, space_count):
    rows, cols = diffusivity.shape
    gap = jnp.zeros((16 - rows - 2 * HALO, cols), jnp.float32)
    diff_frame = jnp.concatenate([diffusivity, d_bot, gap, d_top], axis=0)
    row = jnp.arange(16, dtype=jnp.int32)
    keep = (row < rows) | ((row == rows) & (space_place < space_count - 1)) | (
        (row == 15) & (space_place > 0)
    )
    mask_frame = jnp.broadcast_to(keep.astype(jnp.float32)[:, None], (16, cols))
    return diff_frame, mask_frame


def on_device(spectrum, diffusivity):
    local_count = spectrum.shape[1]
    row_count = spectrum.shape[2]
    col_count = spectrum.shape[3]
    tm_count = lax.axis_size("tm")
    space_count = lax.axis_size("space")
    bit_count = tm_count.bit_length() - 1
    total_steps = local_count * tm_count
    tm_place = lax.axis_index("tm")
    space_place = lax.axis_index("space")
    residue = reverse_bits(tm_place, bit_count)
    index_f = jnp.arange(local_count, dtype=jnp.int32)
    freq_ids = index_f * tm_count + residue
    lam = jnp.stack(shift_parts(freq_ids, total_steps))

    half = local_count // 2
    diff_slot = jnp.broadcast_to(diffusivity[None, None], (2, 1, row_count, col_count))
    top_a, bottom_a = halo_pair(jnp.concatenate([spectrum[:, :half], diff_slot], axis=1), "space", 2, HALO)
    top_b, bottom_b = halo_pair(spectrum[:, half:], "space", 2, HALO)
    diff_frame, mask_frame = frames(diffusivity, top_a[0, half], bottom_a[0, half], space_place, space_count)
    grid_angle = (index_f[:, None] * freq_ids[None, :] % total_steps).astype(jnp.float32) * (
        2.0 * math.pi / total_steps
    )
    cosine = jnp.cos(grid_angle)
    sine = jnp.sin(grid_angle)
    table = jnp.concatenate(
        [jnp.concatenate([cosine, -sine], 1), jnp.concatenate([sine, cosine], 1)], 0
    )
    low = jnp.concatenate([table[:, :half], table[:, local_count:local_count + half]], 1)
    high = jnp.concatenate([table[:, half:local_count], table[:, local_count + half:]], 1)
    first = sweep_call(lam[:, :half], spectrum, 0, top_a, bottom_a, diff_frame, mask_frame, tm_count)
    outgoing = sweep_call(
        lam[:, half:], spectrum, half, top_b, bottom_b, diff_frame, mask_frame, tm_count,
        final=(jnp.concatenate([low, high], 1), first),
    )
    col_block = col_count // tm_count
    outgoing = outgoing.reshape(tm_count, 2, local_count * row_count, col_block)
    arrived = lax.all_to_all(outgoing, "tm", 0, 0, tiled=True)

    step_ids = (
        jnp.arange(tm_count, dtype=jnp.int32)[:, None] * local_count
        + jnp.arange(local_count, dtype=jnp.int32)[None, :]
    ).astype(jnp.float32)
    factor = jnp.exp(step_ids * (-math.log(alpha_wrap) / total_steps)) / math.sqrt(total_steps)
    combined = combine_call(class_weights(tm_count, bit_count), factor, arrived, Q_BLOCK)
    returned = lax.all_to_all(combined, "tm", 0, 0, tiled=True)
    returned = returned.reshape(tm_count, 2, local_count, row_count, col_block)
    return jnp.moveaxis(returned, 0, 3).reshape(2, local_count, row_count, col_count)


def solution(mesh):
    in_specs = (P(None, "tm", "space", None), P("space", None))
    out_specs = P(None, "tm", "space", None)
    return jax.shard_map(
        on_device, mesh=mesh, in_specs=in_specs, out_specs=out_specs, check_vma=False
    )
```

```python
import functools
import math

import jax
import jax.numpy as jnp
import numpy as np
from jax import lax
from jax.experimental import pallas as pl
from jax.experimental.pallas import tpu as pltpu
from jax.sharding import PartitionSpec as P

alpha_wrap = 0.25
step_rate = 0.5
flow_speed = 2.0
sweep_weights = [
    1.0 / (1.0 + 0.7 * math.cos(math.pi * (2 * order + 1) / 6.0)) for order in range(3)
]
Q_BLOCK = 32
F_BLOCK = 16
SWEEP_UNROLL = 16
HALO = 2


def reverse_bits(number, bit_count):
    result = number * 0
    for bit_place in range(bit_count):
        result = result + (number >> bit_place & 1) * (1 << bit_count - 1 - bit_place)
    return result


def shift_parts(freq_ids, total_steps):
    phase_angle = freq_ids.astype(jnp.float32) * (2.0 * math.pi / total_steps)
    root_scale = alpha_wrap ** (1.0 / total_steps)
    return (
        step_rate * (1.0 - root_scale * jnp.cos(phase_angle)),
        step_rate * root_scale * jnp.sin(phase_angle),
    )


def halo_pair(block, axis, dim, width):
    count = lax.axis_size(axis)
    forward = [(i, i + 1) for i in range(count - 1)]
    backward = [(i + 1, i) for i in range(count - 1)]
    size = block.shape[dim]
    top = lax.ppermute(lax.slice_in_dim(block, size - width, size, axis=dim), axis, forward)
    bottom = lax.ppermute(lax.slice_in_dim(block, 0, width, axis=dim), axis, backward)
    return top, bottom


def sweep_kernel(final, lam_ref, rhs_ref, top_ref, bot_ref, diff_ref, mask_ref, *rest):
    if final:
        low_ref, prev_ref, o_ref, field = rest
    else:
        (o_ref,) = rest
        field = o_ref
    block = rhs_ref.shape[1]
    count = lam_ref.shape[1]
    cols = rhs_ref.shape[3]
    base = pl.program_id(0) * block
    diff = diff_ref[...]
    diag_base = 4.0 * diff + flow_speed
    keep = mask_ref[...]
    row8 = lax.broadcasted_iota(jnp.int32, (8, cols), 0)
    col = lax.broadcasted_iota(jnp.int32, (16, cols), 1)

    def frame(x, f):
        local = rhs_ref[x, f]
        bv = bot_ref[x, f]
        tv = top_ref[x, f]
        hi = jnp.where(row8 == 0, jnp.broadcast_to(bv[0:1], (8, cols)), 0.0)
        hi = jnp.where(row8 == 1, jnp.broadcast_to(bv[1:2], (8, cols)), hi)
        hi = jnp.where(row8 == 6, jnp.broadcast_to(tv[0:1], (8, cols)), hi)
        hi = jnp.where(row8 == 7, jnp.broadcast_to(tv[1:2], (8, cols)), hi)
        return jnp.concatenate([local, hi], axis=0)

    def around(v):
        north = pltpu.roll(v, 1, 0)
        south = pltpu.roll(v, 15, 0)
        west = jnp.where(col == 0, 0.0, pltpu.roll(v, 1, 1))
        east = jnp.where(col == cols - 1, 0.0, pltpu.roll(v, cols - 1, 1))
        return north, north + south + west + east

    def body(f, carry):
        lam_r = lam_ref[0, base + f]
        lam_i = lam_ref[1, base + f]
        dr = diag_base + lam_r
        inv_mag = 1.0 / (dr * dr + lam_i * lam_i)
        r_re = frame(0, f)
        r_im = frame(1, f)
        g_re = (r_re * dr + r_im * lam_i) * inv_mag
        g_im = (r_im * dr - r_re * lam_i) * inv_mag
        c_re = sweep_weights[0] * g_re
        c_im = sweep_weights[0] * g_im
        for order in (1, 2):
            n_re, b_re = around(c_re)
            n_im, b_im = around(c_im)
            if order == 2:
                n_re, b_re, n_im, b_im = n_re[0:8], b_re[0:8], n_im[0:8], b_im[0:8]
                c_re, c_im, g_re, g_im = c_re[0:8], c_im[0:8], g_re[0:8], g_im[0:8]
                dr, inv_mag, d = dr[0:8], inv_mag[0:8], diff[0:8]
            else:
                d = diff
            weight = sweep_weights[order]
            t_re = d * b_re + flow_speed * n_re
            t_im = d * b_im + flow_speed * n_im
            scaled = weight * inv_mag
            c_re = c_re + weight * (g_re - c_re) + (t_re * dr + t_im * lam_i) * scaled
            c_im = c_im + weight * (g_im - c_im) + (t_im * dr - t_re * lam_i) * scaled
            if order == 1:
                c_re = c_re * keep
                c_im = c_im * keep
        width = field.shape[2]
        for blk in range(field.shape[0]):
            lanes = slice(blk * width, (blk + 1) * width)
            field[blk, pl.ds(pl.multiple_of((base + f) * 8, 8), 8), :] = c_re[0:8, lanes]
            field[blk, pl.ds(pl.multiple_of((count + base + f) * 8, 8), 8), :] = c_im[0:8, lanes]
        return carry

    lax.fori_loop(0, block, body, 0, unroll=SWEEP_UNROLL)

    if not final:
        return

    @pl.when(pl.program_id(0) == pl.num_programs(0) - 1)
    def _():
        table = low_ref[...]
        rows_out = o_ref.shape[1] // 8
        for blk in range(o_ref.shape[0]):
            for r in range(8):
                first = prev_ref[blk, pl.ds(r, 2 * count, stride=8), :]
                second = field[blk, pl.ds(r, 2 * count, stride=8), :]
                o_ref[blk, pl.ds(r, rows_out, stride=8), :] = jnp.dot(
                    table, jnp.concatenate([first, second], axis=0),
                    precision=lax.Precision.HIGH, preferred_element_type=jnp.float32,
                )


def sweep_call(lam, spectrum, offset, top, bottom, diff_frame, mask_frame, blocks, final=None):
    _, total, rows, cols = spectrum.shape
    count = lam.shape[1]
    block = F_BLOCK
    width = cols // blocks
    skip = offset // block
    big = pl.BlockSpec((2, block, rows, cols), lambda g: (0, g + skip, 0, 0))
    edge = pl.BlockSpec((2, block, HALO, cols), lambda g: (0, g, 0, 0))
    whole = pl.BlockSpec((16, cols), lambda g: (0, 0))
    field_rows = 2 * count * rows
    in_specs = [pl.BlockSpec(memory_space=pltpu.SMEM), big, edge, edge, whole, whole]
    operands = [lam, spectrum, top, bottom, diff_frame, mask_frame]
    scratch = []
    out_rows = field_rows
    if final is not None:
        table, prev = final
        in_specs += [pl.BlockSpec(table.shape, lambda g: (0, 0)), pl.BlockSpec(prev.shape, lambda g: (0, 0, 0))]
        operands += [table, prev]
        scratch = [pltpu.VMEM((blocks, field_rows, width), jnp.float32)]
        out_rows = 2 * total * rows
    return pl.pallas_call(
        functools.partial(sweep_kernel, final is not None),
        out_shape=jax.ShapeDtypeStruct((blocks, out_rows, width), jnp.float32),
        grid=(count // block,),
        in_specs=in_specs,
        out_specs=pl.BlockSpec((blocks, out_rows, width), lambda g: (0, 0, 0)),
        scratch_shapes=scratch,
        compiler_params=pltpu.CompilerParams(dimension_semantics=("arbitrary",)),
        cost_estimate=pl.CostEstimate(
            flops=100 * spectrum.size, transcendentals=0, bytes_accessed=4 * spectrum.size
        ),
    )(*operands)


def combine_kernel(weights, fac_ref, a_ref, o_ref):
    block = a_ref.shape[2] // 8
    base = pl.program_id(0) * block
    half = float(np.float32(1.0 / math.sqrt(2.0)))

    def turn(p, eighths):
        re, im = p
        if eighths == 0:
            return p
        if eighths == 2:
            return -im, re
        if eighths == 1:
            return half * (re - im), half * (re + im)
        return -half * (re + im), half * (re - im)

    def body(qi, carry):
        rows = pl.ds(pl.multiple_of(qi * 8, 8), 8)
        x = [(a_ref[s, 0, rows, :], a_ref[s, 1, rows, :]) for s in range(a_ref.shape[0])]
        span = 1
        while span < len(x):
            y = list(x)
            for start in range(0, len(x), 2 * span):
                for j in range(span):
                    u = x[start + j]
                    v = turn(x[start + j + span], j * len(x) // (2 * span))
                    y[start + j] = (u[0] + v[0], u[1] + v[1])
                    y[start + j + span] = (u[0] - v[0], u[1] - v[1])
            x = y
            span *= 2
        for m, (re, im) in enumerate(x):
            scale = fac_ref[m, base + qi]
            o_ref[m, 0, rows, :] = re * scale
            o_ref[m, 1, rows, :] = im * scale
        return carry

    lax.fori_loop(0, block, body, 0, unroll=SWEEP_UNROLL)


def combine_call(weights, factor, arrived, q_block):
    blocks, _, rows, width = arrived.shape
    spec = pl.BlockSpec((blocks, 2, q_block * 8, width), lambda g: (0, 0, g, 0))
    return pl.pallas_call(
        functools.partial(combine_kernel, weights),
        out_shape=jax.ShapeDtypeStruct(arrived.shape, jnp.float32),
        grid=(rows // (q_block * 8),),
        in_specs=[pl.BlockSpec(memory_space=pltpu.SMEM), spec],
        out_specs=spec,
        compiler_params=pltpu.CompilerParams(dimension_semantics=("arbitrary",)),
        cost_estimate=pl.CostEstimate(
            flops=40 * arrived.size, transcendentals=0, bytes_accessed=8 * arrived.size
        ),
    )(factor, arrived)


def class_weights(tm_count, bit_count):
    rows = []
    for m in range(tm_count):
        row = []
        for source in range(tm_count):
            angle = 2.0 * math.pi * ((m * reverse_bits(source, bit_count)) % tm_count) / tm_count
            c, s = math.cos(angle), math.sin(angle)
            c = float(np.float32(0.0 if abs(c) < 1e-9 else c))
            s = float(np.float32(0.0 if abs(s) < 1e-9 else s))
            row.append((c, s))
        rows.append(tuple(row))
    return tuple(rows)


def frames(diffusivity, d_top, d_bot, space_place, space_count):
    rows, cols = diffusivity.shape
    gap = jnp.zeros((16 - rows - 2 * HALO, cols), jnp.float32)
    diff_frame = jnp.concatenate([diffusivity, d_bot, gap, d_top], axis=0)
    row = jnp.arange(16, dtype=jnp.int32)
    keep = (row < rows) | ((row == rows) & (space_place < space_count - 1)) | (
        (row == 15) & (space_place > 0)
    )
    mask_frame = jnp.broadcast_to(keep.astype(jnp.float32)[:, None], (16, cols))
    return diff_frame, mask_frame


def on_device(spectrum, diffusivity):
    local_count = spectrum.shape[1]
    row_count = spectrum.shape[2]
    col_count = spectrum.shape[3]
    tm_count = lax.axis_size("tm")
    space_count = lax.axis_size("space")
    bit_count = tm_count.bit_length() - 1
    total_steps = local_count * tm_count
    tm_place = lax.axis_index("tm")
    space_place = lax.axis_index("space")
    residue = reverse_bits(tm_place, bit_count)
    index_f = jnp.arange(local_count, dtype=jnp.int32)
    freq_ids = index_f * tm_count + residue
    lam = jnp.stack(shift_parts(freq_ids, total_steps))

    half = local_count // 2
    diff_slot = jnp.broadcast_to(diffusivity[None, None], (2, 1, row_count, col_count))
    top_a, bottom_a = halo_pair(jnp.concatenate([spectrum[:, :half], diff_slot], axis=1), "space", 2, HALO)
    top_b, bottom_b = halo_pair(spectrum[:, half:], "space", 2, HALO)
    diff_frame, mask_frame = frames(diffusivity, top_a[0, half], bottom_a[0, half], space_place, space_count)
    grid_angle = (index_f[:, None] * freq_ids[None, :] % total_steps).astype(jnp.float32) * (
        2.0 * math.pi / total_steps
    )
    cosine = jnp.cos(grid_angle)
    sine = jnp.sin(grid_angle)
    table = jnp.concatenate(
        [jnp.concatenate([cosine, -sine], 1), jnp.concatenate([sine, cosine], 1)], 0
    )
    low = jnp.concatenate([table[:, :half], table[:, local_count:local_count + half]], 1)
    high = jnp.concatenate([table[:, half:local_count], table[:, local_count + half:]], 1)
    first = sweep_call(lam[:, :half], spectrum, 0, top_a, bottom_a, diff_frame, mask_frame, tm_count)
    outgoing = sweep_call(
        lam[:, half:], spectrum, half, top_b, bottom_b, diff_frame, mask_frame, tm_count,
        final=(jnp.concatenate([low, high], 1), first),
    )
    col_block = col_count // tm_count
    outgoing = outgoing.reshape(tm_count, 2, local_count * row_count, col_block)
    arrived = lax.all_to_all(outgoing, "tm", 0, 0, tiled=True)

    step_ids = (
        jnp.arange(tm_count, dtype=jnp.int32)[:, None] * local_count
        + jnp.arange(local_count, dtype=jnp.int32)[None, :]
    ).astype(jnp.float32)
    factor = jnp.exp(step_ids * (-math.log(alpha_wrap) / total_steps)) / math.sqrt(total_steps)
    combined = combine_call(class_weights(tm_count, bit_count), factor, arrived, Q_BLOCK)
    returned = lax.all_to_all(combined, "tm", 0, 0, tiled=True)
    returned = returned.reshape(tm_count, 2, local_count, row_count, col_block)
    return jnp.moveaxis(returned, 0, 3).reshape(2, local_count, row_count, col_count)


def solution(mesh):
    in_specs = (P(None, "tm", "space", None), P("space", None))
    out_specs = P(None, "tm", "space", None)
    return jax.shard_map(
        on_device, mesh=mesh, in_specs=in_specs, out_specs=out_specs, check_vma=False
    )
```
